32 devices in a mesh: lat: 8 (over y, x, core), lon: 4 (over z).
Axes of the slice: x: 2, y: 2, z: 4, core: 2. Of those that a mesh axis runs over, the one named last changes fastest.
Arguments:
- tracers: float32 [5, 4, 64, 2880], P(None, None, 'lat', 'lon'), may hold values from -6 to 6
- courant_x: float32 [4, 64, 2880], P(None, 'lat', 'lon'), may hold values from -0.3 to 0.3
- courant_y: float32 [4, 64, 2880], P(None, 'lat', 'lon'), may hold values from -0.3 to 0.3
- cutoffs: int32 [64], replicated, may hold values from 1 to 720, as said below
Outputs:
- advected: float32 [5, 4, 64, 2880], P(None, None, 'lat', 'lon')
The draws below stay inside these ranges and needn't reach their ends.
Inputs may be any that keep to these rules, and one draw needn't show every extreme that they name: `cutoffs`: some row poleward of 45 degrees keeps exactly 720 wavenumbers.
All inputs are finite; a program needn't handle non-finite values.
Results may differ from the reference program's by a relative error of at most 0.0003.
Values sent between devices are 32-bit elements; how exact they have to be, the bound alone decides.
No kernel may reach another device: no remote copies, remote signals or barrier semaphores. Data moves between devices by JAX's collectives and lax.ppermute only.
A program may use at most 64 MiB of HBM per device.

```python
import math
import jax
import jax.numpy as jnp
from jax import lax

TR = 5
LEV = 4
NLON = 2880
KMAX = 720
SUBSTEPS = 2
NLAT = 64


def draw_cutoffs(key, part):
    first_key, second_key = jax.random.split(jax.random.fold_in(key, 11))
    cut_rows = jax.random.randint(first_key, (NLAT,), 1, KMAX + 1, dtype=jnp.int32)
    chosen = jax.random.randint(second_key, (), 0, NLAT // 4, dtype=jnp.int32)
    return cut_rows.at[chosen].set(KMAX)


def shard_levels(own_key, shape, pieces, smallest, largest):
    gain, own = 1.0, jax.random.fold_in(own_key, 6)
    for axis_at, blocks in pieces:
        heights = jnp.exp(jax.random.uniform(jax.random.fold_in(own, axis_at), (blocks,), jnp.float32, smallest / len(pieces), largest / len(pieces)))
        gain = gain * jnp.repeat(heights, shape[axis_at] // blocks).reshape([-1 if axis == axis_at else 1 for axis in range(len(shape))])
    return gain


def noise(rng, extent, spread, bound, shards=(), kind=jnp.bfloat16):
    drawn = spread * jax.random.normal(rng, extent, jnp.float32)
    if shards:
        drawn = drawn * shard_levels(rng, extent, shards, -0.22, 0.18)
    return jnp.clip(drawn, -bound, bound).astype(kind)


def setup_inputs(seed: int = 0) -> dict:
    splits = jax.random.split(jax.random.key(seed), 5)
    tracers = noise(splits[0], (TR, LEV, NLAT, NLON), 1.0, 6.0, ((2, 8), (3, 4)), jnp.float32)
    courant_x = jnp.clip(jax.random.uniform(splits[1], (LEV, NLAT, NLON), jnp.float32, -0.3, 0.3) * shard_levels(splits[1], (LEV, NLAT, NLON), ((1, 8), (2, 4)), -0.4, 0.0), -0.3, 0.3)
    courant_y = jnp.clip(jax.random.uniform(splits[2], (LEV, NLAT, NLON), jnp.float32, -0.3, 0.3) * shard_levels(splits[2], (LEV, NLAT, NLON), ((1, 8), (2, 4)), -0.4, 0.0), -0.3, 0.3)
    cutoffs = draw_cutoffs(jax.random.fold_in(splits[4], 71), 0)
    return dict(tracers=tracers, courant_x=courant_x, courant_y=courant_y, cutoffs=cutoffs)


def window(values, first_cell, last_cell, dim_at):
    return lax.slice_in_dim(values, first_cell, last_cell, axis=dim_at)


def ppm_flux(padded, courant, dim_at, cell_count):
    edge_values = (7.0 / 12.0) * (window(padded, 1, cell_count + 4, dim_at) + window(padded, 2, cell_count + 5, dim_at)) - (1.0 / 12.0) * (window(padded, 0, cell_count + 3, dim_at) + window(padded, 3, cell_count + 6, dim_at))
    left_edge = window(edge_values, 0, cell_count + 1, dim_at)
    mid_edge = window(edge_values, 1, cell_count + 2, dim_at)
    right_edge = window(edge_values, 2, cell_count + 3, dim_at)
    left_cell = window(padded, 2, cell_count + 3, dim_at)
    right_cell = window(padded, 3, cell_count + 4, dim_at)
    magnitude = jnp.abs(courant)
    six_left = 6.0 * left_cell - 3.0 * (left_edge + mid_edge)
    six_right = 6.0 * right_cell - 3.0 * (mid_edge + right_edge)
    from_left = mid_edge - 0.5 * magnitude * (mid_edge - left_edge - (1.0 - magnitude * (2.0 / 3.0)) * six_left)
    from_right = mid_edge + 0.5 * magnitude * (right_edge - mid_edge + (1.0 - magnitude * (2.0 / 3.0)) * six_right)
    return courant * jnp.where(courant >= 0.0, from_left, from_right)


def reference(tracers, courant_x, courant_y, cutoffs):
    face_rows = jnp.arange(NLAT + 1, dtype=jnp.int32)
    face_angle = (face_rows.astype(jnp.float32) / NLAT - 0.5) * math.pi
    face_weight = jnp.where((face_rows == 0) | (face_rows == NLAT), 0.0, jnp.cos(face_angle))
    cell_rows = jnp.arange(NLAT, dtype=jnp.int32)
    center_weight = jnp.cos(((cell_rows.astype(jnp.float32) + 0.5) / NLAT - 0.5) * math.pi)
    polar_rows = (cell_rows < NLAT // 4) | (cell_rows >= NLAT - NLAT // 4)
    wavenumber = jnp.arange(NLON // 2 + 1, dtype=jnp.int32)
    kept_modes = (wavenumber[None, :] < cutoffs[:, None]).astype(jnp.float32)
    east_courant = jnp.concatenate([courant_x[:, :, -1:], courant_x], axis=2)
    north_courant = jnp.concatenate([courant_y, jnp.zeros_like(courant_y[:, :1])], axis=1)
    state = tracers
    for substep in range(SUBSTEPS):
        wrapped = jnp.concatenate([state[..., -3:], state, state[..., :3]], axis=3)
        zonal = ppm_flux(wrapped, east_courant, 3, NLON)
        south_far = jnp.roll(state[:, :, 2::-1, :], NLON // 2, axis=3)
        north_far = jnp.roll(state[:, :, NLAT - 1:NLAT - 4:-1, :], NLON // 2, axis=3)
        extended = jnp.concatenate([south_far, state, north_far], axis=2)
        meridional = ppm_flux(extended, north_courant, 2, NLAT) * face_weight[:, None]
        change = (zonal[..., 1:] - zonal[..., :-1]) + (meridional[:, :, 1:] - meridional[:, :, :-1]) / center_weight[:, None]
        state = state - change
        spectrum = jnp.fft.rfft(state, axis=3)
        kept_part = spectrum * kept_modes[None, None]
        smooth = jnp.fft.irfft(kept_part, n=NLON, axis=3).astype(state.dtype)
        state = jnp.where(polar_rows[:, None], smooth, state)
    return state
```

```python
import math

import jax
import jax.numpy as jnp
from jax import lax
from jax.sharding import PartitionSpec as P

KMAX = 720
SUBSTEPS = 2
HALO = 3
HIGHEST = lax.Precision.HIGHEST


def shift(x, axis, by, wrap):
    size = lax.axis_size(axis)
    pairs = [(i, (i + by) % size) for i in range(size) if wrap or 0 <= i + by < size]
    return lax.ppermute(x, axis, pairs)


def window(values, first_cell, last_cell, dim_at):
    return lax.slice_in_dim(values, first_cell, last_cell, axis=dim_at)


def ppm_flux(padded, courant, dim_at, cell_count):
    edge_values = 7.0 / 12.0 * (
        window(padded, 1, cell_count + 4, dim_at) + window(padded, 2, cell_count + 5, dim_at)
    ) - 1.0 / 12.0 * (
        window(padded, 0, cell_count + 3, dim_at) + window(padded, 3, cell_count + 6, dim_at)
    )
    left_edge = window(edge_values, 0, cell_count + 1, dim_at)
    mid_edge = window(edge_values, 1, cell_count + 2, dim_at)
    right_edge = window(edge_values, 2, cell_count + 3, dim_at)
    left_cell = window(padded, 2, cell_count + 3, dim_at)
    right_cell = window(padded, 3, cell_count + 4, dim_at)
    magnitude = jnp.abs(courant)
    six_left = 6.0 * left_cell - 3.0 * (left_edge + mid_edge)
    six_right = 6.0 * right_cell - 3.0 * (mid_edge + right_edge)
    from_left = mid_edge - 0.5 * magnitude * (
        mid_edge - left_edge - (1.0 - magnitude * (2.0 / 3.0)) * six_left
    )
    from_right = mid_edge + 0.5 * magnitude * (
        right_edge - mid_edge + (1.0 - magnitude * (2.0 / 3.0)) * six_right
    )
    return courant * jnp.where(courant >= 0.0, from_left, from_right)


def root_table(count):
    d = jnp.arange(count, dtype=jnp.int32)
    angle = (d[:, None] * d[None, :] % count).astype(jnp.float32) * (2.0 * math.pi / count)
    cos_dr, sin_dr = jnp.cos(angle), jnp.sin(angle)
    cos_dr = jnp.where(jnp.abs(cos_dr) < 1e-6, 0.0, cos_dr)
    sin_dr = jnp.where(jnp.abs(sin_dr) < 1e-6, 0.0, sin_dr)
    return cos_dr, sin_dr


def class_basis(tiles, cols, circle):
    per_class = KMAX // tiles
    r = jnp.arange(tiles, dtype=jnp.int32)
    m = jnp.arange(per_class, dtype=jnp.int32)
    q = jnp.arange(-HALO, cols + HALO, dtype=jnp.int32) % circle
    k = tiles * m[None, :] + r[:, None]
    phase = (q[None, :, None] * k[:, None, :]) % circle
    angle = phase.astype(jnp.float32) * (2.0 * math.pi / circle)
    return jnp.concatenate([jnp.cos(angle), jnp.sin(angle)], axis=2)


def filter_rows(rows, basis, roots, weights, polar):
    tiles, count, cols = rows.shape
    cos_dr, sin_dr = roots
    z_re = jnp.sum(cos_dr[:, :, None, None] * rows[None], axis=1)
    z_im = -jnp.sum(sin_dr[:, :, None, None] * rows[None], axis=1)
    z = jnp.concatenate([z_re, z_im], axis=1)
    z = jnp.pad(z, ((0, 0), (0, 0), (HALO, HALO)))
    prod = lax.dot_general(z, basis, (((2,), (1,)), ((0,), (0,))), precision=HIGHEST)
    per_class = basis.shape[2] // 2
    zc, zs = prod[:, :count, :per_class], prod[:, :count, per_class:]
    wc, ws = prod[:, count:, :per_class], prod[:, count:, per_class:]
    real = (zc + ws) * weights
    imag = (zs - wc) * weights
    spec = jnp.concatenate(
        [jnp.concatenate([real, imag], axis=2), jnp.concatenate([-imag, real], axis=2)], axis=1
    )
    back = lax.dot_general(spec, basis, (((2,), (2,)), ((0,), (0,))), precision=HIGHEST)
    w_re, w_im = back[:, :count], back[:, count:]
    smooth = jnp.sum(
        cos_dr[:, :, None, None] * w_re[None] - sin_dr[:, :, None, None] * w_im[None], axis=1
    )
    left = jnp.roll(rows[:, :, cols - HALO :], 1, axis=0)
    right = jnp.roll(rows[:, :, :HALO], -1, axis=0)
    wide = jnp.concatenate([left, rows, right], axis=2)
    return jnp.where(polar[None, :, None], smooth, wide)


def on_device(tracers, courant_x, courant_y, cutoffs):
    tracer_count, level_count, lat_rows, lon_cols = tracers.shape
    field_count = tracer_count * level_count
    lat_devices = lax.axis_size("lat")
    lon_devices = lax.axis_size("lon")
    lat_index = lax.axis_index("lat")
    lon_index = lax.axis_index("lon")
    circle = lon_cols * lon_devices
    total_rows = lat_rows * lat_devices
    row_global = lat_index * lat_rows + jnp.arange(lat_rows, dtype=jnp.int32)
    face_global = lat_index * lat_rows + jnp.arange(lat_rows + 1, dtype=jnp.int32)
    face_angle = (face_global.astype(jnp.float32) / total_rows - 0.5) * math.pi
    face_weight = jnp.where(
        (face_global == 0) | (face_global == total_rows), 0.0, jnp.cos(face_angle)
    )
    center_weight = jnp.cos(((row_global.astype(jnp.float32) + 0.5) / total_rows - 0.5) * math.pi)
    is_south = lat_index == 0
    is_north = lat_index == lat_devices - 1

    count = field_count * lat_rows // lon_devices
    flat = lon_index * count + jnp.arange(count, dtype=jnp.int32)
    held_global = lat_index * lat_rows + flat % lat_rows
    polar = (held_global < total_rows // 4) | (held_global >= total_rows - total_rows // 4)
    cut = jnp.take(cutoffs, held_global)
    per_class = KMAX // lon_devices
    k = lon_devices * jnp.arange(per_class, dtype=jnp.int32)[None, :] + jnp.arange(
        lon_devices, dtype=jnp.int32
    )[:, None]
    scale = jnp.where(k == 0, 1.0 / circle, 2.0 / circle).astype(jnp.float32)
    weights = jnp.where(k[:, None, :] < cut[None, :, None], scale[:, None, :], 0.0)
    basis = class_basis(lon_devices, lon_cols, circle)
    roots = root_table(lon_devices)

    west_cx = shift(courant_x[:, :, lon_cols - 1 :], "lon", 1, True)
    north_cy = shift(courant_y[:, :1], "lat", -1, False)
    east_courant = jnp.concatenate([west_cx, courant_x], axis=2)
    north_courant = jnp.concatenate(
        [courant_y, jnp.where(is_north, 0.0, north_cy)], axis=1
    )

    def lat_halos(state):
        south_in = shift(state[:, :, lat_rows - HALO :], "lat", 1, False)
        north_in = shift(state[:, :, :HALO], "lat", -1, False)
        edge = jnp.where(is_south, state[:, :, :HALO], state[:, :, lat_rows - HALO :])
        far = shift(edge, "lon", lon_devices // 2, True)
        far_rev = jnp.concatenate([far[:, :, 2:3], far[:, :, 1:2], far[:, :, 0:1]], axis=2)
        south_rows = jnp.where(is_south, far_rev, south_in)
        north_rows = jnp.where(is_north, far_rev, north_in)
        return jnp.concatenate([south_rows, state, north_rows], axis=2)

    state = tracers
    west_in = shift(state[..., lon_cols - HALO :], "lon", 1, True)
    east_in = shift(state[..., :HALO], "lon", -1, True)
    wrapped = jnp.concatenate([west_in, state, east_in], axis=3)
    for substep in range(SUBSTEPS):
        extended = lat_halos(state)
        zonal = ppm_flux(wrapped, east_courant, 3, lon_cols)
        meridional = ppm_flux(extended, north_courant, 2, lat_rows) * face_weight[:, None]
        change = (
            zonal[..., 1:]
            - zonal[..., :-1]
            + (meridional[:, :, 1:] - meridional[:, :, :-1]) / center_weight[:, None]
        )
        state = state - change
        rows = state.reshape(lon_devices, count, lon_cols)
        rows = lax.all_to_all(rows, "lon", 0, 0)
        wide = filter_rows(rows, basis, roots, weights, polar)
        if substep == SUBSTEPS - 1:
            wide = wide[:, :, HALO : HALO + lon_cols]
        wide = lax.all_to_all(wide, "lon", 0, 0)
        wrapped = wide.reshape(tracer_count, level_count, lat_rows, wide.shape[2])
        state = wrapped if substep == SUBSTEPS - 1 else wrapped[..., HALO : HALO + lon_cols]
    return state


def solution(mesh):
    in_specs = (P(None, None, "lat", "lon"), P(None, "lat", "lon"), P(None, "lat", "lon"), P())
    out_specs = P(None, None, "lat", "lon")
    return jax.shard_map(
        on_device, mesh=mesh, in_specs=in_specs, out_specs=out_specs, check_vma=False
    )
```

```python
import math

import jax
import jax.numpy as jnp
from jax import lax
from jax.sharding import PartitionSpec as P

KMAX = 720
SUBSTEPS = 2
HALO = 3
HIGHEST = lax.Precision.HIGHEST


def shift(x, axis, by, wrap):
    size = lax.axis_size(axis)
    pairs = [(i, (i + by) % size) for i in range(size) if wrap or 0 <= i + by < size]
    return lax.ppermute(x, axis, pairs)


def window(values, first_cell, last_cell, dim_at):
    return lax.slice_in_dim(values, first_cell, last_cell, axis=dim_at)


def ppm_flux(padded, courant, dim_at, cell_count):
    edge_values = 7.0 / 12.0 * (
        window(padded, 1, cell_count + 4, dim_at) + window(padded, 2, cell_count + 5, dim_at)
    ) - 1.0 / 12.0 * (
        window(padded, 0, cell_count + 3, dim_at) + window(padded, 3, cell_count + 6, dim_at)
    )
    left_edge = window(edge_values, 0, cell_count + 1, dim_at)
    mid_edge = window(edge_values, 1, cell_count + 2, dim_at)
    right_edge = window(edge_values, 2, cell_count + 3, dim_at)
    left_cell = window(padded, 2, cell_count + 3, dim_at)
    right_cell = window(padded, 3, cell_count + 4, dim_at)
    magnitude = jnp.abs(courant)
    six_left = 6.0 * left_cell - 3.0 * (left_edge + mid_edge)
    six_right = 6.0 * right_cell - 3.0 * (mid_edge + right_edge)
    from_left = mid_edge - 0.5 * magnitude * (
        mid_edge - left_edge - (1.0 - magnitude * (2.0 / 3.0)) * six_left
    )
    from_right = mid_edge + 0.5 * magnitude * (
        right_edge - mid_edge + (1.0 - magnitude * (2.0 / 3.0)) * six_right
    )
    return courant * jnp.where(courant >= 0.0, from_left, from_right)


def root_table(count):
    d = jnp.arange(count, dtype=jnp.int32)
    angle = (d[:, None] * d[None, :] % count).astype(jnp.float32) * (2.0 * math.pi / count)
    cos_dr, sin_dr = jnp.cos(angle), jnp.sin(angle)
    cos_dr = jnp.where(jnp.abs(cos_dr) < 1e-6, 0.0, cos_dr)
    sin_dr = jnp.where(jnp.abs(sin_dr) < 1e-6, 0.0, sin_dr)
    return cos_dr, sin_dr


def class_basis(tiles, cols, circle, halo=HALO):
    per_class = KMAX // tiles
    r = jnp.arange(tiles, dtype=jnp.int32)
    m = jnp.arange(per_class, dtype=jnp.int32)
    q = jnp.arange(-halo, cols + halo, dtype=jnp.int32) % circle
    k = tiles * m[None, :] + r[:, None]
    phase = (q[None, :, None] * k[:, None, :]) % circle
    angle = phase.astype(jnp.float32) * (2.0 * math.pi / circle)
    return jnp.concatenate([jnp.cos(angle), jnp.sin(angle)], axis=2)


def filter_rows(rows, basis, roots, weights, polar):
    tiles, count, cols = rows.shape
    cos_dr, sin_dr = roots
    z_re = jnp.sum(cos_dr[:, :, None, None] * rows[None], axis=1)
    z_im = -jnp.sum(sin_dr[:, :, None, None] * rows[None], axis=1)
    z = jnp.concatenate([z_re, z_im], axis=1)
    z = jnp.pad(z, ((0, 0), (0, 0), (HALO, HALO)))
    prod = lax.dot_general(z, basis, (((2,), (1,)), ((0,), (0,))), precision=HIGHEST)
    per_class = basis.shape[2] // 2
    zc, zs = prod[:, :count, :per_class], prod[:, :count, per_class:]
    wc, ws = prod[:, count:, :per_class], prod[:, count:, per_class:]
    real = (zc + ws) * weights
    imag = (zs - wc) * weights
    spec = jnp.concatenate(
        [jnp.concatenate([real, imag], axis=2), jnp.concatenate([-imag, real], axis=2)], axis=1
    )
    back = lax.dot_general(spec, basis, (((2,), (2,)), ((0,), (0,))), precision=HIGHEST)
    w_re, w_im = back[:, :count], back[:, count:]
    smooth = jnp.sum(
        cos_dr[:, :, None, None] * w_re[None] - sin_dr[:, :, None, None] * w_im[None], axis=1
    )
    left = jnp.roll(rows[:, :, cols - HALO :], 1, axis=0)
    right = jnp.roll(rows[:, :, :HALO], -1, axis=0)
    wide = jnp.concatenate([left, rows, right], axis=2)
    return jnp.where(polar[None, :, None], smooth, wide)


def tiled_path(tracers, courant_x, courant_y, cutoffs):
    tracer_count, level_count, lat_rows, lon_cols = tracers.shape
    field_count = tracer_count * level_count
    lat_devices = lax.axis_size("lat")
    lon_devices = lax.axis_size("lon")
    lat_index = lax.axis_index("lat")
    lon_index = lax.axis_index("lon")
    circle = lon_cols * lon_devices
    total_rows = lat_rows * lat_devices
    row_global = lat_index * lat_rows + jnp.arange(lat_rows, dtype=jnp.int32)
    face_global = lat_index * lat_rows + jnp.arange(lat_rows + 1, dtype=jnp.int32)
    face_angle = (face_global.astype(jnp.float32) / total_rows - 0.5) * math.pi
    face_weight = jnp.where(
        (face_global == 0) | (face_global == total_rows), 0.0, jnp.cos(face_angle)
    )
    center_weight = jnp.cos(((row_global.astype(jnp.float32) + 0.5) / total_rows - 0.5) * math.pi)
    is_south = lat_index == 0
    is_north = lat_index == lat_devices - 1

    count = field_count * lat_rows // lon_devices
    flat = lon_index * count + jnp.arange(count, dtype=jnp.int32)
    held_global = lat_index * lat_rows + flat % lat_rows
    polar = (held_global < total_rows // 4) | (held_global >= total_rows - total_rows // 4)
    cut = jnp.take(cutoffs, held_global)
    per_class = KMAX // lon_devices
    k = lon_devices * jnp.arange(per_class, dtype=jnp.int32)[None, :] + jnp.arange(
        lon_devices, dtype=jnp.int32
    )[:, None]
    scale = jnp.where(k == 0, 1.0 / circle, 2.0 / circle).astype(jnp.float32)
    weights = jnp.where(k[:, None, :] < cut[None, :, None], scale[:, None, :], 0.0)
    basis = class_basis(lon_devices, lon_cols, circle)
    roots = root_table(lon_devices)

    west_cx = shift(courant_x[:, :, lon_cols - 1 :], "lon", 1, True)
    north_cy = shift(courant_y[:, :1], "lat", -1, False)
    east_courant = jnp.concatenate([west_cx, courant_x], axis=2)
    north_courant = jnp.concatenate(
        [courant_y, jnp.where(is_north, 0.0, north_cy)], axis=1
    )

    def lat_halos(state):
        south_in = shift(state[:, :, lat_rows - HALO :], "lat", 1, False)
        north_in = shift(state[:, :, :HALO], "lat", -1, False)
        edge = jnp.where(is_south, state[:, :, :HALO], state[:, :, lat_rows - HALO :])
        far = shift(edge, "lon", lon_devices // 2, True)
        far_rev = jnp.concatenate([far[:, :, 2:3], far[:, :, 1:2], far[:, :, 0:1]], axis=2)
        south_rows = jnp.where(is_south, far_rev, south_in)
        north_rows = jnp.where(is_north, far_rev, north_in)
        return jnp.concatenate([south_rows, state, north_rows], axis=2)

    state = tracers
    west_in = shift(state[..., lon_cols - HALO :], "lon", 1, True)
    east_in = shift(state[..., :HALO], "lon", -1, True)
    wrapped = jnp.concatenate([west_in, state, east_in], axis=3)
    for substep in range(SUBSTEPS):
        extended = lat_halos(state)
        zonal = ppm_flux(wrapped, east_courant, 3, lon_cols)
        meridional = ppm_flux(extended, north_courant, 2, lat_rows) * face_weight[:, None]
        change = (
            zonal[..., 1:]
            - zonal[..., :-1]
            + (meridional[:, :, 1:] - meridional[:, :, :-1]) / center_weight[:, None]
        )
        state = state - change
        rows = state.reshape(lon_devices, count, lon_cols)
        rows = lax.all_to_all(rows, "lon", 0, 0)
        wide = filter_rows(rows, basis, roots, weights, polar)
        if substep == SUBSTEPS - 1:
            wide = wide[:, :, HALO : HALO + lon_cols]
        wide = lax.all_to_all(wide, "lon", 0, 0)
        wrapped = wide.reshape(tracer_count, level_count, lat_rows, wide.shape[2])
        state = wrapped if substep == SUBSTEPS - 1 else wrapped[..., HALO : HALO + lon_cols]
    return state


def filter_full(rows, basis, roots, weights):
    count, tiles, cols = rows.shape
    cos_dr, sin_dr = roots
    z_re = jnp.sum(cos_dr[:, None, :, None] * rows[None], axis=2)
    z_im = -jnp.sum(sin_dr[:, None, :, None] * rows[None], axis=2)
    z = jnp.concatenate([z_re, z_im], axis=1)
    prod = lax.dot_general(z, basis, (((2,), (1,)), ((0,), (0,))), precision=HIGHEST)
    per_class = basis.shape[2] // 2
    zc, zs = prod[:, :count, :per_class], prod[:, :count, per_class:]
    wc, ws = prod[:, count:, :per_class], prod[:, count:, per_class:]
    real = (zc + ws) * weights
    imag = (zs - wc) * weights
    spec = jnp.concatenate(
        [jnp.concatenate([real, imag], axis=2), jnp.concatenate([-imag, real], axis=2)], axis=1
    )
    back = lax.dot_general(spec, basis, (((2,), (2,)), ((0,), (0,))), precision=HIGHEST)
    w_re = jnp.transpose(back[:, :count], (1, 0, 2))
    w_im = jnp.transpose(back[:, count:], (1, 0, 2))
    return jnp.sum(
        cos_dr[None, :, :, None] * w_re[:, None] - sin_dr[None, :, :, None] * w_im[:, None], axis=2
    )


def transposed_path(tracers, courant_x, courant_y, cutoffs):
    tracer_count, level_count, lat_rows, lon_cols = tracers.shape
    field_count = tracer_count * level_count
    lat_devices = lax.axis_size("lat")
    lon_devices = lax.axis_size("lon")
    lat_index = lax.axis_index("lat")
    lon_index = lax.axis_index("lon")
    circle = lon_cols * lon_devices
    total_rows = lat_rows * lat_devices
    per_device = field_count // lon_devices
    row_global = lat_index * lat_rows + jnp.arange(lat_rows, dtype=jnp.int32)
    face_global = lat_index * lat_rows + jnp.arange(lat_rows + 1, dtype=jnp.int32)
    face_angle = (face_global.astype(jnp.float32) / total_rows - 0.5) * math.pi
    face_weight = jnp.where(
        (face_global == 0) | (face_global == total_rows), 0.0, jnp.cos(face_angle)
    )
    center_weight = jnp.cos(((row_global.astype(jnp.float32) + 0.5) / total_rows - 0.5) * math.pi)
    is_south = lat_index == 0
    is_north = lat_index == lat_devices - 1

    tiles = tracers.reshape(lon_devices, per_device, lat_rows, lon_cols)
    tiles = lax.all_to_all(tiles, "lon", 0, 0)
    state = jnp.transpose(tiles, (1, 2, 0, 3)).reshape(per_device, lat_rows, circle)

    north_cy = shift(courant_y[:, :1], "lat", -1, False)
    north_cy = jnp.where(is_north, 0.0, north_cy)
    own = jnp.concatenate([courant_x, courant_y, north_cy], axis=1)
    pieces = jnp.stack([own] + [shift(own, "lon", s, True) for s in range(1, lon_devices)])
    source = (lon_index - jnp.arange(lon_devices, dtype=jnp.int32)) % lon_devices
    full = jnp.take(pieces, source, axis=0)
    full = jnp.transpose(full, (1, 2, 0, 3)).reshape(level_count, 2 * lat_rows + 1, circle)
    levels = (lon_index * per_device + jnp.arange(per_device, dtype=jnp.int32)) % level_count
    held = jnp.take(full, levels, axis=0)
    cx = held[:, :lat_rows]
    north_courant = held[:, lat_rows:]
    east_courant = jnp.concatenate([cx[..., circle - 1 :], cx], axis=2)

    count = per_device * lat_rows
    held_global = lat_index * lat_rows + jnp.arange(count, dtype=jnp.int32) % lat_rows
    polar = (held_global < total_rows // 4) | (held_global >= total_rows - total_rows // 4)
    cut = jnp.take(cutoffs, held_global)
    per_class = KMAX // lon_devices
    k = lon_devices * jnp.arange(per_class, dtype=jnp.int32)[None, :] + jnp.arange(
        lon_devices, dtype=jnp.int32
    )[:, None]
    scale = jnp.where(k == 0, 1.0 / circle, 2.0 / circle).astype(jnp.float32)
    weights = jnp.where(k[:, None, :] < cut[None, :, None], scale[:, None, :], 0.0)
    basis = class_basis(lon_devices, lon_cols, circle, 0)
    roots = root_table(lon_devices)

    for substep in range(SUBSTEPS):
        south_in = shift(state[:, lat_rows - HALO :], "lat", 1, False)
        north_in = shift(state[:, :HALO], "lat", -1, False)
        edge = jnp.where(is_south, state[:, :HALO], state[:, lat_rows - HALO :])
        far = jnp.roll(edge, circle // 2, axis=2)
        far_rev = jnp.concatenate([far[:, 2:3], far[:, 1:2], far[:, 0:1]], axis=1)
        south_rows = jnp.where(is_south, far_rev, south_in)
        north_rows = jnp.where(is_north, far_rev, north_in)
        extended = jnp.concatenate([south_rows, state, north_rows], axis=1)
        wrapped = jnp.concatenate([state[..., circle - HALO :], state, state[..., :HALO]], axis=2)
        zonal = ppm_flux(wrapped, east_courant, 2, circle)
        meridional = ppm_flux(extended, north_courant, 1, lat_rows) * face_weight[:, None]
        change = (
            zonal[..., 1:]
            - zonal[..., :-1]
            + (meridional[:, 1:] - meridional[:, :-1]) / center_weight[:, None]
        )
        state = state - change
        rows = state.reshape(count, lon_devices, lon_cols)
        smooth = filter_full(rows, basis, roots, weights)
        state = jnp.where(polar[:, None, None], smooth, rows).reshape(per_device, lat_rows, circle)

    tiles = jnp.transpose(state.reshape(per_device, lat_rows, lon_devices, lon_cols), (2, 0, 1, 3))
    tiles = lax.all_to_all(tiles, "lon", 0, 0)
    return tiles.reshape(tracer_count, level_count, lat_rows, lon_cols)


def on_device(tracers, courant_x, courant_y, cutoffs):
    field_count = tracers.shape[0] * tracers.shape[1]
    if field_count % lax.axis_size("lon") == 0 and tracers.shape[2] >= HALO:
        return transposed_path(tracers, courant_x, courant_y, cutoffs)
    return tiled_path(tracers, courant_x, courant_y, cutoffs)


def solution(mesh):
    in_specs = (P(None, None, "lat", "lon"), P(None, "lat", "lon"), P(None, "lat", "lon"), P())
    out_specs = P(None, None, "lat", "lon")
    return jax.shard_map(
        on_device, mesh=mesh, in_specs=in_specs, out_specs=out_specs, check_vma=False
    )
```

```python
import math

import jax
import jax.numpy as jnp
from jax import lax
from jax.sharding import PartitionSpec as P

KMAX = 720
SUBSTEPS = 2
HALO = 3
HIGHEST = lax.Precision.HIGHEST


def shift(x, axis, by, wrap):
    size = lax.axis_size(axis)
    pairs = [(i, (i + by) % size) for i in range(size) if wrap or 0 <= i + by < size]
    return lax.ppermute(x, axis, pairs)


def window(values, first_cell, last_cell, dim_at):
    return lax.slice_in_dim(values, first_cell, last_cell, axis=dim_at)


def ppm_flux(padded, courant, dim_at, cell_count):
    edge_values = 7.0 / 12.0 * (
        window(padded, 1, cell_count + 4, dim_at) + window(padded, 2, cell_count + 5, dim_at)
    ) - 1.0 / 12.0 * (
        window(padded, 0, cell_count + 3, dim_at) + window(padded, 3, cell_count + 6, dim_at)
    )
    left_edge = window(edge_values, 0, cell_count + 1, dim_at)
    mid_edge = window(edge_values, 1, cell_count + 2, dim_at)
    right_edge = window(edge_values, 2, cell_count + 3, dim_at)
    left_cell = window(padded, 2, cell_count + 3, dim_at)
    right_cell = window(padded, 3, cell_count + 4, dim_at)
    magnitude = jnp.abs(courant)
    six_left = 6.0 * left_cell - 3.0 * (left_edge + mid_edge)
    six_right = 6.0 * right_cell - 3.0 * (mid_edge + right_edge)
    from_left = mid_edge - 0.5 * magnitude * (
        mid_edge - left_edge - (1.0 - magnitude * (2.0 / 3.0)) * six_left
    )
    from_right = mid_edge + 0.5 * magnitude * (
        right_edge - mid_edge + (1.0 - magnitude * (2.0 / 3.0)) * six_right
    )
    return courant * jnp.where(courant >= 0.0, from_left, from_right)


def root_table(count):
    d = jnp.arange(count, dtype=jnp.int32)
    angle = (d[:, None] * d[None, :] % count).astype(jnp.float32) * (2.0 * math.pi / count)
    cos_dr, sin_dr = jnp.cos(angle), jnp.sin(angle)
    cos_dr = jnp.where(jnp.abs(cos_dr) < 1e-6, 0.0, cos_dr)
    sin_dr = jnp.where(jnp.abs(sin_dr) < 1e-6, 0.0, sin_dr)
    return cos_dr, sin_dr


def class_basis(tiles, cols, circle, halo=HALO):
    per_class = KMAX // tiles
    r = jnp.arange(tiles, dtype=jnp.int32)
    m = jnp.arange(per_class, dtype=jnp.int32)
    q = jnp.arange(-halo, cols + halo, dtype=jnp.int32) % circle
    k = tiles * m[None, :] + r[:, None]
    phase = (q[None, :, None] * k[:, None, :]) % circle
    angle = phase.astype(jnp.float32) * (2.0 * math.pi / circle)
    return jnp.concatenate([jnp.cos(angle), jnp.sin(angle)], axis=2)


def filter_rows(rows, basis, roots, weights, polar, halo=HALO):
    tiles, count, cols = rows.shape
    cos_dr, sin_dr = roots
    z_re = jnp.sum(cos_dr[:, :, None, None] * rows[None], axis=1)
    z_im = -jnp.sum(sin_dr[:, :, None, None] * rows[None], axis=1)
    z = jnp.concatenate([z_re, z_im], axis=1)
    z = jnp.pad(z, ((0, 0), (0, 0), (halo, halo)))
    prod = lax.dot_general(z, basis, (((2,), (1,)), ((0,), (0,))), precision=HIGHEST)
    per_class = basis.shape[2] // 2
    zc, zs = prod[:, :count, :per_class], prod[:, :count, per_class:]
    wc, ws = prod[:, count:, :per_class], prod[:, count:, per_class:]
    real = (zc + ws) * weights
    imag = (zs - wc) * weights
    spec = jnp.concatenate(
        [jnp.concatenate([real, imag], axis=2), jnp.concatenate([-imag, real], axis=2)], axis=1
    )
    back = lax.dot_general(spec, basis, (((2,), (2,)), ((0,), (0,))), precision=HIGHEST)
    w_re, w_im = back[:, :count], back[:, count:]
    smooth = jnp.sum(
        cos_dr[:, :, None, None] * w_re[None] - sin_dr[:, :, None, None] * w_im[None], axis=1
    )
    wide = rows
    if halo:
        left = jnp.roll(rows[:, :, cols - halo :], 1, axis=0)
        right = jnp.roll(rows[:, :, :halo], -1, axis=0)
        wide = jnp.concatenate([left, rows, right], axis=2)
    return jnp.where(polar[None, :, None], smooth, wide)


def tiled_path(tracers, courant_x, courant_y, cutoffs):
    tracer_count, level_count, lat_rows, lon_cols = tracers.shape
    field_count = tracer_count * level_count
    lat_devices = lax.axis_size("lat")
    lon_devices = lax.axis_size("lon")
    lat_index = lax.axis_index("lat")
    lon_index = lax.axis_index("lon")
    circle = lon_cols * lon_devices
    total_rows = lat_rows * lat_devices
    row_global = lat_index * lat_rows + jnp.arange(lat_rows, dtype=jnp.int32)
    face_global = lat_index * lat_rows + jnp.arange(lat_rows + 1, dtype=jnp.int32)
    face_angle = (face_global.astype(jnp.float32) / total_rows - 0.5) * math.pi
    face_weight = jnp.where(
        (face_global == 0) | (face_global == total_rows), 0.0, jnp.cos(face_angle)
    )
    center_weight = jnp.cos(((row_global.astype(jnp.float32) + 0.5) / total_rows - 0.5) * math.pi)
    is_south = lat_index == 0
    is_north = lat_index == lat_devices - 1

    count = field_count * lat_rows // lon_devices
    flat = lon_index * count + jnp.arange(count, dtype=jnp.int32)
    held_global = lat_index * lat_rows + flat % lat_rows
    polar = (held_global < total_rows // 4) | (held_global >= total_rows - total_rows // 4)
    cut = jnp.take(cutoffs, held_global)
    per_class = KMAX // lon_devices
    k = lon_devices * jnp.arange(per_class, dtype=jnp.int32)[None, :] + jnp.arange(
        lon_devices, dtype=jnp.int32
    )[:, None]
    scale = jnp.where(k == 0, 1.0 / circle, 2.0 / circle).astype(jnp.float32)
    weights = jnp.where(k[:, None, :] < cut[None, :, None], scale[:, None, :], 0.0)
    basis = class_basis(lon_devices, lon_cols, circle)
    roots = root_table(lon_devices)

    west_cx = shift(courant_x[:, :, lon_cols - 1 :], "lon", 1, True)
    north_cy = shift(courant_y[:, :1], "lat", -1, False)
    east_courant = jnp.concatenate([west_cx, courant_x], axis=2)
    north_courant = jnp.concatenate(
        [courant_y, jnp.where(is_north, 0.0, north_cy)], axis=1
    )

    def lat_halos(state):
        south_in = shift(state[:, :, lat_rows - HALO :], "lat", 1, False)
        north_in = shift(state[:, :, :HALO], "lat", -1, False)
        edge = jnp.where(is_south, state[:, :, :HALO], state[:, :, lat_rows - HALO :])
        far = shift(edge, "lon", lon_devices // 2, True)
        far_rev = jnp.concatenate([far[:, :, 2:3], far[:, :, 1:2], far[:, :, 0:1]], axis=2)
        south_rows = jnp.where(is_south, far_rev, south_in)
        north_rows = jnp.where(is_north, far_rev, north_in)
        return jnp.concatenate([south_rows, state, north_rows], axis=2)

    state = tracers
    west_in = shift(state[..., lon_cols - HALO :], "lon", 1, True)
    east_in = shift(state[..., :HALO], "lon", -1, True)
    wrapped = jnp.concatenate([west_in, state, east_in], axis=3)
    for substep in range(SUBSTEPS):
        extended = lat_halos(state)
        zonal = ppm_flux(wrapped, east_courant, 3, lon_cols)
        meridional = ppm_flux(extended, north_courant, 2, lat_rows) * face_weight[:, None]
        change = (
            zonal[..., 1:]
            - zonal[..., :-1]
            + (meridional[:, :, 1:] - meridional[:, :, :-1]) / center_weight[:, None]
        )
        state = state - change
        rows = state.reshape(lon_devices, count, lon_cols)
        rows = lax.all_to_all(rows, "lon", 0, 0)
        wide = filter_rows(rows, basis, roots, weights, polar)
        if substep == SUBSTEPS - 1:
            wide = wide[:, :, HALO : HALO + lon_cols]
        wide = lax.all_to_all(wide, "lon", 0, 0)
        wrapped = wide.reshape(tracer_count, level_count, lat_rows, wide.shape[2])
        state = wrapped if substep == SUBSTEPS - 1 else wrapped[..., HALO : HALO + lon_cols]
    return state


def transposed_path(tracers, courant_x, courant_y, cutoffs):
    tracer_count, level_count, lat_rows, lon_cols = tracers.shape
    lat_devices = lax.axis_size("lat")
    lon_devices = lax.axis_size("lon")
    lat_index = lax.axis_index("lat")
    circle = lon_cols * lon_devices
    total_rows = lat_rows * lat_devices
    row_global = lat_index * lat_rows + jnp.arange(lat_rows, dtype=jnp.int32)
    face_global = lat_index * lat_rows + jnp.arange(lat_rows + 1, dtype=jnp.int32)
    face_angle = (face_global.astype(jnp.float32) / total_rows - 0.5) * math.pi
    face_weight = jnp.where(
        (face_global == 0) | (face_global == total_rows), 0.0, jnp.cos(face_angle)
    )
    center_weight = jnp.cos(((row_global.astype(jnp.float32) + 0.5) / total_rows - 0.5) * math.pi)
    is_south = lat_index == 0
    is_north = lat_index == lat_devices - 1

    north_cy = shift(courant_y[:, :1], "lat", -1, False)
    north_cy = jnp.where(is_north, 0.0, north_cy)
    count = tracer_count * lat_rows
    payload = jnp.concatenate(
        [
            jnp.transpose(tracers, (1, 0, 2, 3)).reshape(level_count, count, lon_cols),
            courant_x,
            courant_y,
            north_cy,
        ],
        axis=1,
    )
    payload = lax.all_to_all(payload, "lon", 0, 0)
    state = payload[:, :count].reshape(lon_devices, tracer_count, lat_rows, lon_cols)
    cx = payload[:, None, count : count + lat_rows]
    north_courant = payload[:, None, count + lat_rows :]
    east_courant = jnp.concatenate([jnp.roll(cx[..., lon_cols - 1 :], 1, axis=0), cx], axis=3)

    held_global = lat_index * lat_rows + jnp.arange(count, dtype=jnp.int32) % lat_rows
    polar = (held_global < total_rows // 4) | (held_global >= total_rows - total_rows // 4)
    cut = jnp.take(cutoffs, held_global)
    per_class = KMAX // lon_devices
    k = lon_devices * jnp.arange(per_class, dtype=jnp.int32)[None, :] + jnp.arange(
        lon_devices, dtype=jnp.int32
    )[:, None]
    scale = jnp.where(k == 0, 1.0 / circle, 2.0 / circle).astype(jnp.float32)
    weights = jnp.where(k[:, None, :] < cut[None, :, None], scale[:, None, :], 0.0)
    basis = class_basis(lon_devices, lon_cols, circle, 0)
    roots = root_table(lon_devices)

    for substep in range(SUBSTEPS):
        south_in = shift(state[:, :, lat_rows - HALO :], "lat", 1, False)
        north_in = shift(state[:, :, :HALO], "lat", -1, False)
        edge = jnp.where(is_south, state[:, :, :HALO], state[:, :, lat_rows - HALO :])
        far = jnp.roll(edge, lon_devices // 2, axis=0)
        far_rev = jnp.concatenate([far[:, :, 2:3], far[:, :, 1:2], far[:, :, 0:1]], axis=2)
        south_rows = jnp.where(is_south, far_rev, south_in)
        north_rows = jnp.where(is_north, far_rev, north_in)
        extended = jnp.concatenate([south_rows, state, north_rows], axis=2)
        wrapped = jnp.concatenate(
            [
                jnp.roll(state[..., lon_cols - HALO :], 1, axis=0),
                state,
                jnp.roll(state[..., :HALO], -1, axis=0),
            ],
            axis=3,
        )
        zonal = ppm_flux(wrapped, east_courant, 3, lon_cols)
        meridional = ppm_flux(extended, north_courant, 2, lat_rows) * face_weight[:, None]
        change = (
            zonal[..., 1:]
            - zonal[..., :-1]
            + (meridional[:, :, 1:] - meridional[:, :, :-1]) / center_weight[:, None]
        )
        state = state - change
        rows = state.reshape(lon_devices, count, lon_cols)
        rows = filter_rows(rows, basis, roots, weights, polar, 0)
        state = rows.reshape(lon_devices, tracer_count, lat_rows, lon_cols)

    tiles = lax.all_to_all(state, "lon", 0, 0)
    return jnp.transpose(tiles, (1, 0, 2, 3))


def on_device(tracers, courant_x, courant_y, cutoffs):
    field_count = tracers.shape[0] * tracers.shape[1]
    if tracers.shape[1] == lax.axis_size("lon") and tracers.shape[2] >= HALO:
        return transposed_path(tracers, courant_x, courant_y, cutoffs)
    return tiled_path(tracers, courant_x, courant_y, cutoffs)


def solution(mesh):
    in_specs = (P(None, None, "lat", "lon"), P(None, "lat", "lon"), P(None, "lat", "lon"), P())
    out_specs = P(None, None, "lat", "lon")
    return jax.shard_map(
        on_device, mesh=mesh, in_specs=in_specs, out_specs=out_specs, check_vma=False
    )
```

```python
import math

import jax
import jax.numpy as jnp
from jax import lax
from jax.sharding import PartitionSpec as P

KMAX = 720
SUBSTEPS = 2
HALO = 3
MATMUL_PRECISION = lax.Precision.HIGH


def shift(x, axis, by, wrap):
    size = lax.axis_size(axis)
    pairs = [(i, (i + by) % size) for i in range(size) if wrap or 0 <= i + by < size]
    return lax.ppermute(x, axis, pairs)


def window(values, first_cell, last_cell, dim_at):
    return lax.slice_in_dim(values, first_cell, last_cell, axis=dim_at)


def ppm_flux(padded, courant, dim_at, cell_count):
    edge_values = 7.0 / 12.0 * (
        window(padded, 1, cell_count + 4, dim_at) + window(padded, 2, cell_count + 5, dim_at)
    ) - 1.0 / 12.0 * (
        window(padded, 0, cell_count + 3, dim_at) + window(padded, 3, cell_count + 6, dim_at)
    )
    left_edge = window(edge_values, 0, cell_count + 1, dim_at)
    mid_edge = window(edge_values, 1, cell_count + 2, dim_at)
    right_edge = window(edge_values, 2, cell_count + 3, dim_at)
    left_cell = window(padded, 2, cell_count + 3, dim_at)
    right_cell = window(padded, 3, cell_count + 4, dim_at)
    magnitude = jnp.abs(courant)
    six_left = 6.0 * left_cell - 3.0 * (left_edge + mid_edge)
    six_right = 6.0 * right_cell - 3.0 * (mid_edge + right_edge)
    from_left = mid_edge - 0.5 * magnitude * (
        mid_edge - left_edge - (1.0 - magnitude * (2.0 / 3.0)) * six_left
    )
    from_right = mid_edge + 0.5 * magnitude * (
        right_edge - mid_edge + (1.0 - magnitude * (2.0 / 3.0)) * six_right
    )
    return courant * jnp.where(courant >= 0.0, from_left, from_right)


def root_table(count):
    d = jnp.arange(count, dtype=jnp.int32)
    angle = (d[:, None] * d[None, :] % count).astype(jnp.float32) * (2.0 * math.pi / count)
    cos_dr, sin_dr = jnp.cos(angle), jnp.sin(angle)
    cos_dr = jnp.where(jnp.abs(cos_dr) < 1e-6, 0.0, cos_dr)
    sin_dr = jnp.where(jnp.abs(sin_dr) < 1e-6, 0.0, sin_dr)
    return cos_dr, sin_dr


def class_basis(tiles, cols, circle, halo=HALO):
    per_class = KMAX // tiles
    r = jnp.arange(tiles, dtype=jnp.int32)
    m = jnp.arange(per_class, dtype=jnp.int32)
    q = jnp.arange(-halo, cols + halo, dtype=jnp.int32) % circle
    k = tiles * m[None, :] + r[:, None]
    phase = (q[None, :, None] * k[:, None, :]) % circle
    angle = phase.astype(jnp.float32) * (2.0 * math.pi / circle)
    return jnp.concatenate([jnp.cos(angle), jnp.sin(angle)], axis=2)


def filter_rows(rows, basis, roots, weights, polar, halo=HALO):
    tiles, count, cols = rows.shape
    cos_dr, sin_dr = roots
    z_re = jnp.sum(cos_dr[:, :, None, None] * rows[None], axis=1)
    z_im = -jnp.sum(sin_dr[:, :, None, None] * rows[None], axis=1)
    z = jnp.concatenate([z_re, z_im], axis=1)
    z = jnp.pad(z, ((0, 0), (0, 0), (halo, halo)))
    prod = lax.dot_general(z, basis, (((2,), (1,)), ((0,), (0,))), precision=MATMUL_PRECISION)
    per_class = basis.shape[2] // 2
    zc, zs = prod[:, :count, :per_class], prod[:, :count, per_class:]
    wc, ws = prod[:, count:, :per_class], prod[:, count:, per_class:]
    real = (zc + ws) * weights
    imag = (zs - wc) * weights
    spec = jnp.concatenate(
        [jnp.concatenate([real, imag], axis=2), jnp.concatenate([-imag, real], axis=2)], axis=1
    )
    back = lax.dot_general(spec, basis, (((2,), (2,)), ((0,), (0,))), precision=MATMUL_PRECISION)
    w_re, w_im = back[:, :count], back[:, count:]
    smooth = jnp.sum(
        cos_dr[:, :, None, None] * w_re[None] - sin_dr[:, :, None, None] * w_im[None], axis=1
    )
    wide = rows
    if halo:
        left = jnp.roll(rows[:, :, cols - halo :], 1, axis=0)
        right = jnp.roll(rows[:, :, :halo], -1, axis=0)
        wide = jnp.concatenate([left, rows, right], axis=2)
    return jnp.where(polar[None, :, None], smooth, wide)


def tiled_path(tracers, courant_x, courant_y, cutoffs):
    tracer_count, level_count, lat_rows, lon_cols = tracers.shape
    field_count = tracer_count * level_count
    lat_devices = lax.axis_size("lat")
    lon_devices = lax.axis_size("lon")
    lat_index = lax.axis_index("lat")
    lon_index = lax.axis_index("lon")
    circle = lon_cols * lon_devices
    total_rows = lat_rows * lat_devices
    row_global = lat_index * lat_rows + jnp.arange(lat_rows, dtype=jnp.int32)
    face_global = lat_index * lat_rows + jnp.arange(lat_rows + 1, dtype=jnp.int32)
    face_angle = (face_global.astype(jnp.float32) / total_rows - 0.5) * math.pi
    face_weight = jnp.where(
        (face_global == 0) | (face_global == total_rows), 0.0, jnp.cos(face_angle)
    )
    center_weight = jnp.cos(((row_global.astype(jnp.float32) + 0.5) / total_rows - 0.5) * math.pi)
    is_south = lat_index == 0
    is_north = lat_index == lat_devices - 1

    count = field_count * lat_rows // lon_devices
    flat = lon_index * count + jnp.arange(count, dtype=jnp.int32)
    held_global = lat_index * lat_rows + flat % lat_rows
    polar = (held_global < total_rows // 4) | (held_global >= total_rows - total_rows // 4)
    cut = jnp.take(cutoffs, held_global)
    per_class = KMAX // lon_devices
    k = lon_devices * jnp.arange(per_class, dtype=jnp.int32)[None, :] + jnp.arange(
        lon_devices, dtype=jnp.int32
    )[:, None]
    scale = jnp.where(k == 0, 1.0 / circle, 2.0 / circle).astype(jnp.float32)
    weights = jnp.where(k[:, None, :] < cut[None, :, None], scale[:, None, :], 0.0)
    basis = class_basis(lon_devices, lon_cols, circle)
    roots = root_table(lon_devices)

    west_cx = shift(courant_x[:, :, lon_cols - 1 :], "lon", 1, True)
    north_cy = shift(courant_y[:, :1], "lat", -1, False)
    east_courant = jnp.concatenate([west_cx, courant_x], axis=2)
    north_courant = jnp.concatenate(
        [courant_y, jnp.where(is_north, 0.0, north_cy)], axis=1
    )

    def lat_halos(state):
        south_in = shift(state[:, :, lat_rows - HALO :], "lat", 1, False)
        north_in = shift(state[:, :, :HALO], "lat", -1, False)
        edge = jnp.where(is_south, state[:, :, :HALO], state[:, :, lat_rows - HALO :])
        far = shift(edge, "lon", lon_devices // 2, True)
        far_rev = jnp.concatenate([far[:, :, 2:3], far[:, :, 1:2], far[:, :, 0:1]], axis=2)
        south_rows = jnp.where(is_south, far_rev, south_in)
        north_rows = jnp.where(is_north, far_rev, north_in)
        return jnp.concatenate([south_rows, state, north_rows], axis=2)

    state = tracers
    west_in = shift(state[..., lon_cols - HALO :], "lon", 1, True)
    east_in = shift(state[..., :HALO], "lon", -1, True)
    wrapped = jnp.concatenate([west_in, state, east_in], axis=3)
    for substep in range(SUBSTEPS):
        extended = lat_halos(state)
        zonal = ppm_flux(wrapped, east_courant, 3, lon_cols)
        meridional = ppm_flux(extended, north_courant, 2, lat_rows) * face_weight[:, None]
        change = (
            zonal[..., 1:]
            - zonal[..., :-1]
            + (meridional[:, :, 1:] - meridional[:, :, :-1]) / center_weight[:, None]
        )
        state = state - change
        rows = state.reshape(lon_devices, count, lon_cols)
        rows = lax.all_to_all(rows, "lon", 0, 0)
        wide = filter_rows(rows, basis, roots, weights, polar)
        if substep == SUBSTEPS - 1:
            wide = wide[:, :, HALO : HALO + lon_cols]
        wide = lax.all_to_all(wide, "lon", 0, 0)
        wrapped = wide.reshape(tracer_count, level_count, lat_rows, wide.shape[2])
        state = wrapped if substep == SUBSTEPS - 1 else wrapped[..., HALO : HALO + lon_cols]
    return state


def transposed_path(tracers, courant_x, courant_y, cutoffs):
    tracer_count, level_count, lat_rows, lon_cols = tracers.shape
    lat_devices = lax.axis_size("lat")
    lon_devices = lax.axis_size("lon")
    lat_index = lax.axis_index("lat")
    circle = lon_cols * lon_devices
    total_rows = lat_rows * lat_devices
    row_global = lat_index * lat_rows + jnp.arange(lat_rows, dtype=jnp.int32)
    face_global = lat_index * lat_rows + jnp.arange(lat_rows + 1, dtype=jnp.int32)
    face_angle = (face_global.astype(jnp.float32) / total_rows - 0.5) * math.pi
    face_weight = jnp.where(
        (face_global == 0) | (face_global == total_rows), 0.0, jnp.cos(face_angle)
    )
    center_weight = jnp.cos(((row_global.astype(jnp.float32) + 0.5) / total_rows - 0.5) * math.pi)
    is_south = lat_index == 0
    is_north = lat_index == lat_devices - 1

    north_cy = shift(courant_y[:, :1], "lat", -1, False)
    north_cy = jnp.where(is_north, 0.0, north_cy)
    count = tracer_count * lat_rows
    payload = jnp.concatenate(
        [
            jnp.transpose(tracers, (1, 0, 2, 3)).reshape(level_count, count, lon_cols),
            courant_x,
            courant_y,
            north_cy,
        ],
        axis=1,
    )
    payload = lax.all_to_all(payload, "lon", 0, 0)
    state = payload[:, :count].reshape(lon_devices, tracer_count, lat_rows, lon_cols)
    cx = payload[:, None, count : count + lat_rows]
    north_courant = payload[:, None, count + lat_rows :]
    east_courant = jnp.concatenate([jnp.roll(cx[..., lon_cols - 1 :], 1, axis=0), cx], axis=3)

    held_global = lat_index * lat_rows + jnp.arange(count, dtype=jnp.int32) % lat_rows
    polar = (held_global < total_rows // 4) | (held_global >= total_rows - total_rows // 4)
    cut = jnp.take(cutoffs, held_global)
    per_class = KMAX // lon_devices
    k = lon_devices * jnp.arange(per_class, dtype=jnp.int32)[None, :] + jnp.arange(
        lon_devices, dtype=jnp.int32
    )[:, None]
    scale = jnp.where(k == 0, 1.0 / circle, 2.0 / circle).astype(jnp.float32)
    weights = jnp.where(k[:, None, :] < cut[None, :, None], scale[:, None, :], 0.0)
    basis = class_basis(lon_devices, lon_cols, circle, 0)
    roots = root_table(lon_devices)

    for substep in range(SUBSTEPS):
        south_in = shift(state[:, :, lat_rows - HALO :], "lat", 1, False)
        north_in = shift(state[:, :, :HALO], "lat", -1, False)
        edge = jnp.where(is_south, state[:, :, :HALO], state[:, :, lat_rows - HALO :])
        far = jnp.roll(edge, lon_devices // 2, axis=0)
        far_rev = jnp.concatenate([far[:, :, 2:3], far[:, :, 1:2], far[:, :, 0:1]], axis=2)
        south_rows = jnp.where(is_south, far_rev, south_in)
        north_rows = jnp.where(is_north, far_rev, north_in)
        extended = jnp.concatenate([south_rows, state, north_rows], axis=2)
        wrapped = jnp.concatenate(
            [
                jnp.roll(state[..., lon_cols - HALO :], 1, axis=0),
                state,
                jnp.roll(state[..., :HALO], -1, axis=0),
            ],
            axis=3,
        )
        zonal = ppm_flux(wrapped, east_courant, 3, lon_cols)
        meridional = ppm_flux(extended, north_courant, 2, lat_rows) * face_weight[:, None]
        change = (
            zonal[..., 1:]
            - zonal[..., :-1]
            + (meridional[:, :, 1:] - meridional[:, :, :-1]) / center_weight[:, None]
        )
        state = state - change
        rows = state.reshape(lon_devices, count, lon_cols)
        rows = filter_rows(rows, basis, roots, weights, polar, 0)
        state = rows.reshape(lon_devices, tracer_count, lat_rows, lon_cols)

    tiles = lax.all_to_all(state, "lon", 0, 0)
    return jnp.transpose(tiles, (1, 0, 2, 3))


def on_device(tracers, courant_x, courant_y, cutoffs):
    field_count = tracers.shape[0] * tracers.shape[1]
    if tracers.shape[1] == lax.axis_size("lon") and tracers.shape[2] >= HALO:
        return transposed_path(tracers, courant_x, courant_y, cutoffs)
    return tiled_path(tracers, courant_x, courant_y, cutoffs)


def solution(mesh):
    in_specs = (P(None, None, "lat", "lon"), P(None, "lat", "lon"), P(None, "lat", "lon"), P())
    out_specs = P(None, None, "lat", "lon")
    return jax.shard_map(
        on_device, mesh=mesh, in_specs=in_specs, out_specs=out_specs, check_vma=False
    )
```

```python
import math

import jax
import jax.numpy as jnp
from jax import lax
from jax.sharding import PartitionSpec as P

KMAX = 720
SUBSTEPS = 2
HALO = 3
MATMUL_PRECISION = lax.Precision.HIGH


def shift(x, axis, by, wrap):
    size = lax.axis_size(axis)
    pairs = [(i, (i + by) % size) for i in range(size) if wrap or 0 <= i + by < size]
    return lax.ppermute(x, axis, pairs)


def exchange(x, axis):
    size = lax.axis_size(axis)
    me = lax.axis_index(axis)
    pieces = [lax.dynamic_index_in_dim(x, me, 0, keepdims=False)]
    for by in range(1, size):
        part = lax.dynamic_index_in_dim(x, (me + by) % size, 0, keepdims=False)
        pieces.append(shift(part, axis, by, True))
    order = (me - jnp.arange(size, dtype=jnp.int32)) % size
    return jnp.take(jnp.stack(pieces), order, axis=0)


def window(values, first_cell, last_cell, dim_at):
    return lax.slice_in_dim(values, first_cell, last_cell, axis=dim_at)


def ppm_flux(padded, courant, dim_at, cell_count):
    edge_values = 7.0 / 12.0 * (
        window(padded, 1, cell_count + 4, dim_at) + window(padded, 2, cell_count + 5, dim_at)
    ) - 1.0 / 12.0 * (
        window(padded, 0, cell_count + 3, dim_at) + window(padded, 3, cell_count + 6, dim_at)
    )
    left_edge = window(edge_values, 0, cell_count + 1, dim_at)
    mid_edge = window(edge_values, 1, cell_count + 2, dim_at)
    right_edge = window(edge_values, 2, cell_count + 3, dim_at)
    left_cell = window(padded, 2, cell_count + 3, dim_at)
    right_cell = window(padded, 3, cell_count + 4, dim_at)
    magnitude = jnp.abs(courant)
    six_left = 6.0 * left_cell - 3.0 * (left_edge + mid_edge)
    six_right = 6.0 * right_cell - 3.0 * (mid_edge + right_edge)
    from_left = mid_edge - 0.5 * magnitude * (
        mid_edge - left_edge - (1.0 - magnitude * (2.0 / 3.0)) * six_left
    )
    from_right = mid_edge + 0.5 * magnitude * (
        right_edge - mid_edge + (1.0 - magnitude * (2.0 / 3.0)) * six_right
    )
    return courant * jnp.where(courant >= 0.0, from_left, from_right)


def root_table(count):
    d = jnp.arange(count, dtype=jnp.int32)
    angle = (d[:, None] * d[None, :] % count).astype(jnp.float32) * (2.0 * math.pi / count)
    cos_dr, sin_dr = jnp.cos(angle), jnp.sin(angle)
    cos_dr = jnp.where(jnp.abs(cos_dr) < 1e-6, 0.0, cos_dr)
    sin_dr = jnp.where(jnp.abs(sin_dr) < 1e-6, 0.0, sin_dr)
    return cos_dr, sin_dr


def class_basis(tiles, cols, circle, halo=HALO):
    per_class = KMAX // tiles
    r = jnp.arange(tiles, dtype=jnp.int32)
    m = jnp.arange(per_class, dtype=jnp.int32)
    q = jnp.arange(-halo, cols + halo, dtype=jnp.int32) % circle
    k = tiles * m[None, :] + r[:, None]
    phase = (q[None, :, None] * k[:, None, :]) % circle
    angle = phase.astype(jnp.float32) * (2.0 * math.pi / circle)
    return jnp.concatenate([jnp.cos(angle), jnp.sin(angle)], axis=2)


def filter_rows(rows, basis, roots, weights, polar, halo=HALO):
    tiles, count, cols = rows.shape
    cos_dr, sin_dr = roots
    z_re = jnp.sum(cos_dr[:, :, None, None] * rows[None], axis=1)
    z_im = -jnp.sum(sin_dr[:, :, None, None] * rows[None], axis=1)
    z = jnp.concatenate([z_re, z_im], axis=1)
    z = jnp.pad(z, ((0, 0), (0, 0), (halo, halo)))
    prod = lax.dot_general(z, basis, (((2,), (1,)), ((0,), (0,))), precision=MATMUL_PRECISION)
    per_class = basis.shape[2] // 2
    zc, zs = prod[:, :count, :per_class], prod[:, :count, per_class:]
    wc, ws = prod[:, count:, :per_class], prod[:, count:, per_class:]
    real = (zc + ws) * weights
    imag = (zs - wc) * weights
    spec = jnp.concatenate(
        [jnp.concatenate([real, imag], axis=2), jnp.concatenate([-imag, real], axis=2)], axis=1
    )
    back = lax.dot_general(spec, basis, (((2,), (2,)), ((0,), (0,))), precision=MATMUL_PRECISION)
    w_re, w_im = back[:, :count], back[:, count:]
    smooth = jnp.sum(
        cos_dr[:, :, None, None] * w_re[None] - sin_dr[:, :, None, None] * w_im[None], axis=1
    )
    wide = rows
    if halo:
        left = jnp.roll(rows[:, :, cols - halo :], 1, axis=0)
        right = jnp.roll(rows[:, :, :halo], -1, axis=0)
        wide = jnp.concatenate([left, rows, right], axis=2)
    return jnp.where(polar[None, :, None], smooth, wide)


def tiled_path(tracers, courant_x, courant_y, cutoffs):
    tracer_count, level_count, lat_rows, lon_cols = tracers.shape
    field_count = tracer_count * level_count
    lat_devices = lax.axis_size("lat")
    lon_devices = lax.axis_size("lon")
    lat_index = lax.axis_index("lat")
    lon_index = lax.axis_index("lon")
    circle = lon_cols * lon_devices
    total_rows = lat_rows * lat_devices
    row_global = lat_index * lat_rows + jnp.arange(lat_rows, dtype=jnp.int32)
    face_global = lat_index * lat_rows + jnp.arange(lat_rows + 1, dtype=jnp.int32)
    face_angle = (face_global.astype(jnp.float32) / total_rows - 0.5) * math.pi
    face_weight = jnp.where(
        (face_global == 0) | (face_global == total_rows), 0.0, jnp.cos(face_angle)
    )
    center_weight = jnp.cos(((row_global.astype(jnp.float32) + 0.5) / total_rows - 0.5) * math.pi)
    is_south = lat_index == 0
    is_north = lat_index == lat_devices - 1

    count = field_count * lat_rows // lon_devices
    flat = lon_index * count + jnp.arange(count, dtype=jnp.int32)
    held_global = lat_index * lat_rows + flat % lat_rows
    polar = (held_global < total_rows // 4) | (held_global >= total_rows - total_rows // 4)
    cut = jnp.take(cutoffs, held_global)
    per_class = KMAX // lon_devices
    k = lon_devices * jnp.arange(per_class, dtype=jnp.int32)[None, :] + jnp.arange(
        lon_devices, dtype=jnp.int32
    )[:, None]
    scale = jnp.where(k == 0, 1.0 / circle, 2.0 / circle).astype(jnp.float32)
    weights = jnp.where(k[:, None, :] < cut[None, :, None], scale[:, None, :], 0.0)
    basis = class_basis(lon_devices, lon_cols, circle)
    roots = root_table(lon_devices)

    west_cx = shift(courant_x[:, :, lon_cols - 1 :], "lon", 1, True)
    north_cy = shift(courant_y[:, :1], "lat", -1, False)
    east_courant = jnp.concatenate([west_cx, courant_x], axis=2)
    north_courant = jnp.concatenate(
        [courant_y, jnp.where(is_north, 0.0, north_cy)], axis=1
    )

    def lat_halos(state):
        south_in = shift(state[:, :, lat_rows - HALO :], "lat", 1, False)
        north_in = shift(state[:, :, :HALO], "lat", -1, False)
        edge = jnp.where(is_south, state[:, :, :HALO], state[:, :, lat_rows - HALO :])
        far = shift(edge, "lon", lon_devices // 2, True)
        far_rev = jnp.concatenate([far[:, :, 2:3], far[:, :, 1:2], far[:, :, 0:1]], axis=2)
        south_rows = jnp.where(is_south, far_rev, south_in)
        north_rows = jnp.where(is_north, far_rev, north_in)
        return jnp.concatenate([south_rows, state, north_rows], axis=2)

    state = tracers
    west_in = shift(state[..., lon_cols - HALO :], "lon", 1, True)
    east_in = shift(state[..., :HALO], "lon", -1, True)
    wrapped = jnp.concatenate([west_in, state, east_in], axis=3)
    for substep in range(SUBSTEPS):
        extended = lat_halos(state)
        zonal = ppm_flux(wrapped, east_courant, 3, lon_cols)
        meridional = ppm_flux(extended, north_courant, 2, lat_rows) * face_weight[:, None]
        change = (
            zonal[..., 1:]
            - zonal[..., :-1]
            + (meridional[:, :, 1:] - meridional[:, :, :-1]) / center_weight[:, None]
        )
        state = state - change
        rows = state.reshape(lon_devices, count, lon_cols)
        rows = lax.all_to_all(rows, "lon", 0, 0)
        wide = filter_rows(rows, basis, roots, weights, polar)
        if substep == SUBSTEPS - 1:
            wide = wide[:, :, HALO : HALO + lon_cols]
        wide = lax.all_to_all(wide, "lon", 0, 0)
        wrapped = wide.reshape(tracer_count, level_count, lat_rows, wide.shape[2])
        state = wrapped if substep == SUBSTEPS - 1 else wrapped[..., HALO : HALO + lon_cols]
    return state


def transposed_path(tracers, courant_x, courant_y, cutoffs):
    tracer_count, level_count, lat_rows, lon_cols = tracers.shape
    lat_devices = lax.axis_size("lat")
    lon_devices = lax.axis_size("lon")
    lat_index = lax.axis_index("lat")
    circle = lon_cols * lon_devices
    total_rows = lat_rows * lat_devices
    row_global = lat_index * lat_rows + jnp.arange(lat_rows, dtype=jnp.int32)
    face_global = lat_index * lat_rows + jnp.arange(lat_rows + 1, dtype=jnp.int32)
    face_angle = (face_global.astype(jnp.float32) / total_rows - 0.5) * math.pi
    face_weight = jnp.where(
        (face_global == 0) | (face_global == total_rows), 0.0, jnp.cos(face_angle)
    )
    center_weight = jnp.cos(((row_global.astype(jnp.float32) + 0.5) / total_rows - 0.5) * math.pi)
    is_south = lat_index == 0
    is_north = lat_index == lat_devices - 1

    count = tracer_count * lat_rows
    payload = jnp.concatenate(
        [
            jnp.transpose(tracers, (1, 0, 2, 3)).reshape(level_count, count, lon_cols),
            courant_x,
            courant_y,
        ],
        axis=1,
    )
    payload = exchange(payload, "lon")
    state = payload[:, :count].reshape(lon_devices, tracer_count, lat_rows, lon_cols)
    cx = payload[:, None, count : count + lat_rows]
    cy = payload[:, None, count + lat_rows :]
    north_cy = jnp.where(is_north, 0.0, shift(cy[:, :, :1], "lat", -1, False))
    north_courant = jnp.concatenate([cy, north_cy], axis=2)
    east_courant = jnp.concatenate([jnp.roll(cx[..., lon_cols - 1 :], 1, axis=0), cx], axis=3)

    held_global = lat_index * lat_rows + jnp.arange(count, dtype=jnp.int32) % lat_rows
    polar = (held_global < total_rows // 4) | (held_global >= total_rows - total_rows // 4)
    cut = jnp.take(cutoffs, held_global)
    per_class = KMAX // lon_devices
    k = lon_devices * jnp.arange(per_class, dtype=jnp.int32)[None, :] + jnp.arange(
        lon_devices, dtype=jnp.int32
    )[:, None]
    scale = jnp.where(k == 0, 1.0 / circle, 2.0 / circle).astype(jnp.float32)
    weights = jnp.where(k[:, None, :] < cut[None, :, None], scale[:, None, :], 0.0)
    basis = class_basis(lon_devices, lon_cols, circle, 0)
    roots = root_table(lon_devices)

    for substep in range(SUBSTEPS):
        south_in = shift(state[:, :, lat_rows - HALO :], "lat", 1, False)
        north_in = shift(state[:, :, :HALO], "lat", -1, False)
        edge = jnp.where(is_south, state[:, :, :HALO], state[:, :, lat_rows - HALO :])
        far = jnp.roll(edge, lon_devices // 2, axis=0)
        far_rev = jnp.concatenate([far[:, :, 2:3], far[:, :, 1:2], far[:, :, 0:1]], axis=2)
        south_rows = jnp.where(is_south, far_rev, south_in)
        north_rows = jnp.where(is_north, far_rev, north_in)
        extended = jnp.concatenate([south_rows, state, north_rows], axis=2)
        wrapped = jnp.concatenate(
            [
                jnp.roll(state[..., lon_cols - HALO :], 1, axis=0),
                state,
                jnp.roll(state[..., :HALO], -1, axis=0),
            ],
            axis=3,
        )
        zonal = ppm_flux(wrapped, east_courant, 3, lon_cols)
        meridional = ppm_flux(extended, north_courant, 2, lat_rows) * face_weight[:, None]
        change = (
            zonal[..., 1:]
            - zonal[..., :-1]
            + (meridional[:, :, 1:] - meridional[:, :, :-1]) / center_weight[:, None]
        )
        state = state - change
        rows = state.reshape(lon_devices, count, lon_cols)
        rows = filter_rows(rows, basis, roots, weights, polar, 0)
        state = rows.reshape(lon_devices, tracer_count, lat_rows, lon_cols)

    tiles = exchange(state, "lon")
    return jnp.transpose(tiles, (1, 0, 2, 3))


def on_device(tracers, courant_x, courant_y, cutoffs):
    field_count = tracers.shape[0] * tracers.shape[1]
    if tracers.shape[1] == lax.axis_size("lon") and tracers.shape[2] >= HALO:
        return transposed_path(tracers, courant_x, courant_y, cutoffs)
    return tiled_path(tracers, courant_x, courant_y, cutoffs)


def solution(mesh):
    in_specs = (P(None, None, "lat", "lon"), P(None, "lat", "lon"), P(None, "lat", "lon"), P())
    out_specs = P(None, None, "lat", "lon")
    return jax.shard_map(
        on_device, mesh=mesh, in_specs=in_specs, out_specs=out_specs, check_vma=False
    )
```

```python
import math

import jax
import jax.numpy as jnp
from jax import lax
from jax.sharding import PartitionSpec as P

KMAX = 720
SUBSTEPS = 2
HALO = 3
MATMUL_PRECISION = lax.Precision.HIGH


def shift(x, axis, by, wrap):
    size = lax.axis_size(axis)
    pairs = [(i, (i + by) % size) for i in range(size) if wrap or 0 <= i + by < size]
    return lax.ppermute(x, axis, pairs)


def gather_arrival(x, axis):
    size = lax.axis_size(axis)
    me = lax.axis_index(axis)
    pieces = [lax.dynamic_index_in_dim(x, me, 0, keepdims=False)]
    for by in range(1, size):
        part = lax.dynamic_index_in_dim(x, (me + by) % size, 0, keepdims=False)
        pieces.append(shift(part, axis, by, True))
    return jnp.stack(pieces)


def scatter_arrival(x, axis):
    size = lax.axis_size(axis)
    me = lax.axis_index(axis)
    pieces = [x[0]] + [shift(x[(size - by) % size], axis, by, True) for by in range(1, size)]
    order = (me - jnp.arange(size, dtype=jnp.int32)) % size
    return jnp.take(jnp.stack(pieces), order, axis=0)


def product_basis(tiles, cols, circle):
    split = max(b for b in range(1, cols + 1) if cols % b == 0 and b * b <= cols)
    per_class = KMAX // tiles
    k = tiles * jnp.arange(per_class, dtype=jnp.int32)[None, :] + jnp.arange(
        tiles, dtype=jnp.int32
    )[:, None]
    a = jnp.arange(cols // split, dtype=jnp.int32)
    b = jnp.arange(split, dtype=jnp.int32)
    step = 2.0 * math.pi / circle
    coarse = ((split * a[None, :, None] * k[:, None, :]) % circle).astype(jnp.float32) * step
    fine = ((b[None, :, None] * k[:, None, :]) % circle).astype(jnp.float32) * step
    ca, sa = jnp.cos(coarse)[:, :, None], jnp.sin(coarse)[:, :, None]
    cb, sb = jnp.cos(fine)[:, None], jnp.sin(fine)[:, None]
    cos_qk = (ca * cb - sa * sb).reshape(tiles, cols, per_class)
    sin_qk = (sa * cb + ca * sb).reshape(tiles, cols, per_class)
    return jnp.concatenate([cos_qk, sin_qk], axis=2)


def window(values, first_cell, last_cell, dim_at):
    return lax.slice_in_dim(values, first_cell, last_cell, axis=dim_at)


def ppm_flux(padded, courant, dim_at, cell_count):
    edge_values = 7.0 / 12.0 * (
        window(padded, 1, cell_count + 4, dim_at) + window(padded, 2, cell_count + 5, dim_at)
    ) - 1.0 / 12.0 * (
        window(padded, 0, cell_count + 3, dim_at) + window(padded, 3, cell_count + 6, dim_at)
    )
    left_edge = window(edge_values, 0, cell_count + 1, dim_at)
    mid_edge = window(edge_values, 1, cell_count + 2, dim_at)
    right_edge = window(edge_values, 2, cell_count + 3, dim_at)
    left_cell = window(padded, 2, cell_count + 3, dim_at)
    right_cell = window(padded, 3, cell_count + 4, dim_at)
    magnitude = jnp.abs(courant)
    six_left = 6.0 * left_cell - 3.0 * (left_edge + mid_edge)
    six_right = 6.0 * right_cell - 3.0 * (mid_edge + right_edge)
    from_left = mid_edge - 0.5 * magnitude * (
        mid_edge - left_edge - (1.0 - magnitude * (2.0 / 3.0)) * six_left
    )
    from_right = mid_edge + 0.5 * magnitude * (
        right_edge - mid_edge + (1.0 - magnitude * (2.0 / 3.0)) * six_right
    )
    return courant * jnp.where(courant >= 0.0, from_left, from_right)


def root_table(count, tile_of=None):
    d = jnp.arange(count, dtype=jnp.int32)
    tile = d if tile_of is None else tile_of
    angle = (d[:, None] * tile[None, :] % count).astype(jnp.float32) * (2.0 * math.pi / count)
    cos_dr, sin_dr = jnp.cos(angle), jnp.sin(angle)
    cos_dr = jnp.where(jnp.abs(cos_dr) < 1e-6, 0.0, cos_dr)
    sin_dr = jnp.where(jnp.abs(sin_dr) < 1e-6, 0.0, sin_dr)
    return cos_dr, sin_dr


def class_basis(tiles, cols, circle, halo=HALO):
    per_class = KMAX // tiles
    r = jnp.arange(tiles, dtype=jnp.int32)
    m = jnp.arange(per_class, dtype=jnp.int32)
    q = jnp.arange(-halo, cols + halo, dtype=jnp.int32) % circle
    k = tiles * m[None, :] + r[:, None]
    phase = (q[None, :, None] * k[:, None, :]) % circle
    angle = phase.astype(jnp.float32) * (2.0 * math.pi / circle)
    return jnp.concatenate([jnp.cos(angle), jnp.sin(angle)], axis=2)


def filter_rows(rows, basis, roots, weights, polar, halo=HALO):
    tiles, count, cols = rows.shape
    cos_dr, sin_dr = roots
    z_re = jnp.sum(cos_dr[:, :, None, None] * rows[None], axis=1)
    z_im = -jnp.sum(sin_dr[:, :, None, None] * rows[None], axis=1)
    z = jnp.concatenate([z_re, z_im], axis=1)
    z = jnp.pad(z, ((0, 0), (0, 0), (halo, halo)))
    prod = lax.dot_general(z, basis, (((2,), (1,)), ((0,), (0,))), precision=MATMUL_PRECISION)
    per_class = basis.shape[2] // 2
    zc, zs = prod[:, :count, :per_class], prod[:, :count, per_class:]
    wc, ws = prod[:, count:, :per_class], prod[:, count:, per_class:]
    real = (zc + ws) * weights
    imag = (zs - wc) * weights
    spec = jnp.concatenate(
        [jnp.concatenate([real, imag], axis=2), jnp.concatenate([-imag, real], axis=2)], axis=1
    )
    back = lax.dot_general(spec, basis, (((2,), (2,)), ((0,), (0,))), precision=MATMUL_PRECISION)
    w_re, w_im = back[:, :count], back[:, count:]
    smooth = jnp.sum(
        cos_dr[:, :, None, None] * w_re[:, None] - sin_dr[:, :, None, None] * w_im[:, None], axis=0
    )
    wide = rows
    if halo:
        left = jnp.roll(rows[:, :, cols - halo :], 1, axis=0)
        right = jnp.roll(rows[:, :, :halo], -1, axis=0)
        wide = jnp.concatenate([left, rows, right], axis=2)
    return jnp.where(polar[None, :, None], smooth, wide)


def tiled_path(tracers, courant_x, courant_y, cutoffs):
    tracer_count, level_count, lat_rows, lon_cols = tracers.shape
    field_count = tracer_count * level_count
    lat_devices = lax.axis_size("lat")
    lon_devices = lax.axis_size("lon")
    lat_index = lax.axis_index("lat")
    lon_index = lax.axis_index("lon")
    circle = lon_cols * lon_devices
    total_rows = lat_rows * lat_devices
    row_global = lat_index * lat_rows + jnp.arange(lat_rows, dtype=jnp.int32)
    face_global = lat_index * lat_rows + jnp.arange(lat_rows + 1, dtype=jnp.int32)
    face_angle = (face_global.astype(jnp.float32) / total_rows - 0.5) * math.pi
    face_weight = jnp.where(
        (face_global == 0) | (face_global == total_rows), 0.0, jnp.cos(face_angle)
    )
    center_weight = jnp.cos(((row_global.astype(jnp.float32) + 0.5) / total_rows - 0.5) * math.pi)
    is_south = lat_index == 0
    is_north = lat_index == lat_devices - 1

    count = field_count * lat_rows // lon_devices
    flat = lon_index * count + jnp.arange(count, dtype=jnp.int32)
    held_global = lat_index * lat_rows + flat % lat_rows
    polar = (held_global < total_rows // 4) | (held_global >= total_rows - total_rows // 4)
    cut = jnp.take(cutoffs, held_global)
    per_class = KMAX // lon_devices
    k = lon_devices * jnp.arange(per_class, dtype=jnp.int32)[None, :] + jnp.arange(
        lon_devices, dtype=jnp.int32
    )[:, None]
    scale = jnp.where(k == 0, 1.0 / circle, 2.0 / circle).astype(jnp.float32)
    weights = jnp.where(k[:, None, :] < cut[None, :, None], scale[:, None, :], 0.0)
    basis = class_basis(lon_devices, lon_cols, circle)
    roots = root_table(lon_devices)

    west_cx = shift(courant_x[:, :, lon_cols - 1 :], "lon", 1, True)
    north_cy = shift(courant_y[:, :1], "lat", -1, False)
    east_courant = jnp.concatenate([west_cx, courant_x], axis=2)
    north_courant = jnp.concatenate(
        [courant_y, jnp.where(is_north, 0.0, north_cy)], axis=1
    )

    def lat_halos(state):
        south_in = shift(state[:, :, lat_rows - HALO :], "lat", 1, False)
        north_in = shift(state[:, :, :HALO], "lat", -1, False)
        edge = jnp.where(is_south, state[:, :, :HALO], state[:, :, lat_rows - HALO :])
        far = shift(edge, "lon", lon_devices // 2, True)
        far_rev = jnp.concatenate([far[:, :, 2:3], far[:, :, 1:2], far[:, :, 0:1]], axis=2)
        south_rows = jnp.where(is_south, far_rev, south_in)
        north_rows = jnp.where(is_north, far_rev, north_in)
        return jnp.concatenate([south_rows, state, north_rows], axis=2)

    state = tracers
    west_in = shift(state[..., lon_cols - HALO :], "lon", 1, True)
    east_in = shift(state[..., :HALO], "lon", -1, True)
    wrapped = jnp.concatenate([west_in, state, east_in], axis=3)
    for substep in range(SUBSTEPS):
        extended = lat_halos(state)
        zonal = ppm_flux(wrapped, east_courant, 3, lon_cols)
        meridional = ppm_flux(extended, north_courant, 2, lat_rows) * face_weight[:, None]
        change = (
            zonal[..., 1:]
            - zonal[..., :-1]
            + (meridional[:, :, 1:] - meridional[:, :, :-1]) / center_weight[:, None]
        )
        state = state - change
        rows = state.reshape(lon_devices, count, lon_cols)
        rows = lax.all_to_all(rows, "lon", 0, 0)
        wide = filter_rows(rows, basis, roots, weights, polar)
        if substep == SUBSTEPS - 1:
            wide = wide[:, :, HALO : HALO + lon_cols]
        wide = lax.all_to_all(wide, "lon", 0, 0)
        wrapped = wide.reshape(tracer_count, level_count, lat_rows, wide.shape[2])
        state = wrapped if substep == SUBSTEPS - 1 else wrapped[..., HALO : HALO + lon_cols]
    return state


def transposed_path(tracers, courant_x, courant_y, cutoffs):
    tracer_count, level_count, lat_rows, lon_cols = tracers.shape
    lat_devices = lax.axis_size("lat")
    lon_devices = lax.axis_size("lon")
    lat_index = lax.axis_index("lat")
    circle = lon_cols * lon_devices
    total_rows = lat_rows * lat_devices
    row_global = lat_index * lat_rows + jnp.arange(lat_rows, dtype=jnp.int32)
    face_global = lat_index * lat_rows + jnp.arange(lat_rows + 1, dtype=jnp.int32)
    face_angle = (face_global.astype(jnp.float32) / total_rows - 0.5) * math.pi
    face_weight = jnp.where(
        (face_global == 0) | (face_global == total_rows), 0.0, jnp.cos(face_angle)
    )
    center_weight = jnp.cos(((row_global.astype(jnp.float32) + 0.5) / total_rows - 0.5) * math.pi)
    is_south = lat_index == 0
    is_north = lat_index == lat_devices - 1

    count = tracer_count * lat_rows
    payload = jnp.concatenate(
        [
            jnp.transpose(tracers, (1, 0, 2, 3)).reshape(level_count, count, lon_cols),
            courant_x,
            courant_y,
        ],
        axis=1,
    )
    payload = gather_arrival(payload, "lon")
    state = payload[:, :count].reshape(lon_devices, tracer_count, lat_rows, lon_cols)
    cx = payload[:, None, count : count + lat_rows]
    cy = payload[:, None, count + lat_rows :]
    north_cy = jnp.where(is_north, 0.0, shift(cy[:, :, :1], "lat", -1, False))
    north_courant = jnp.concatenate([cy, north_cy], axis=2)
    east_courant = jnp.concatenate([jnp.roll(cx[..., lon_cols - 1 :], -1, axis=0), cx], axis=3)

    held_global = lat_index * lat_rows + jnp.arange(count, dtype=jnp.int32) % lat_rows
    polar = (held_global < total_rows // 4) | (held_global >= total_rows - total_rows // 4)
    cut = jnp.take(cutoffs, held_global)
    per_class = KMAX // lon_devices
    k = lon_devices * jnp.arange(per_class, dtype=jnp.int32)[None, :] + jnp.arange(
        lon_devices, dtype=jnp.int32
    )[:, None]
    scale = jnp.where(k == 0, 1.0 / circle, 2.0 / circle).astype(jnp.float32)
    weights = jnp.where(k[:, None, :] < cut[None, :, None], scale[:, None, :], 0.0)
    basis = product_basis(lon_devices, lon_cols, circle)
    roots = root_table(
        lon_devices, (lax.axis_index("lon") - jnp.arange(lon_devices, dtype=jnp.int32)) % lon_devices
    )

    for substep in range(SUBSTEPS):
        south_in = shift(state[:, :, lat_rows - HALO :], "lat", 1, False)
        north_in = shift(state[:, :, :HALO], "lat", -1, False)
        edge = jnp.where(is_south, state[:, :, :HALO], state[:, :, lat_rows - HALO :])
        far = jnp.roll(edge, lon_devices // 2, axis=0)
        far_rev = jnp.concatenate([far[:, :, 2:3], far[:, :, 1:2], far[:, :, 0:1]], axis=2)
        south_rows = jnp.where(is_south, far_rev, south_in)
        north_rows = jnp.where(is_north, far_rev, north_in)
        extended = jnp.concatenate([south_rows, state, north_rows], axis=2)
        wrapped = jnp.concatenate(
            [
                jnp.roll(state[..., lon_cols - HALO :], -1, axis=0),
                state,
                jnp.roll(state[..., :HALO], 1, axis=0),
            ],
            axis=3,
        )
        zonal = ppm_flux(wrapped, east_courant, 3, lon_cols)
        meridional = ppm_flux(extended, north_courant, 2, lat_rows) * face_weight[:, None]
        change = (
            zonal[..., 1:]
            - zonal[..., :-1]
            + (meridional[:, :, 1:] - meridional[:, :, :-1]) / center_weight[:, None]
        )
        state = state - change
        rows = state.reshape(lon_devices, count, lon_cols)
        rows = filter_rows(rows, basis, roots, weights, polar, 0)
        state = rows.reshape(lon_devices, tracer_count, lat_rows, lon_cols)

    tiles = scatter_arrival(state, "lon")
    return jnp.transpose(tiles, (1, 0, 2, 3))


def on_device(tracers, courant_x, courant_y, cutoffs):
    field_count = tracers.shape[0] * tracers.shape[1]
    if tracers.shape[1] == lax.axis_size("lon") and tracers.shape[2] >= HALO:
        return transposed_path(tracers, courant_x, courant_y, cutoffs)
    return tiled_path(tracers, courant_x, courant_y, cutoffs)


def solution(mesh):
    in_specs = (P(None, None, "lat", "lon"), P(None, "lat", "lon"), P(None, "lat", "lon"), P())
    out_specs = P(None, None, "lat", "lon")
    return jax.shard_map(
        on_device, mesh=mesh, in_specs=in_specs, out_specs=out_specs, check_vma=False
    )
```

```python
import math

import jax
import jax.numpy as jnp
from jax import lax
from jax.sharding import PartitionSpec as P

KMAX = 720
SUBSTEPS = 2
HALO = 3
MATMUL_PRECISION = lax.Precision.HIGH


def shift(x, axis, by, wrap):
    size = lax.axis_size(axis)
    pairs = [(i, (i + by) % size) for i in range(size) if wrap or 0 <= i + by < size]
    return lax.ppermute(x, axis, pairs)


def product_basis(tiles, cols, circle):
    split = max(b for b in range(1, cols + 1) if cols % b == 0 and b * b <= cols)
    per_class = KMAX // tiles
    k = tiles * jnp.arange(per_class, dtype=jnp.int32)[None, :] + jnp.arange(
        tiles, dtype=jnp.int32
    )[:, None]
    a = jnp.arange(cols // split, dtype=jnp.int32)
    b = jnp.arange(split, dtype=jnp.int32)
    step = 2.0 * math.pi / circle
    coarse = ((split * a[None, :, None] * k[:, None, :]) % circle).astype(jnp.float32) * step
    fine = ((b[None, :, None] * k[:, None, :]) % circle).astype(jnp.float32) * step
    ca, sa = jnp.cos(coarse)[:, :, None], jnp.sin(coarse)[:, :, None]
    cb, sb = jnp.cos(fine)[:, None], jnp.sin(fine)[:, None]
    cos_qk = (ca * cb - sa * sb).reshape(tiles, cols, per_class)
    sin_qk = (sa * cb + ca * sb).reshape(tiles, cols, per_class)
    return jnp.concatenate([cos_qk, sin_qk], axis=2)


def window(values, first_cell, last_cell, dim_at):
    return lax.slice_in_dim(values, first_cell, last_cell, axis=dim_at)


def ppm_flux(padded, courant, dim_at, cell_count):
    edge_values = 7.0 / 12.0 * (
        window(padded, 1, cell_count + 4, dim_at) + window(padded, 2, cell_count + 5, dim_at)
    ) - 1.0 / 12.0 * (
        window(padded, 0, cell_count + 3, dim_at) + window(padded, 3, cell_count + 6, dim_at)
    )
    left_edge = window(edge_values, 0, cell_count + 1, dim_at)
    mid_edge = window(edge_values, 1, cell_count + 2, dim_at)
    right_edge = window(edge_values, 2, cell_count + 3, dim_at)
    left_cell = window(padded, 2, cell_count + 3, dim_at)
    right_cell = window(padded, 3, cell_count + 4, dim_at)
    magnitude = jnp.abs(courant)
    six_left = 6.0 * left_cell - 3.0 * (left_edge + mid_edge)
    six_right = 6.0 * right_cell - 3.0 * (mid_edge + right_edge)
    from_left = mid_edge - 0.5 * magnitude * (
        mid_edge - left_edge - (1.0 - magnitude * (2.0 / 3.0)) * six_left
    )
    from_right = mid_edge + 0.5 * magnitude * (
        right_edge - mid_edge + (1.0 - magnitude * (2.0 / 3.0)) * six_right
    )
    return courant * jnp.where(courant >= 0.0, from_left, from_right)


def root_table(count, tile_of=None):
    d = jnp.arange(count, dtype=jnp.int32)
    tile = d if tile_of is None else tile_of
    angle = (d[:, None] * tile[None, :] % count).astype(jnp.float32) * (2.0 * math.pi / count)
    cos_dr, sin_dr = jnp.cos(angle), jnp.sin(angle)
    cos_dr = jnp.where(jnp.abs(cos_dr) < 1e-6, 0.0, cos_dr)
    sin_dr = jnp.where(jnp.abs(sin_dr) < 1e-6, 0.0, sin_dr)
    return cos_dr, sin_dr


def class_basis(tiles, cols, circle, halo=HALO):
    per_class = KMAX // tiles
    r = jnp.arange(tiles, dtype=jnp.int32)
    m = jnp.arange(per_class, dtype=jnp.int32)
    q = jnp.arange(-halo, cols + halo, dtype=jnp.int32) % circle
    k = tiles * m[None, :] + r[:, None]
    phase = (q[None, :, None] * k[:, None, :]) % circle
    angle = phase.astype(jnp.float32) * (2.0 * math.pi / circle)
    return jnp.concatenate([jnp.cos(angle), jnp.sin(angle)], axis=2)


def filter_rows(rows, basis, roots, weights, polar, halo=HALO):
    tiles, count, cols = rows.shape
    cos_dr, sin_dr = roots
    z_re = jnp.sum(cos_dr[:, :, None, None] * rows[None], axis=1)
    z_im = -jnp.sum(sin_dr[:, :, None, None] * rows[None], axis=1)
    z = jnp.concatenate([z_re, z_im], axis=1)
    z = jnp.pad(z, ((0, 0), (0, 0), (halo, halo)))
    prod = lax.dot_general(z, basis, (((2,), (1,)), ((0,), (0,))), precision=MATMUL_PRECISION)
    per_class = basis.shape[2] // 2
    zc, zs = prod[:, :count, :per_class], prod[:, :count, per_class:]
    wc, ws = prod[:, count:, :per_class], prod[:, count:, per_class:]
    real = (zc + ws) * weights
    imag = (zs - wc) * weights
    spec = jnp.concatenate(
        [jnp.concatenate([real, imag], axis=2), jnp.concatenate([-imag, real], axis=2)], axis=1
    )
    back = lax.dot_general(spec, basis, (((2,), (2,)), ((0,), (0,))), precision=MATMUL_PRECISION)
    w_re, w_im = back[:, :count], back[:, count:]
    smooth = jnp.sum(
        cos_dr[:, :, None, None] * w_re[:, None] - sin_dr[:, :, None, None] * w_im[:, None], axis=0
    )
    wide = rows
    if halo:
        left = jnp.roll(rows[:, :, cols - halo :], 1, axis=0)
        right = jnp.roll(rows[:, :, :halo], -1, axis=0)
        wide = jnp.concatenate([left, rows, right], axis=2)
    return jnp.where(polar[None, :, None], smooth, wide)


def tiled_path(tracers, courant_x, courant_y, cutoffs):
    tracer_count, level_count, lat_rows, lon_cols = tracers.shape
    field_count = tracer_count * level_count
    lat_devices = lax.axis_size("lat")
    lon_devices = lax.axis_size("lon")
    lat_index = lax.axis_index("lat")
    lon_index = lax.axis_index("lon")
    circle = lon_cols * lon_devices
    total_rows = lat_rows * lat_devices
    row_global = lat_index * lat_rows + jnp.arange(lat_rows, dtype=jnp.int32)
    face_global = lat_index * lat_rows + jnp.arange(lat_rows + 1, dtype=jnp.int32)
    face_angle = (face_global.astype(jnp.float32) / total_rows - 0.5) * math.pi
    face_weight = jnp.where(
        (face_global == 0) | (face_global == total_rows), 0.0, jnp.cos(face_angle)
    )
    center_weight = jnp.cos(((row_global.astype(jnp.float32) + 0.5) / total_rows - 0.5) * math.pi)
    is_south = lat_index == 0
    is_north = lat_index == lat_devices - 1

    count = field_count * lat_rows // lon_devices
    flat = lon_index * count + jnp.arange(count, dtype=jnp.int32)
    held_global = lat_index * lat_rows + flat % lat_rows
    polar = (held_global < total_rows // 4) | (held_global >= total_rows - total_rows // 4)
    cut = jnp.take(cutoffs, held_global)
    per_class = KMAX // lon_devices
    k = lon_devices * jnp.arange(per_class, dtype=jnp.int32)[None, :] + jnp.arange(
        lon_devices, dtype=jnp.int32
    )[:, None]
    scale = jnp.where(k == 0, 1.0 / circle, 2.0 / circle).astype(jnp.float32)
    weights = jnp.where(k[:, None, :] < cut[None, :, None], scale[:, None, :], 0.0)
    basis = class_basis(lon_devices, lon_cols, circle)
    roots = root_table(lon_devices)

    west_cx = shift(courant_x[:, :, lon_cols - 1 :], "lon", 1, True)
    north_cy = shift(courant_y[:, :1], "lat", -1, False)
    east_courant = jnp.concatenate([west_cx, courant_x], axis=2)
    north_courant = jnp.concatenate(
        [courant_y, jnp.where(is_north, 0.0, north_cy)], axis=1
    )

    def lat_halos(state):
        south_in = shift(state[:, :, lat_rows - HALO :], "lat", 1, False)
        north_in = shift(state[:, :, :HALO], "lat", -1, False)
        edge = jnp.where(is_south, state[:, :, :HALO], state[:, :, lat_rows - HALO :])
        far = shift(edge, "lon", lon_devices // 2, True)
        far_rev = jnp.concatenate([far[:, :, 2:3], far[:, :, 1:2], far[:, :, 0:1]], axis=2)
        south_rows = jnp.where(is_south, far_rev, south_in)
        north_rows = jnp.where(is_north, far_rev, north_in)
        return jnp.concatenate([south_rows, state, north_rows], axis=2)

    state = tracers
    west_in = shift(state[..., lon_cols - HALO :], "lon", 1, True)
    east_in = shift(state[..., :HALO], "lon", -1, True)
    wrapped = jnp.concatenate([west_in, state, east_in], axis=3)
    for substep in range(SUBSTEPS):
        extended = lat_halos(state)
        zonal = ppm_flux(wrapped, east_courant, 3, lon_cols)
        meridional = ppm_flux(extended, north_courant, 2, lat_rows) * face_weight[:, None]
        change = (
            zonal[..., 1:]
            - zonal[..., :-1]
            + (meridional[:, :, 1:] - meridional[:, :, :-1]) / center_weight[:, None]
        )
        state = state - change
        rows = state.reshape(lon_devices, count, lon_cols)
        rows = lax.all_to_all(rows, "lon", 0, 0)
        wide = filter_rows(rows, basis, roots, weights, polar)
        if substep == SUBSTEPS - 1:
            wide = wide[:, :, HALO : HALO + lon_cols]
        wide = lax.all_to_all(wide, "lon", 0, 0)
        wrapped = wide.reshape(tracer_count, level_count, lat_rows, wide.shape[2])
        state = wrapped if substep == SUBSTEPS - 1 else wrapped[..., HALO : HALO + lon_cols]
    return state


def transposed_path(tracers, courant_x, courant_y, cutoffs):
    tracer_count, level_count, lat_rows, lon_cols = tracers.shape
    lat_devices = lax.axis_size("lat")
    lon_devices = lax.axis_size("lon")
    lat_index = lax.axis_index("lat")
    circle = lon_cols * lon_devices
    total_rows = lat_rows * lat_devices
    row_global = lat_index * lat_rows + jnp.arange(lat_rows, dtype=jnp.int32)
    face_global = lat_index * lat_rows + jnp.arange(lat_rows + 1, dtype=jnp.int32)
    face_angle = (face_global.astype(jnp.float32) / total_rows - 0.5) * math.pi
    face_weight = jnp.where(
        (face_global == 0) | (face_global == total_rows), 0.0, jnp.cos(face_angle)
    )
    center_weight = jnp.cos(((row_global.astype(jnp.float32) + 0.5) / total_rows - 0.5) * math.pi)
    is_south = lat_index == 0
    is_north = lat_index == lat_devices - 1

    count = tracer_count * lat_rows
    lon_index = lax.axis_index("lon")

    def payload_for(level):
        return jnp.concatenate(
            [
                lax.dynamic_index_in_dim(tracers, level, 1, keepdims=False).reshape(count, lon_cols),
                lax.dynamic_index_in_dim(courant_x, level, 0, keepdims=False),
                lax.dynamic_index_in_dim(courant_y, level, 0, keepdims=False),
            ],
            axis=0,
        )

    pieces = [payload_for(lon_index)]
    for by in range(1, lon_devices):
        pieces.append(shift(payload_for((lon_index + by) % lon_devices), "lon", by, True))
    payload = jnp.stack(pieces)
    state = payload[:, :count].reshape(lon_devices, tracer_count, lat_rows, lon_cols)
    cx = payload[:, None, count : count + lat_rows]
    cy = payload[:, None, count + lat_rows :]
    east_courant = jnp.concatenate([jnp.roll(cx[..., lon_cols - 1 :], -1, axis=0), cx], axis=3)

    held_global = lat_index * lat_rows + jnp.arange(count, dtype=jnp.int32) % lat_rows
    polar = (held_global < total_rows // 4) | (held_global >= total_rows - total_rows // 4)
    cut = jnp.take(cutoffs, held_global)
    per_class = KMAX // lon_devices
    k = lon_devices * jnp.arange(per_class, dtype=jnp.int32)[None, :] + jnp.arange(
        lon_devices, dtype=jnp.int32
    )[:, None]
    scale = jnp.where(k == 0, 1.0 / circle, 2.0 / circle).astype(jnp.float32)
    weights = jnp.where(k[:, None, :] < cut[None, :, None], scale[:, None, :], 0.0)
    basis = product_basis(lon_devices, lon_cols, circle)
    roots = root_table(
        lon_devices, (lax.axis_index("lon") - jnp.arange(lon_devices, dtype=jnp.int32)) % lon_devices
    )

    for substep in range(SUBSTEPS):
        south_in = shift(state[:, :, lat_rows - HALO :], "lat", 1, False)
        if substep == 0:
            going = jnp.concatenate(
                [state[:, :, :HALO].reshape(lon_devices, tracer_count * HALO, lon_cols), cy[:, 0, :1]],
                axis=1,
            )
            coming = shift(going, "lat", -1, False)
            north_in = coming[:, : tracer_count * HALO].reshape(
                lon_devices, tracer_count, HALO, lon_cols
            )
            north_cy = jnp.where(is_north, 0.0, coming[:, None, tracer_count * HALO :])
            north_courant = jnp.concatenate([cy, north_cy], axis=2)
        else:
            north_in = shift(state[:, :, :HALO], "lat", -1, False)
        edge = jnp.where(is_south, state[:, :, :HALO], state[:, :, lat_rows - HALO :])
        far = jnp.roll(edge, lon_devices // 2, axis=0)
        far_rev = jnp.concatenate([far[:, :, 2:3], far[:, :, 1:2], far[:, :, 0:1]], axis=2)
        south_rows = jnp.where(is_south, far_rev, south_in)
        north_rows = jnp.where(is_north, far_rev, north_in)
        extended = jnp.concatenate([south_rows, state, north_rows], axis=2)
        wrapped = jnp.concatenate(
            [
                jnp.roll(state[..., lon_cols - HALO :], -1, axis=0),
                state,
                jnp.roll(state[..., :HALO], 1, axis=0),
            ],
            axis=3,
        )
        zonal = ppm_flux(wrapped, east_courant, 3, lon_cols)
        meridional = ppm_flux(extended, north_courant, 2, lat_rows) * face_weight[:, None]
        change = (
            zonal[..., 1:]
            - zonal[..., :-1]
            + (meridional[:, :, 1:] - meridional[:, :, :-1]) / center_weight[:, None]
        )
        state = state - change
        rows = state.reshape(lon_devices, count, lon_cols)
        rows = filter_rows(rows, basis, roots, weights, polar, 0)
        state = rows.reshape(lon_devices, tracer_count, lat_rows, lon_cols)

    back = [state[0]] + [
        shift(state[(lon_devices - by) % lon_devices], "lon", by, True) for by in range(1, lon_devices)
    ]
    levels = []
    for level in range(level_count):
        pick = back[0]
        for by in range(1, lon_devices):
            pick = jnp.where((lon_index - by) % lon_devices == level, back[by], pick)
        levels.append(pick)
    return jnp.stack(levels, axis=1)


def on_device(tracers, courant_x, courant_y, cutoffs):
    field_count = tracers.shape[0] * tracers.shape[1]
    if tracers.shape[1] == lax.axis_size("lon") and tracers.shape[2] >= HALO:
        return transposed_path(tracers, courant_x, courant_y, cutoffs)
    return tiled_path(tracers, courant_x, courant_y, cutoffs)


def solution(mesh):
    in_specs = (P(None, None, "lat", "lon"), P(None, "lat", "lon"), P(None, "lat", "lon"), P())
    out_specs = P(None, None, "lat", "lon")
    return jax.shard_map(
        on_device, mesh=mesh, in_specs=in_specs, out_specs=out_specs, check_vma=False
    )
```

```python
import math

import jax
import jax.numpy as jnp
from jax import lax
from jax.sharding import PartitionSpec as P

KMAX = 720
SUBSTEPS = 2
HALO = 3


def shift(x, axis, by, wrap):
    size = lax.axis_size(axis)
    pairs = [(i, (i + by) % size) for i in range(size) if wrap or 0 <= i + by < size]
    return lax.ppermute(x, axis, pairs)


def product_basis(tiles, cols, circle):
    split = max(b for b in range(1, cols + 1) if cols % b == 0 and b * b <= cols)
    per_class = KMAX // tiles
    k = tiles * jnp.arange(per_class, dtype=jnp.int32)[None, :] + jnp.arange(
        tiles, dtype=jnp.int32
    )[:, None]
    a = jnp.arange(cols // split, dtype=jnp.int32)
    b = jnp.arange(split, dtype=jnp.int32)
    step = 2.0 * math.pi / circle
    coarse = ((split * a[None, :, None] * k[:, None, :]) % circle).astype(jnp.float32) * step
    fine = ((b[None, :, None] * k[:, None, :]) % circle).astype(jnp.float32) * step
    ca, sa = jnp.cos(coarse)[:, :, None], jnp.sin(coarse)[:, :, None]
    cb, sb = jnp.cos(fine)[:, None], jnp.sin(fine)[:, None]
    cos_qk = (ca * cb - sa * sb).reshape(tiles, cols, per_class)
    sin_qk = (sa * cb + ca * sb).reshape(tiles, cols, per_class)
    return jnp.concatenate([cos_qk, sin_qk], axis=2)


def window(values, first_cell, last_cell, dim_at):
    return lax.slice_in_dim(values, first_cell, last_cell, axis=dim_at)


def ppm_flux(padded, courant, dim_at, cell_count):
    edge_values = 7.0 / 12.0 * (
        window(padded, 1, cell_count + 4, dim_at) + window(padded, 2, cell_count + 5, dim_at)
    ) - 1.0 / 12.0 * (
        window(padded, 0, cell_count + 3, dim_at) + window(padded, 3, cell_count + 6, dim_at)
    )
    left_edge = window(edge_values, 0, cell_count + 1, dim_at)
    mid_edge = window(edge_values, 1, cell_count + 2, dim_at)
    right_edge = window(edge_values, 2, cell_count + 3, dim_at)
    left_cell = window(padded, 2, cell_count + 3, dim_at)
    right_cell = window(padded, 3, cell_count + 4, dim_at)
    magnitude = jnp.abs(courant)
    six_left = 6.0 * left_cell - 3.0 * (left_edge + mid_edge)
    six_right = 6.0 * right_cell - 3.0 * (mid_edge + right_edge)
    from_left = mid_edge - 0.5 * magnitude * (
        mid_edge - left_edge - (1.0 - magnitude * (2.0 / 3.0)) * six_left
    )
    from_right = mid_edge + 0.5 * magnitude * (
        right_edge - mid_edge + (1.0 - magnitude * (2.0 / 3.0)) * six_right
    )
    return courant * jnp.where(courant >= 0.0, from_left, from_right)


def root_table(count, tile_of=None):
    d = jnp.arange(count, dtype=jnp.int32)
    tile = d if tile_of is None else tile_of
    angle = (d[:, None] * tile[None, :] % count).astype(jnp.float32) * (2.0 * math.pi / count)
    cos_dr, sin_dr = jnp.cos(angle), jnp.sin(angle)
    cos_dr = jnp.where(jnp.abs(cos_dr) < 1e-6, 0.0, cos_dr)
    sin_dr = jnp.where(jnp.abs(sin_dr) < 1e-6, 0.0, sin_dr)
    return cos_dr, sin_dr


def class_basis(tiles, cols, circle, halo=HALO):
    per_class = KMAX // tiles
    r = jnp.arange(tiles, dtype=jnp.int32)
    m = jnp.arange(per_class, dtype=jnp.int32)
    q = jnp.arange(-halo, cols + halo, dtype=jnp.int32) % circle
    k = tiles * m[None, :] + r[:, None]
    phase = (q[None, :, None] * k[:, None, :]) % circle
    angle = phase.astype(jnp.float32) * (2.0 * math.pi / circle)
    return jnp.concatenate([jnp.cos(angle), jnp.sin(angle)], axis=2)


def split_bf16(x):
    high = lax.reduce_precision(x, exponent_bits=8, mantissa_bits=7)
    return high.astype(jnp.bfloat16), (x - high).astype(jnp.bfloat16)


def split_basis(basis):
    high, low = split_bf16(basis)
    return jnp.concatenate([high, low, high], axis=1), jnp.concatenate([high, low, high], axis=2)


def three_products(lhs, rhs, lhs_axis, rhs_axis):
    high, low = split_bf16(lhs)
    wide = jnp.concatenate([high, high, low], axis=2)
    return lax.dot_general(
        wide, rhs, (((2,), (rhs_axis,)), ((0,), (0,))), preferred_element_type=jnp.float32
    )


def filter_rows(rows, bases, roots, weights, polar, halo=HALO):
    tiles, count, cols = rows.shape
    along_q, along_m = bases
    cos_dr, sin_dr = roots
    z_re = jnp.sum(cos_dr[:, :, None, None] * rows[None], axis=1)
    z_im = -jnp.sum(sin_dr[:, :, None, None] * rows[None], axis=1)
    z = jnp.concatenate([z_re, z_im], axis=1)
    z = jnp.pad(z, ((0, 0), (0, 0), (halo, halo)))
    prod = three_products(z, along_q, 2, 1)
    per_class = along_m.shape[2] // 6
    zc, zs = prod[:, :count, :per_class], prod[:, :count, per_class:]
    wc, ws = prod[:, count:, :per_class], prod[:, count:, per_class:]
    real = (zc + ws) * weights
    imag = (zs - wc) * weights
    spec = jnp.concatenate(
        [jnp.concatenate([real, imag], axis=2), jnp.concatenate([-imag, real], axis=2)], axis=1
    )
    back = three_products(spec, along_m, 2, 2)
    w_re, w_im = back[:, :count], back[:, count:]
    smooth = jnp.sum(
        cos_dr[:, :, None, None] * w_re[:, None] - sin_dr[:, :, None, None] * w_im[:, None], axis=0
    )
    wide = rows
    if halo:
        left = jnp.roll(rows[:, :, cols - halo :], 1, axis=0)
        right = jnp.roll(rows[:, :, :halo], -1, axis=0)
        wide = jnp.concatenate([left, rows, right], axis=2)
    return jnp.where(polar[None, :, None], smooth, wide)


def tiled_path(tracers, courant_x, courant_y, cutoffs):
    tracer_count, level_count, lat_rows, lon_cols = tracers.shape
    field_count = tracer_count * level_count
    lat_devices = lax.axis_size("lat")
    lon_devices = lax.axis_size("lon")
    lat_index = lax.axis_index("lat")
    lon_index = lax.axis_index("lon")
    circle = lon_cols * lon_devices
    total_rows = lat_rows * lat_devices
    row_global = lat_index * lat_rows + jnp.arange(lat_rows, dtype=jnp.int32)
    face_global = lat_index * lat_rows + jnp.arange(lat_rows + 1, dtype=jnp.int32)
    face_angle = (face_global.astype(jnp.float32) / total_rows - 0.5) * math.pi
    face_weight = jnp.where(
        (face_global == 0) | (face_global == total_rows), 0.0, jnp.cos(face_angle)
    )
    center_weight = jnp.cos(((row_global.astype(jnp.float32) + 0.5) / total_rows - 0.5) * math.pi)
    is_south = lat_index == 0
    is_north = lat_index == lat_devices - 1

    count = field_count * lat_rows // lon_devices
    flat = lon_index * count + jnp.arange(count, dtype=jnp.int32)
    held_global = lat_index * lat_rows + flat % lat_rows
    polar = (held_global < total_rows // 4) | (held_global >= total_rows - total_rows // 4)
    cut = jnp.take(cutoffs, held_global)
    per_class = KMAX // lon_devices
    k = lon_devices * jnp.arange(per_class, dtype=jnp.int32)[None, :] + jnp.arange(
        lon_devices, dtype=jnp.int32
    )[:, None]
    scale = jnp.where(k == 0, 1.0 / circle, 2.0 / circle).astype(jnp.float32)
    weights = jnp.where(k[:, None, :] < cut[None, :, None], scale[:, None, :], 0.0)
    basis = split_basis(class_basis(lon_devices, lon_cols, circle))
    roots = root_table(lon_devices)

    west_cx = shift(courant_x[:, :, lon_cols - 1 :], "lon", 1, True)
    north_cy = shift(courant_y[:, :1], "lat", -1, False)
    east_courant = jnp.concatenate([west_cx, courant_x], axis=2)
    north_courant = jnp.concatenate(
        [courant_y, jnp.where(is_north, 0.0, north_cy)], axis=1
    )

    def lat_halos(state):
        south_in = shift(state[:, :, lat_rows - HALO :], "lat", 1, False)
        north_in = shift(state[:, :, :HALO], "lat", -1, False)
        edge = jnp.where(is_south, state[:, :, :HALO], state[:, :, lat_rows - HALO :])
        far = shift(edge, "lon", lon_devices // 2, True)
        far_rev = jnp.concatenate([far[:, :, 2:3], far[:, :, 1:2], far[:, :, 0:1]], axis=2)
        south_rows = jnp.where(is_south, far_rev, south_in)
        north_rows = jnp.where(is_north, far_rev, north_in)
        return jnp.concatenate([south_rows, state, north_rows], axis=2)

    state = tracers
    west_in = shift(state[..., lon_cols - HALO :], "lon", 1, True)
    east_in = shift(state[..., :HALO], "lon", -1, True)
    wrapped = jnp.concatenate([west_in, state, east_in], axis=3)
    for substep in range(SUBSTEPS):
        extended = lat_halos(state)
        zonal = ppm_flux(wrapped, east_courant, 3, lon_cols)
        meridional = ppm_flux(extended, north_courant, 2, lat_rows) * face_weight[:, None]
        change = (
            zonal[..., 1:]
            - zonal[..., :-1]
            + (meridional[:, :, 1:] - meridional[:, :, :-1]) / center_weight[:, None]
        )
        state = state - change
        rows = state.reshape(lon_devices, count, lon_cols)
        rows = lax.all_to_all(rows, "lon", 0, 0)
        wide = filter_rows(rows, basis, roots, weights, polar)
        if substep == SUBSTEPS - 1:
            wide = wide[:, :, HALO : HALO + lon_cols]
        wide = lax.all_to_all(wide, "lon", 0, 0)
        wrapped = wide.reshape(tracer_count, level_count, lat_rows, wide.shape[2])
        state = wrapped if substep == SUBSTEPS - 1 else wrapped[..., HALO : HALO + lon_cols]
    return state


def transposed_path(tracers, courant_x, courant_y, cutoffs):
    tracer_count, level_count, lat_rows, lon_cols = tracers.shape
    lat_devices = lax.axis_size("lat")
    lon_devices = lax.axis_size("lon")
    lat_index = lax.axis_index("lat")
    circle = lon_cols * lon_devices
    total_rows = lat_rows * lat_devices
    row_global = lat_index * lat_rows + jnp.arange(lat_rows, dtype=jnp.int32)
    face_global = lat_index * lat_rows + jnp.arange(lat_rows + 1, dtype=jnp.int32)
    face_angle = (face_global.astype(jnp.float32) / total_rows - 0.5) * math.pi
    face_weight = jnp.where(
        (face_global == 0) | (face_global == total_rows), 0.0, jnp.cos(face_angle)
    )
    center_weight = jnp.cos(((row_global.astype(jnp.float32) + 0.5) / total_rows - 0.5) * math.pi)
    is_south = lat_index == 0
    is_north = lat_index == lat_devices - 1

    count = tracer_count * lat_rows
    lon_index = lax.axis_index("lon")

    def payload_for(level):
        return jnp.concatenate(
            [
                lax.dynamic_index_in_dim(tracers, level, 1, keepdims=False).reshape(count, lon_cols),
                lax.dynamic_index_in_dim(courant_x, level, 0, keepdims=False),
                lax.dynamic_index_in_dim(courant_y, level, 0, keepdims=False),
            ],
            axis=0,
        )

    pieces = [payload_for(lon_index)]
    for by in range(1, lon_devices):
        pieces.append(shift(payload_for((lon_index + by) % lon_devices), "lon", by, True))
    payload = jnp.stack(pieces)
    state = payload[:, :count].reshape(lon_devices, tracer_count, lat_rows, lon_cols)
    cx = payload[:, None, count : count + lat_rows]
    cy = payload[:, None, count + lat_rows :]
    east_courant = jnp.concatenate([jnp.roll(cx[..., lon_cols - 1 :], -1, axis=0), cx], axis=3)

    held_global = lat_index * lat_rows + jnp.arange(count, dtype=jnp.int32) % lat_rows
    polar = (held_global < total_rows // 4) | (held_global >= total_rows - total_rows // 4)
    cut = jnp.take(cutoffs, held_global)
    per_class = KMAX // lon_devices
    k = lon_devices * jnp.arange(per_class, dtype=jnp.int32)[None, :] + jnp.arange(
        lon_devices, dtype=jnp.int32
    )[:, None]
    scale = jnp.where(k == 0, 1.0 / circle, 2.0 / circle).astype(jnp.float32)
    weights = jnp.where(k[:, None, :] < cut[None, :, None], scale[:, None, :], 0.0)
    basis = split_basis(product_basis(lon_devices, lon_cols, circle))
    roots = root_table(
        lon_devices, (lax.axis_index("lon") - jnp.arange(lon_devices, dtype=jnp.int32)) % lon_devices
    )

    for substep in range(SUBSTEPS):
        south_in = shift(state[:, :, lat_rows - HALO :], "lat", 1, False)
        if substep == 0:
            going = jnp.concatenate(
                [state[:, :, :HALO].reshape(lon_devices, tracer_count * HALO, lon_cols), cy[:, 0, :1]],
                axis=1,
            )
            coming = shift(going, "lat", -1, False)
            north_in = coming[:, : tracer_count * HALO].reshape(
                lon_devices, tracer_count, HALO, lon_cols
            )
            north_cy = jnp.where(is_north, 0.0, coming[:, None, tracer_count * HALO :])
            north_courant = jnp.concatenate([cy, north_cy], axis=2)
        else:
            north_in = shift(state[:, :, :HALO], "lat", -1, False)
        edge = jnp.where(is_south, state[:, :, :HALO], state[:, :, lat_rows - HALO :])
        far = jnp.roll(edge, lon_devices // 2, axis=0)
        far_rev = jnp.concatenate([far[:, :, 2:3], far[:, :, 1:2], far[:, :, 0:1]], axis=2)
        south_rows = jnp.where(is_south, far_rev, south_in)
        north_rows = jnp.where(is_north, far_rev, north_in)
        extended = jnp.concatenate([south_rows, state, north_rows], axis=2)
        wrapped = jnp.concatenate(
            [
                jnp.roll(state[..., lon_cols - HALO :], -1, axis=0),
                state,
                jnp.roll(state[..., :HALO], 1, axis=0),
            ],
            axis=3,
        )
        zonal = ppm_flux(wrapped, east_courant, 3, lon_cols)
        meridional = ppm_flux(extended, north_courant, 2, lat_rows) * face_weight[:, None]
        change = (
            zonal[..., 1:]
            - zonal[..., :-1]
            + (meridional[:, :, 1:] - meridional[:, :, :-1]) / center_weight[:, None]
        )
        state = state - change
        rows = state.reshape(lon_devices, count, lon_cols)
        rows = filter_rows(rows, basis, roots, weights, polar, 0)
        state = rows.reshape(lon_devices, tracer_count, lat_rows, lon_cols)

    back = [state[0]] + [
        shift(state[(lon_devices - by) % lon_devices], "lon", by, True) for by in range(1, lon_devices)
    ]
    levels = []
    for level in range(level_count):
        pick = back[0]
        for by in range(1, lon_devices):
            pick = jnp.where((lon_index - by) % lon_devices == level, back[by], pick)
        levels.append(pick)
    return jnp.stack(levels, axis=1)


def on_device(tracers, courant_x, courant_y, cutoffs):
    field_count = tracers.shape[0] * tracers.shape[1]
    if tracers.shape[1] == lax.axis_size("lon") and tracers.shape[2] >= HALO:
        return transposed_path(tracers, courant_x, courant_y, cutoffs)
    return tiled_path(tracers, courant_x, courant_y, cutoffs)


def solution(mesh):
    in_specs = (P(None, None, "lat", "lon"), P(None, "lat", "lon"), P(None, "lat", "lon"), P())
    out_specs = P(None, None, "lat", "lon")
    return jax.shard_map(
        on_device, mesh=mesh, in_specs=in_specs, out_specs=out_specs, check_vma=False
    )
```

```python
import math

import jax
import jax.numpy as jnp
from jax import lax
from jax.sharding import PartitionSpec as P

KMAX = 720
SUBSTEPS = 2
HALO = 3
MATMUL_PRECISION = lax.Precision.HIGH


def shift(x, axis, by, wrap):
    size = lax.axis_size(axis)
    pairs = [(i, (i + by) % size) for i in range(size) if wrap or 0 <= i + by < size]
    return lax.ppermute(x, axis, pairs)


def product_basis(tiles, cols, circle):
    split = max(b for b in range(1, cols + 1) if cols % b == 0 and b * b <= cols)
    per_class = KMAX // tiles
    k = tiles * jnp.arange(per_class, dtype=jnp.int32)[None, :] + jnp.arange(
        tiles, dtype=jnp.int32
    )[:, None]
    a = jnp.arange(cols // split, dtype=jnp.int32)
    b = jnp.arange(split, dtype=jnp.int32)
    step = 2.0 * math.pi / circle
    coarse = ((split * a[None, :, None] * k[:, None, :]) % circle).astype(jnp.float32) * step
    fine = ((b[None, :, None] * k[:, None, :]) % circle).astype(jnp.float32) * step
    ca, sa = jnp.cos(coarse)[:, :, None], jnp.sin(coarse)[:, :, None]
    cb, sb = jnp.cos(fine)[:, None], jnp.sin(fine)[:, None]
    cos_qk = (ca * cb - sa * sb).reshape(tiles, cols, per_class)
    sin_qk = (sa * cb + ca * sb).reshape(tiles, cols, per_class)
    return jnp.concatenate([cos_qk, sin_qk], axis=2)


def window(values, first_cell, last_cell, dim_at):
    return lax.slice_in_dim(values, first_cell, last_cell, axis=dim_at)


def ppm_flux(padded, courant, dim_at, cell_count):
    edge_values = 7.0 / 12.0 * (
        window(padded, 1, cell_count + 4, dim_at) + window(padded, 2, cell_count + 5, dim_at)
    ) - 1.0 / 12.0 * (
        window(padded, 0, cell_count + 3, dim_at) + window(padded, 3, cell_count + 6, dim_at)
    )
    left_edge = window(edge_values, 0, cell_count + 1, dim_at)
    mid_edge = window(edge_values, 1, cell_count + 2, dim_at)
    right_edge = window(edge_values, 2, cell_count + 3, dim_at)
    left_cell = window(padded, 2, cell_count + 3, dim_at)
    right_cell = window(padded, 3, cell_count + 4, dim_at)
    magnitude = jnp.abs(courant)
    six_left = 6.0 * left_cell - 3.0 * (left_edge + mid_edge)
    six_right = 6.0 * right_cell - 3.0 * (mid_edge + right_edge)
    from_left = mid_edge - 0.5 * magnitude * (
        mid_edge - left_edge - (1.0 - magnitude * (2.0 / 3.0)) * six_left
    )
    from_right = mid_edge + 0.5 * magnitude * (
        right_edge - mid_edge + (1.0 - magnitude * (2.0 / 3.0)) * six_right
    )
    return courant * jnp.where(courant >= 0.0, from_left, from_right)


def root_table(count, tile_of=None):
    d = jnp.arange(count, dtype=jnp.int32)
    tile = d if tile_of is None else tile_of
    angle = (d[:, None] * tile[None, :] % count).astype(jnp.float32) * (2.0 * math.pi / count)
    cos_dr, sin_dr = jnp.cos(angle), jnp.sin(angle)
    cos_dr = jnp.where(jnp.abs(cos_dr) < 1e-6, 0.0, cos_dr)
    sin_dr = jnp.where(jnp.abs(sin_dr) < 1e-6, 0.0, sin_dr)
    return cos_dr, sin_dr


def class_basis(tiles, cols, circle, halo=HALO):
    per_class = KMAX // tiles
    r = jnp.arange(tiles, dtype=jnp.int32)
    m = jnp.arange(per_class, dtype=jnp.int32)
    q = jnp.arange(-halo, cols + halo, dtype=jnp.int32) % circle
    k = tiles * m[None, :] + r[:, None]
    phase = (q[None, :, None] * k[:, None, :]) % circle
    angle = phase.astype(jnp.float32) * (2.0 * math.pi / circle)
    return jnp.concatenate([jnp.cos(angle), jnp.sin(angle)], axis=2)


def filter_rows(rows, basis, roots, weights, polar, halo=HALO):
    tiles, count, cols = rows.shape
    cos_dr, sin_dr = roots
    z_re = jnp.sum(cos_dr[:, :, None, None] * rows[None], axis=1)
    z_im = -jnp.sum(sin_dr[:, :, None, None] * rows[None], axis=1)
    z = jnp.concatenate([z_re, z_im], axis=1)
    z = jnp.pad(z, ((0, 0), (0, 0), (halo, halo)))
    prod = lax.dot_general(z, basis, (((2,), (1,)), ((0,), (0,))), precision=MATMUL_PRECISION)
    per_class = basis.shape[2] // 2
    zc, zs = prod[:, :count, :per_class], prod[:, :count, per_class:]
    wc, ws = prod[:, count:, :per_class], prod[:, count:, per_class:]
    real = (zc + ws) * weights
    imag = (zs - wc) * weights
    spec = jnp.concatenate(
        [jnp.concatenate([real, imag], axis=2), jnp.concatenate([-imag, real], axis=2)], axis=1
    )
    back = lax.dot_general(spec, basis, (((2,), (2,)), ((0,), (0,))), precision=MATMUL_PRECISION)
    w_re, w_im = back[:, :count], back[:, count:]
    smooth = jnp.sum(
        cos_dr[:, :, None, None] * w_re[:, None] - sin_dr[:, :, None, None] * w_im[:, None], axis=0
    )
    wide = rows
    if halo:
        left = jnp.roll(rows[:, :, cols - halo :], 1, axis=0)
        right = jnp.roll(rows[:, :, :halo], -1, axis=0)
        wide = jnp.concatenate([left, rows, right], axis=2)
    return jnp.where(polar[None, :, None], smooth, wide)


def tiled_path(tracers, courant_x, courant_y, cutoffs):
    tracer_count, level_count, lat_rows, lon_cols = tracers.shape
    field_count = tracer_count * level_count
    lat_devices = lax.axis_size("lat")
    lon_devices = lax.axis_size("lon")
    lat_index = lax.axis_index("lat")
    lon_index = lax.axis_index("lon")
    circle = lon_cols * lon_devices
    total_rows = lat_rows * lat_devices
    row_global = lat_index * lat_rows + jnp.arange(lat_rows, dtype=jnp.int32)
    face_global = lat_index * lat_rows + jnp.arange(lat_rows + 1, dtype=jnp.int32)
    face_angle = (face_global.astype(jnp.float32) / total_rows - 0.5) * math.pi
    face_weight = jnp.where(
        (face_global == 0) | (face_global == total_rows), 0.0, jnp.cos(face_angle)
    )
    center_weight = jnp.cos(((row_global.astype(jnp.float32) + 0.5) / total_rows - 0.5) * math.pi)
    is_south = lat_index == 0
    is_north = lat_index == lat_devices - 1

    count = field_count * lat_rows // lon_devices
    flat = lon_index * count + jnp.arange(count, dtype=jnp.int32)
    held_global = lat_index * lat_rows + flat % lat_rows
    polar = (held_global < total_rows // 4) | (held_global >= total_rows - total_rows // 4)
    cut = jnp.take(cutoffs, held_global)
    per_class = KMAX // lon_devices
    k = lon_devices * jnp.arange(per_class, dtype=jnp.int32)[None, :] + jnp.arange(
        lon_devices, dtype=jnp.int32
    )[:, None]
    scale = jnp.where(k == 0, 1.0 / circle, 2.0 / circle).astype(jnp.float32)
    weights = jnp.where(k[:, None, :] < cut[None, :, None], scale[:, None, :], 0.0)
    basis = class_basis(lon_devices, lon_cols, circle)
    roots = root_table(lon_devices)

    west_cx = shift(courant_x[:, :, lon_cols - 1 :], "lon", 1, True)
    north_cy = shift(courant_y[:, :1], "lat", -1, False)
    east_courant = jnp.concatenate([west_cx, courant_x], axis=2)
    north_courant = jnp.concatenate(
        [courant_y, jnp.where(is_north, 0.0, north_cy)], axis=1
    )

    def lat_halos(state):
        south_in = shift(state[:, :, lat_rows - HALO :], "lat", 1, False)
        north_in = shift(state[:, :, :HALO], "lat", -1, False)
        edge = jnp.where(is_south, state[:, :, :HALO], state[:, :, lat_rows - HALO :])
        far = shift(edge, "lon", lon_devices // 2, True)
        far_rev = jnp.concatenate([far[:, :, 2:3], far[:, :, 1:2], far[:, :, 0:1]], axis=2)
        south_rows = jnp.where(is_south, far_rev, south_in)
        north_rows = jnp.where(is_north, far_rev, north_in)
        return jnp.concatenate([south_rows, state, north_rows], axis=2)

    state = tracers
    west_in = shift(state[..., lon_cols - HALO :], "lon", 1, True)
    east_in = shift(state[..., :HALO], "lon", -1, True)
    wrapped = jnp.concatenate([west_in, state, east_in], axis=3)
    for substep in range(SUBSTEPS):
        extended = lat_halos(state)
        zonal = ppm_flux(wrapped, east_courant, 3, lon_cols)
        meridional = ppm_flux(extended, north_courant, 2, lat_rows) * face_weight[:, None]
        change = (
            zonal[..., 1:]
            - zonal[..., :-1]
            + (meridional[:, :, 1:] - meridional[:, :, :-1]) / center_weight[:, None]
        )
        state = state - change
        rows = state.reshape(lon_devices, count, lon_cols)
        rows = lax.all_to_all(rows, "lon", 0, 0)
        wide = filter_rows(rows, basis, roots, weights, polar)
        if substep == SUBSTEPS - 1:
            wide = wide[:, :, HALO : HALO + lon_cols]
        wide = lax.all_to_all(wide, "lon", 0, 0)
        wrapped = wide.reshape(tracer_count, level_count, lat_rows, wide.shape[2])
        state = wrapped if substep == SUBSTEPS - 1 else wrapped[..., HALO : HALO + lon_cols]
    return state


def transposed_path(tracers, courant_x, courant_y, cutoffs):
    tracer_count, level_count, lat_rows, lon_cols = tracers.shape
    lat_devices = lax.axis_size("lat")
    lon_devices = lax.axis_size("lon")
    lat_index = lax.axis_index("lat")
    circle = lon_cols * lon_devices
    total_rows = lat_rows * lat_devices
    is_south = lat_index == 0
    is_north = lat_index == lat_devices - 1

    count = tracer_count * lat_rows
    lon_index = lax.axis_index("lon")

    def payload_for(level):
        return jnp.concatenate(
            [
                lax.dynamic_index_in_dim(tracers, level, 1, keepdims=False).reshape(count, lon_cols),
                lax.dynamic_index_in_dim(courant_x, level, 0, keepdims=False),
                lax.dynamic_index_in_dim(courant_y, level, 0, keepdims=False),
            ],
            axis=0,
        )

    pieces = [payload_for(lon_index)]
    for by in range(1, lon_devices):
        pieces.append(shift(payload_for((lon_index + by) % lon_devices), "lon", by, True))
    payload = jnp.stack(pieces)
    state = payload[:, :count].reshape(lon_devices, tracer_count, lat_rows, lon_cols)
    cx = payload[:, None, count : count + lat_rows]
    cy = payload[:, None, count + lat_rows :]

    wide_rows = lat_rows + 2 * HALO
    deep = 2 * HALO
    per_class = KMAX // lon_devices
    k = lon_devices * jnp.arange(per_class, dtype=jnp.int32)[None, :] + jnp.arange(
        lon_devices, dtype=jnp.int32
    )[:, None]
    scale = jnp.where(k == 0, 1.0 / circle, 2.0 / circle).astype(jnp.float32)

    def row_tables(first_row, rows_out):
        held = lat_index * lat_rows + first_row + jnp.arange(tracer_count * rows_out) % rows_out
        polar = (held < total_rows // 4) | (held >= total_rows - total_rows // 4)
        cut = jnp.take(cutoffs, jnp.clip(held, 0, total_rows - 1))
        weights = jnp.where(k[:, None, :] < cut[None, :, None], scale[:, None, :], 0.0)
        return polar, weights

    tables = [row_tables(-HALO, wide_rows), row_tables(0, lat_rows)]
    basis = product_basis(lon_devices, lon_cols, circle)
    roots = root_table(
        lon_devices, (lax.axis_index("lon") - jnp.arange(lon_devices, dtype=jnp.int32)) % lon_devices
    )

    def flip(rows):
        return jnp.concatenate([rows[:, :, i : i + 1] for i in range(rows.shape[2] - 1, -1, -1)], axis=2)

    def poles(south, band, north, depth):
        edge = jnp.where(is_south, band[:, :, :depth], band[:, :, band.shape[2] - depth :])
        far = flip(jnp.roll(edge, lon_devices // 2, axis=0))
        return jnp.where(is_south, far, south), jnp.where(is_north, far, north)

    def advance(extended, first_row, rows_out, cx_rows, cy_faces, polar, weights):
        faces = lat_index * lat_rows + first_row + jnp.arange(rows_out + 1, dtype=jnp.int32)
        face_angle = (faces.astype(jnp.float32) / total_rows - 0.5) * math.pi
        face_weight = jnp.where((faces == 0) | (faces == total_rows), 0.0, jnp.cos(face_angle))
        cells = lat_index * lat_rows + first_row + jnp.arange(rows_out, dtype=jnp.int32)
        center_weight = jnp.cos(((cells.astype(jnp.float32) + 0.5) / total_rows - 0.5) * math.pi)
        state = extended[:, :, HALO : HALO + rows_out]
        wrapped = jnp.concatenate(
            [
                jnp.roll(state[..., lon_cols - HALO :], -1, axis=0),
                state,
                jnp.roll(state[..., :HALO], 1, axis=0),
            ],
            axis=3,
        )
        east_courant = jnp.concatenate(
            [jnp.roll(cx_rows[..., lon_cols - 1 :], -1, axis=0), cx_rows], axis=3
        )
        zonal = ppm_flux(wrapped, east_courant, 3, lon_cols)
        meridional = ppm_flux(extended, cy_faces, 2, rows_out) * face_weight[:, None]
        change = (
            zonal[..., 1:]
            - zonal[..., :-1]
            + (meridional[:, :, 1:] - meridional[:, :, :-1]) / center_weight[:, None]
        )
        state = state - change
        rows = state.reshape(lon_devices, tracer_count * rows_out, lon_cols)
        rows = filter_rows(rows, basis, roots, weights, polar, 0)
        return rows.reshape(lon_devices, tracer_count, rows_out, lon_cols)

    up = jnp.concatenate(
        [
            state[:, :, lat_rows - deep :].reshape(lon_devices, tracer_count * deep, lon_cols),
            cx[:, 0, lat_rows - HALO :],
            cy[:, 0, lat_rows - HALO :],
        ],
        axis=1,
    )
    down = jnp.concatenate(
        [
            state[:, :, :deep].reshape(lon_devices, tracer_count * deep, lon_cols),
            cx[:, 0, :HALO],
            cy[:, 0, : HALO + 1],
        ],
        axis=1,
    )
    from_south = shift(up, "lat", 1, False)
    from_north = shift(down, "lat", -1, False)
    rows6 = tracer_count * deep
    south = from_south[:, :rows6].reshape(lon_devices, tracer_count, deep, lon_cols)
    north = from_north[:, :rows6].reshape(lon_devices, tracer_count, deep, lon_cols)
    south, north = poles(south, state, north, deep)
    extended = jnp.concatenate([south, state, north], axis=2)
    cx_wide = jnp.concatenate(
        [from_south[:, rows6 : rows6 + HALO], cx[:, 0], from_north[:, rows6 : rows6 + HALO]], axis=1
    )[:, None]
    cy_wide = jnp.concatenate(
        [from_south[:, rows6 + HALO :], cy[:, 0], from_north[:, rows6 + HALO :]], axis=1
    )[:, None]

    wide = advance(extended, -HALO, wide_rows, cx_wide, cy_wide, *tables[0])
    south, north = poles(
        wide[:, :, :HALO], wide[:, :, HALO : HALO + lat_rows], wide[:, :, HALO + lat_rows :], HALO
    )
    extended = jnp.concatenate([south, wide[:, :, HALO : HALO + lat_rows], north], axis=2)
    state = advance(
        extended, 0, lat_rows, cx, cy_wide[:, :, HALO : HALO + lat_rows + 1], *tables[1]
    )
    for substep in range(2, SUBSTEPS):
        south_in = shift(state[:, :, lat_rows - HALO :], "lat", 1, False)
        north_in = shift(state[:, :, :HALO], "lat", -1, False)
        south, north = poles(south_in, state, north_in, HALO)
        extended = jnp.concatenate([south, state, north], axis=2)
        state = advance(
            extended, 0, lat_rows, cx, cy_wide[:, :, HALO : HALO + lat_rows + 1], *tables[1]
        )

    back = [state[0]] + [
        shift(state[(lon_devices - by) % lon_devices], "lon", by, True) for by in range(1, lon_devices)
    ]
    levels = []
    for level in range(level_count):
        pick = back[0]
        for by in range(1, lon_devices):
            pick = jnp.where((lon_index - by) % lon_devices == level, back[by], pick)
        levels.append(pick)
    return jnp.stack(levels, axis=1)


def on_device(tracers, courant_x, courant_y, cutoffs):
    field_count = tracers.shape[0] * tracers.shape[1]
    if tracers.shape[1] == lax.axis_size("lon") and tracers.shape[2] >= 2 * HALO and SUBSTEPS >= 2:
        return transposed_path(tracers, courant_x, courant_y, cutoffs)
    return tiled_path(tracers, courant_x, courant_y, cutoffs)


def solution(mesh):
    in_specs = (P(None, None, "lat", "lon"), P(None, "lat", "lon"), P(None, "lat", "lon"), P())
    out_specs = P(None, None, "lat", "lon")
    return jax.shard_map(
        on_device, mesh=mesh, in_specs=in_specs, out_specs=out_specs, check_vma=False
    )
```

```python
import math

import jax
import jax.numpy as jnp
from jax import lax
from jax.sharding import PartitionSpec as P

KMAX = 720
SUBSTEPS = 2
HALO = 3
MATMUL_PRECISION = lax.Precision.HIGH


def shift(x, axis, by, wrap):
    size = lax.axis_size(axis)
    pairs = [(i, (i + by) % size) for i in range(size) if wrap or 0 <= i + by < size]
    return lax.ppermute(x, axis, pairs)


def product_basis(tiles, cols, circle):
    split = max(b for b in range(1, cols + 1) if cols % b == 0 and b * b <= cols)
    per_class = KMAX // tiles
    k = tiles * jnp.arange(per_class, dtype=jnp.int32)[None, :] + jnp.arange(
        tiles, dtype=jnp.int32
    )[:, None]
    a = jnp.arange(cols // split, dtype=jnp.int32)
    b = jnp.arange(split, dtype=jnp.int32)
    step = 2.0 * math.pi / circle
    coarse = ((split * a[None, None, :] * k[:, :, None]) % circle).astype(jnp.float32) * step
    fine = ((b[None, None, :] * k[:, :, None]) % circle).astype(jnp.float32) * step
    ca, sa = jnp.cos(coarse)[:, :, :, None], jnp.sin(coarse)[:, :, :, None]
    cb, sb = jnp.cos(fine)[:, :, None], jnp.sin(fine)[:, :, None]
    cos_qk = (ca * cb - sa * sb).reshape(tiles, per_class, cols)
    sin_qk = (sa * cb + ca * sb).reshape(tiles, per_class, cols)
    return jnp.concatenate([cos_qk, sin_qk], axis=1)


def window(values, first_cell, last_cell, dim_at):
    return lax.slice_in_dim(values, first_cell, last_cell, axis=dim_at)


def ppm_flux(padded, courant, dim_at, cell_count):
    edge_values = 7.0 / 12.0 * (
        window(padded, 1, cell_count + 4, dim_at) + window(padded, 2, cell_count + 5, dim_at)
    ) - 1.0 / 12.0 * (
        window(padded, 0, cell_count + 3, dim_at) + window(padded, 3, cell_count + 6, dim_at)
    )
    left_edge = window(edge_values, 0, cell_count + 1, dim_at)
    mid_edge = window(edge_values, 1, cell_count + 2, dim_at)
    right_edge = window(edge_values, 2, cell_count + 3, dim_at)
    left_cell = window(padded, 2, cell_count + 3, dim_at)
    right_cell = window(padded, 3, cell_count + 4, dim_at)
    magnitude = jnp.abs(courant)
    six_left = 6.0 * left_cell - 3.0 * (left_edge + mid_edge)
    six_right = 6.0 * right_cell - 3.0 * (mid_edge + right_edge)
    from_left = mid_edge - 0.5 * magnitude * (
        mid_edge - left_edge - (1.0 - magnitude * (2.0 / 3.0)) * six_left
    )
    from_right = mid_edge + 0.5 * magnitude * (
        right_edge - mid_edge + (1.0 - magnitude * (2.0 / 3.0)) * six_right
    )
    return courant * jnp.where(courant >= 0.0, from_left, from_right)


def root_table(count, tile_of=None):
    d = jnp.arange(count, dtype=jnp.int32)
    tile = d if tile_of is None else tile_of
    angle = (d[:, None] * tile[None, :] % count).astype(jnp.float32) * (2.0 * math.pi / count)
    cos_dr, sin_dr = jnp.cos(angle), jnp.sin(angle)
    cos_dr = jnp.where(jnp.abs(cos_dr) < 1e-6, 0.0, cos_dr)
    sin_dr = jnp.where(jnp.abs(sin_dr) < 1e-6, 0.0, sin_dr)
    return cos_dr, sin_dr


def class_basis(tiles, cols, circle, halo=HALO):
    per_class = KMAX // tiles
    r = jnp.arange(tiles, dtype=jnp.int32)
    m = jnp.arange(per_class, dtype=jnp.int32)
    q = jnp.arange(-halo, cols + halo, dtype=jnp.int32) % circle
    k = tiles * m[None, :] + r[:, None]
    phase = (q[None, :, None] * k[:, None, :]) % circle
    angle = phase.astype(jnp.float32) * (2.0 * math.pi / circle)
    return jnp.concatenate([jnp.cos(angle), jnp.sin(angle)], axis=2)


def filter_rows(rows, basis, roots, weights, polar, halo=HALO, m_major=False):
    tiles, count, cols = rows.shape
    cos_dr, sin_dr = roots
    z_re = jnp.sum(cos_dr[:, :, None, None] * rows[None], axis=1)
    z_im = -jnp.sum(sin_dr[:, :, None, None] * rows[None], axis=1)
    z = jnp.concatenate([z_re, z_im], axis=1)
    z = jnp.pad(z, ((0, 0), (0, 0), (halo, halo)))
    q_axis, m_axis = (2, 1) if m_major else (1, 2)
    prod = lax.dot_general(z, basis, (((2,), (q_axis,)), ((0,), (0,))), precision=MATMUL_PRECISION)
    per_class = basis.shape[m_axis] // 2
    zc, zs = prod[:, :count, :per_class], prod[:, :count, per_class:]
    wc, ws = prod[:, count:, :per_class], prod[:, count:, per_class:]
    real = (zc + ws) * weights
    imag = (zs - wc) * weights
    spec = jnp.concatenate(
        [jnp.concatenate([real, imag], axis=2), jnp.concatenate([-imag, real], axis=2)], axis=1
    )
    back = lax.dot_general(spec, basis, (((2,), (m_axis,)), ((0,), (0,))), precision=MATMUL_PRECISION)
    w_re, w_im = back[:, :count], back[:, count:]
    smooth = jnp.sum(
        cos_dr[:, :, None, None] * w_re[:, None] - sin_dr[:, :, None, None] * w_im[:, None], axis=0
    )
    wide = rows
    if halo:
        left = jnp.roll(rows[:, :, cols - halo :], 1, axis=0)
        right = jnp.roll(rows[:, :, :halo], -1, axis=0)
        wide = jnp.concatenate([left, rows, right], axis=2)
    return jnp.where(polar[None, :, None], smooth, wide)


def tiled_path(tracers, courant_x, courant_y, cutoffs):
    tracer_count, level_count, lat_rows, lon_cols = tracers.shape
    field_count = tracer_count * level_count
    lat_devices = lax.axis_size("lat")
    lon_devices = lax.axis_size("lon")
    lat_index = lax.axis_index("lat")
    lon_index = lax.axis_index("lon")
    circle = lon_cols * lon_devices
    total_rows = lat_rows * lat_devices
    row_global = lat_index * lat_rows + jnp.arange(lat_rows, dtype=jnp.int32)
    face_global = lat_index * lat_rows + jnp.arange(lat_rows + 1, dtype=jnp.int32)
    face_angle = (face_global.astype(jnp.float32) / total_rows - 0.5) * math.pi
    face_weight = jnp.where(
        (face_global == 0) | (face_global == total_rows), 0.0, jnp.cos(face_angle)
    )
    center_weight = jnp.cos(((row_global.astype(jnp.float32) + 0.5) / total_rows - 0.5) * math.pi)
    is_south = lat_index == 0
    is_north = lat_index == lat_devices - 1

    count = field_count * lat_rows // lon_devices
    flat = lon_index * count + jnp.arange(count, dtype=jnp.int32)
    held_global = lat_index * lat_rows + flat % lat_rows
    polar = (held_global < total_rows // 4) | (held_global >= total_rows - total_rows // 4)
    cut = jnp.take(cutoffs, held_global)
    per_class = KMAX // lon_devices
    k = lon_devices * jnp.arange(per_class, dtype=jnp.int32)[None, :] + jnp.arange(
        lon_devices, dtype=jnp.int32
    )[:, None]
    scale = jnp.where(k == 0, 1.0 / circle, 2.0 / circle).astype(jnp.float32)
    weights = jnp.where(k[:, None, :] < cut[None, :, None], scale[:, None, :], 0.0)
    basis = class_basis(lon_devices, lon_cols, circle)
    roots = root_table(lon_devices)

    west_cx = shift(courant_x[:, :, lon_cols - 1 :], "lon", 1, True)
    north_cy = shift(courant_y[:, :1], "lat", -1, False)
    east_courant = jnp.concatenate([west_cx, courant_x], axis=2)
    north_courant = jnp.concatenate(
        [courant_y, jnp.where(is_north, 0.0, north_cy)], axis=1
    )

    def lat_halos(state):
        south_in = shift(state[:, :, lat_rows - HALO :], "lat", 1, False)
        north_in = shift(state[:, :, :HALO], "lat", -1, False)
        edge = jnp.where(is_south, state[:, :, :HALO], state[:, :, lat_rows - HALO :])
        far = shift(edge, "lon", lon_devices // 2, True)
        far_rev = jnp.concatenate([far[:, :, 2:3], far[:, :, 1:2], far[:, :, 0:1]], axis=2)
        south_rows = jnp.where(is_south, far_rev, south_in)
        north_rows = jnp.where(is_north, far_rev, north_in)
        return jnp.concatenate([south_rows, state, north_rows], axis=2)

    state = tracers
    west_in = shift(state[..., lon_cols - HALO :], "lon", 1, True)
    east_in = shift(state[..., :HALO], "lon", -1, True)
    wrapped = jnp.concatenate([west_in, state, east_in], axis=3)
    for substep in range(SUBSTEPS):
        extended = lat_halos(state)
        zonal = ppm_flux(wrapped, east_courant, 3, lon_cols)
        meridional = ppm_flux(extended, north_courant, 2, lat_rows) * face_weight[:, None]
        change = (
            zonal[..., 1:]
            - zonal[..., :-1]
            + (meridional[:, :, 1:] - meridional[:, :, :-1]) / center_weight[:, None]
        )
        state = state - change
        rows = state.reshape(lon_devices, count, lon_cols)
        rows = lax.all_to_all(rows, "lon", 0, 0)
        wide = filter_rows(rows, basis, roots, weights, polar)
        if substep == SUBSTEPS - 1:
            wide = wide[:, :, HALO : HALO + lon_cols]
        wide = lax.all_to_all(wide, "lon", 0, 0)
        wrapped = wide.reshape(tracer_count, level_count, lat_rows, wide.shape[2])
        state = wrapped if substep == SUBSTEPS - 1 else wrapped[..., HALO : HALO + lon_cols]
    return state


def transposed_path(tracers, courant_x, courant_y, cutoffs):
    tracer_count, level_count, lat_rows, lon_cols = tracers.shape
    lat_devices = lax.axis_size("lat")
    lon_devices = lax.axis_size("lon")
    lat_index = lax.axis_index("lat")
    circle = lon_cols * lon_devices
    total_rows = lat_rows * lat_devices
    row_global = lat_index * lat_rows + jnp.arange(lat_rows, dtype=jnp.int32)
    face_global = lat_index * lat_rows + jnp.arange(lat_rows + 1, dtype=jnp.int32)
    face_angle = (face_global.astype(jnp.float32) / total_rows - 0.5) * math.pi
    face_weight = jnp.where(
        (face_global == 0) | (face_global == total_rows), 0.0, jnp.cos(face_angle)
    )
    center_weight = jnp.cos(((row_global.astype(jnp.float32) + 0.5) / total_rows - 0.5) * math.pi)
    is_south = lat_index == 0
    is_north = lat_index == lat_devices - 1

    count = tracer_count * lat_rows
    lon_index = lax.axis_index("lon")

    def payload_for(level):
        return jnp.concatenate(
            [
                lax.dynamic_index_in_dim(tracers, level, 1, keepdims=False).reshape(count, lon_cols),
                lax.dynamic_index_in_dim(courant_x, level, 0, keepdims=False),
                lax.dynamic_index_in_dim(courant_y, level, 0, keepdims=False),
            ],
            axis=0,
        )

    pieces = [payload_for(lon_index)]
    for by in range(1, lon_devices):
        pieces.append(shift(payload_for((lon_index + by) % lon_devices), "lon", by, True))
    payload = jnp.stack(pieces)
    state = payload[:, :count].reshape(lon_devices, tracer_count, lat_rows, lon_cols)
    cx = payload[:, None, count : count + lat_rows]
    cy = payload[:, None, count + lat_rows :]
    east_courant = jnp.concatenate([jnp.roll(cx[..., lon_cols - 1 :], -1, axis=0), cx], axis=3)

    held_global = lat_index * lat_rows + jnp.arange(count, dtype=jnp.int32) % lat_rows
    polar = (held_global < total_rows // 4) | (held_global >= total_rows - total_rows // 4)
    cut = jnp.take(cutoffs, held_global)
    per_class = KMAX // lon_devices
    k = lon_devices * jnp.arange(per_class, dtype=jnp.int32)[None, :] + jnp.arange(
        lon_devices, dtype=jnp.int32
    )[:, None]
    scale = jnp.where(k == 0, 1.0 / circle, 2.0 / circle).astype(jnp.float32)
    weights = jnp.where(k[:, None, :] < cut[None, :, None], scale[:, None, :], 0.0)
    basis = product_basis(lon_devices, lon_cols, circle)
    roots = root_table(
        lon_devices, (lax.axis_index("lon") - jnp.arange(lon_devices, dtype=jnp.int32)) % lon_devices
    )

    for substep in range(SUBSTEPS):
        south_in = shift(state[:, :, lat_rows - HALO :], "lat", 1, False)
        if substep == 0:
            going = jnp.concatenate(
                [state[:, :, :HALO].reshape(lon_devices, tracer_count * HALO, lon_cols), cy[:, 0, :1]],
                axis=1,
            )
            coming = shift(going, "lat", -1, False)
            north_in = coming[:, : tracer_count * HALO].reshape(
                lon_devices, tracer_count, HALO, lon_cols
            )
            north_cy = jnp.where(is_north, 0.0, coming[:, None, tracer_count * HALO :])
            north_courant = jnp.concatenate([cy, north_cy], axis=2)
        else:
            north_in = shift(state[:, :, :HALO], "lat", -1, False)
        edge = jnp.where(is_south, state[:, :, :HALO], state[:, :, lat_rows - HALO :])
        far = jnp.roll(edge, lon_devices // 2, axis=0)
        far_rev = jnp.concatenate([far[:, :, 2:3], far[:, :, 1:2], far[:, :, 0:1]], axis=2)
        south_rows = jnp.where(is_south, far_rev, south_in)
        north_rows = jnp.where(is_north, far_rev, north_in)
        extended = jnp.concatenate([south_rows, state, north_rows], axis=2)
        wrapped = jnp.concatenate(
            [
                jnp.roll(state[..., lon_cols - HALO :], -1, axis=0),
                state,
                jnp.roll(state[..., :HALO], 1, axis=0),
            ],
            axis=3,
        )
        zonal = ppm_flux(wrapped, east_courant, 3, lon_cols)
        meridional = ppm_flux(extended, north_courant, 2, lat_rows) * face_weight[:, None]
        change = (
            zonal[..., 1:]
            - zonal[..., :-1]
            + (meridional[:, :, 1:] - meridional[:, :, :-1]) / center_weight[:, None]
        )
        state = state - change
        rows = state.reshape(lon_devices, count, lon_cols)
        rows = filter_rows(rows, basis, roots, weights, polar, 0, True)
        state = rows.reshape(lon_devices, tracer_count, lat_rows, lon_cols)

    back = [state[0]] + [
        shift(state[(lon_devices - by) % lon_devices], "lon", by, True) for by in range(1, lon_devices)
    ]
    levels = []
    for level in range(level_count):
        pick = back[0]
        for by in range(1, lon_devices):
            pick = jnp.where((lon_index - by) % lon_devices == level, back[by], pick)
        levels.append(pick)
    return jnp.stack(levels, axis=1)


def on_device(tracers, courant_x, courant_y, cutoffs):
    field_count = tracers.shape[0] * tracers.shape[1]
    if tracers.shape[1] == lax.axis_size("lon") and tracers.shape[2] >= HALO:
        return transposed_path(tracers, courant_x, courant_y, cutoffs)
    return tiled_path(tracers, courant_x, courant_y, cutoffs)


def solution(mesh):
    in_specs = (P(None, None, "lat", "lon"), P(None, "lat", "lon"), P(None, "lat", "lon"), P())
    out_specs = P(None, None, "lat", "lon")
    return jax.shard_map(
        on_device, mesh=mesh, in_specs=in_specs, out_specs=out_specs, check_vma=False
    )
```

```python
import math

import jax
import jax.numpy as jnp
from jax import lax
from jax.sharding import PartitionSpec as P


KMAX = 720
SUBSTEPS = 2
HALO = 3
MATMUL_PRECISION = lax.Precision.HIGH


def shift(x, axis, by, wrap):
    size = lax.axis_size(axis)
    pairs = [(i, (i + by) % size) for i in range(size) if wrap or 0 <= i + by < size]
    return lax.ppermute(x, axis, pairs)


def product_basis(tiles, cols, circle):
    split = max(b for b in range(1, cols + 1) if cols % b == 0 and b * b <= cols)
    per_class = KMAX // tiles
    k = tiles * jnp.arange(per_class, dtype=jnp.int32)[None, :] + jnp.arange(
        tiles, dtype=jnp.int32
    )[:, None]
    a = jnp.arange(cols // split, dtype=jnp.int32)
    b = jnp.arange(split, dtype=jnp.int32)
    step = 2.0 * math.pi / circle
    coarse = ((split * a[None, None, :] * k[:, :, None]) % circle).astype(jnp.float32) * step
    fine = ((b[None, None, :] * k[:, :, None]) % circle).astype(jnp.float32) * step
    ca, sa = jnp.cos(coarse)[:, :, :, None], jnp.sin(coarse)[:, :, :, None]
    cb, sb = jnp.cos(fine)[:, :, None], jnp.sin(fine)[:, :, None]
    cos_qk = (ca * cb - sa * sb).reshape(tiles, per_class, cols)
    sin_qk = (sa * cb + ca * sb).reshape(tiles, per_class, cols)
    return jnp.concatenate([cos_qk, sin_qk], axis=1)


def window(values, first_cell, last_cell, dim_at):
    return lax.slice_in_dim(values, first_cell, last_cell, axis=dim_at)


def ppm_flux(padded, courant, dim_at, cell_count):
    edge_values = 7.0 / 12.0 * (
        window(padded, 1, cell_count + 4, dim_at) + window(padded, 2, cell_count + 5, dim_at)
    ) - 1.0 / 12.0 * (
        window(padded, 0, cell_count + 3, dim_at) + window(padded, 3, cell_count + 6, dim_at)
    )
    left_edge = window(edge_values, 0, cell_count + 1, dim_at)
    mid_edge = window(edge_values, 1, cell_count + 2, dim_at)
    right_edge = window(edge_values, 2, cell_count + 3, dim_at)
    left_cell = window(padded, 2, cell_count + 3, dim_at)
    right_cell = window(padded, 3, cell_count + 4, dim_at)
    magnitude = jnp.abs(courant)
    six_left = 6.0 * left_cell - 3.0 * (left_edge + mid_edge)
    six_right = 6.0 * right_cell - 3.0 * (mid_edge + right_edge)
    from_left = mid_edge - 0.5 * magnitude * (
        mid_edge - left_edge - (1.0 - magnitude * (2.0 / 3.0)) * six_left
    )
    from_right = mid_edge + 0.5 * magnitude * (
        right_edge - mid_edge + (1.0 - magnitude * (2.0 / 3.0)) * six_right
    )
    return courant * jnp.where(courant >= 0.0, from_left, from_right)


def root_table(count, tile_of=None):
    d = jnp.arange(count, dtype=jnp.int32)
    tile = d if tile_of is None else tile_of
    angle = (d[:, None] * tile[None, :] % count).astype(jnp.float32) * (2.0 * math.pi / count)
    cos_dr, sin_dr = jnp.cos(angle), jnp.sin(angle)
    cos_dr = jnp.where(jnp.abs(cos_dr) < 1e-6, 0.0, cos_dr)
    sin_dr = jnp.where(jnp.abs(sin_dr) < 1e-6, 0.0, sin_dr)
    return cos_dr, sin_dr


def class_basis(tiles, cols, circle, halo=HALO):
    per_class = KMAX // tiles
    r = jnp.arange(tiles, dtype=jnp.int32)
    m = jnp.arange(per_class, dtype=jnp.int32)
    q = jnp.arange(-halo, cols + halo, dtype=jnp.int32) % circle
    k = tiles * m[None, :] + r[:, None]
    phase = (q[None, :, None] * k[:, None, :]) % circle
    angle = phase.astype(jnp.float32) * (2.0 * math.pi / circle)
    return jnp.concatenate([jnp.cos(angle), jnp.sin(angle)], axis=2)


def filter_rows(rows, basis, roots, weights, polar, halo=HALO, m_major=False):
    _, count, cols = rows.shape
    cos_dr, sin_dr = roots
    z_re = jnp.sum(cos_dr[:, :, None, None] * rows[None], axis=1)
    z_im = -jnp.sum(sin_dr[:, :, None, None] * rows[None], axis=1)
    z = jnp.concatenate([z_re, z_im], axis=1)
    z = jnp.pad(z, ((0, 0), (0, 0), (halo, halo)))
    q_axis, m_axis = (2, 1) if m_major else (1, 2)
    prod = lax.dot_general(z, basis, (((2,), (q_axis,)), ((0,), (0,))), precision=MATMUL_PRECISION)
    per_class = basis.shape[m_axis] // 2
    zc, zs = prod[:, :count, :per_class], prod[:, :count, per_class:]
    wc, ws = prod[:, count:, :per_class], prod[:, count:, per_class:]
    real = (zc + ws) * weights
    imag = (zs - wc) * weights
    spec = jnp.concatenate(
        [jnp.concatenate([real, imag], axis=2), jnp.concatenate([-imag, real], axis=2)], axis=1
    )
    back = lax.dot_general(spec, basis, (((2,), (m_axis,)), ((0,), (0,))), precision=MATMUL_PRECISION)
    w_re, w_im = back[:, :count], back[:, count:]
    smooth = jnp.sum(
        cos_dr[:, :, None, None] * w_re[:, None] - sin_dr[:, :, None, None] * w_im[:, None], axis=0
    )
    wide = rows
    if halo:
        left = jnp.roll(rows[:, :, cols - halo :], 1, axis=0)
        right = jnp.roll(rows[:, :, :halo], -1, axis=0)
        wide = jnp.concatenate([left, rows, right], axis=2)
    return jnp.where(polar[None, :, None], smooth, wide)


def tiled_path(tracers, courant_x, courant_y, cutoffs):
    tracer_count, level_count, lat_rows, lon_cols = tracers.shape
    field_count = tracer_count * level_count
    lat_devices = lax.axis_size("lat")
    lon_devices = lax.axis_size("lon")
    lat_index = lax.axis_index("lat")
    lon_index = lax.axis_index("lon")
    circle = lon_cols * lon_devices
    total_rows = lat_rows * lat_devices
    row_global = lat_index * lat_rows + jnp.arange(lat_rows, dtype=jnp.int32)
    face_global = lat_index * lat_rows + jnp.arange(lat_rows + 1, dtype=jnp.int32)
    face_angle = (face_global.astype(jnp.float32) / total_rows - 0.5) * math.pi
    face_weight = jnp.where(
        (face_global == 0) | (face_global == total_rows), 0.0, jnp.cos(face_angle)
    )
    center_weight = jnp.cos(((row_global.astype(jnp.float32) + 0.5) / total_rows - 0.5) * math.pi)
    is_south = lat_index == 0
    is_north = lat_index == lat_devices - 1

    count = field_count * lat_rows // lon_devices
    flat = lon_index * count + jnp.arange(count, dtype=jnp.int32)
    held_global = lat_index * lat_rows + flat % lat_rows
    polar = (held_global < total_rows // 4) | (held_global >= total_rows - total_rows // 4)
    cut = jnp.take(cutoffs, held_global)
    per_class = KMAX // lon_devices
    k = lon_devices * jnp.arange(per_class, dtype=jnp.int32)[None, :] + jnp.arange(
        lon_devices, dtype=jnp.int32
    )[:, None]
    scale = jnp.where(k == 0, 1.0 / circle, 2.0 / circle).astype(jnp.float32)
    weights = jnp.where(k[:, None, :] < cut[None, :, None], scale[:, None, :], 0.0)
    basis = class_basis(lon_devices, lon_cols, circle)
    roots = root_table(lon_devices)

    west_cx = shift(courant_x[:, :, lon_cols - 1 :], "lon", 1, True)
    north_cy = shift(courant_y[:, :1], "lat", -1, False)
    east_courant = jnp.concatenate([west_cx, courant_x], axis=2)
    north_courant = jnp.concatenate(
        [courant_y, jnp.where(is_north, 0.0, north_cy)], axis=1
    )

    def lat_halos(state):
        south_in = shift(state[:, :, lat_rows - HALO :], "lat", 1, False)
        north_in = shift(state[:, :, :HALO], "lat", -1, False)
        edge = jnp.where(is_south, state[:, :, :HALO], state[:, :, lat_rows - HALO :])
        far = shift(edge, "lon", lon_devices // 2, True)
        far_rev = jnp.concatenate([far[:, :, 2:3], far[:, :, 1:2], far[:, :, 0:1]], axis=2)
        south_rows = jnp.where(is_south, far_rev, south_in)
        north_rows = jnp.where(is_north, far_rev, north_in)
        return jnp.concatenate([south_rows, state, north_rows], axis=2)

    state = tracers
    west_in = shift(state[..., lon_cols - HALO :], "lon", 1, True)
    east_in = shift(state[..., :HALO], "lon", -1, True)
    wrapped = jnp.concatenate([west_in, state, east_in], axis=3)
    for substep in range(SUBSTEPS):
        extended = lat_halos(state)
        zonal = ppm_flux(wrapped, east_courant, 3, lon_cols)
        meridional = ppm_flux(extended, north_courant, 2, lat_rows) * face_weight[:, None]
        change = (
            zonal[..., 1:]
            - zonal[..., :-1]
            + (meridional[:, :, 1:] - meridional[:, :, :-1]) / center_weight[:, None]
        )
        state = state - change
        rows = state.reshape(lon_devices, count, lon_cols)
        rows = lax.all_to_all(rows, "lon", 0, 0)
        wide = filter_rows(rows, basis, roots, weights, polar)
        if substep == SUBSTEPS - 1:
            wide = wide[:, :, HALO : HALO + lon_cols]
        wide = lax.all_to_all(wide, "lon", 0, 0)
        wrapped = wide.reshape(tracer_count, level_count, lat_rows, wide.shape[2])
        state = wrapped if substep == SUBSTEPS - 1 else wrapped[..., HALO : HALO + lon_cols]
    return state


def transposed_path(tracers, courant_x, courant_y, cutoffs):
    tracer_count, level_count, lat_rows, lon_cols = tracers.shape
    lat_devices = lax.axis_size("lat")
    lon_devices = lax.axis_size("lon")
    lat_index = lax.axis_index("lat")
    circle = lon_cols * lon_devices
    total_rows = lat_rows * lat_devices
    row_global = lat_index * lat_rows + jnp.arange(lat_rows, dtype=jnp.int32)
    face_global = lat_index * lat_rows + jnp.arange(lat_rows + 1, dtype=jnp.int32)
    face_angle = (face_global.astype(jnp.float32) / total_rows - 0.5) * math.pi
    face_weight = jnp.where(
        (face_global == 0) | (face_global == total_rows), 0.0, jnp.cos(face_angle)
    )
    center_weight = jnp.cos(((row_global.astype(jnp.float32) + 0.5) / total_rows - 0.5) * math.pi)
    is_south = lat_index == 0
    is_north = lat_index == lat_devices - 1

    count = tracer_count * lat_rows
    lon_index = lax.axis_index("lon")

    def payload_for(level):
        return jnp.concatenate(
            [
                lax.dynamic_index_in_dim(tracers, level, 1, keepdims=False).reshape(count, lon_cols),
                lax.dynamic_index_in_dim(courant_x, level, 0, keepdims=False),
                lax.dynamic_index_in_dim(courant_y, level, 0, keepdims=False),
            ],
            axis=0,
        )

    pieces = [payload_for(lon_index)]
    for by in range(1, lon_devices):
        pieces.append(shift(payload_for((lon_index + by) % lon_devices), "lon", by, True))
    payload = jnp.stack(pieces)
    state = payload[:, :count].reshape(lon_devices, tracer_count, lat_rows, lon_cols)
    cx = payload[:, None, count : count + lat_rows]
    cy = payload[:, None, count + lat_rows :]
    east_courant = jnp.concatenate([jnp.roll(cx[..., lon_cols - 1 :], -1, axis=0), cx], axis=3)

    held_global = lat_index * lat_rows + jnp.arange(count, dtype=jnp.int32) % lat_rows
    polar = (held_global < total_rows // 4) | (held_global >= total_rows - total_rows // 4)
    cut = jnp.take(cutoffs, held_global)
    per_class = KMAX // lon_devices
    k = lon_devices * jnp.arange(per_class, dtype=jnp.int32)[None, :] + jnp.arange(
        lon_devices, dtype=jnp.int32
    )[:, None]
    scale = jnp.where(k == 0, 1.0 / circle, 2.0 / circle).astype(jnp.float32)
    weights = jnp.where(k[:, None, :] < cut[None, :, None], scale[:, None, :], 0.0)
    basis = product_basis(lon_devices, lon_cols, circle)
    roots = root_table(
        lon_devices, (lax.axis_index("lon") - jnp.arange(lon_devices, dtype=jnp.int32)) % lon_devices
    )

    for substep in range(SUBSTEPS):
        south_in = shift(state[:, :, lat_rows - HALO :], "lat", 1, False)
        if substep == 0:
            going = jnp.concatenate(
                [state[:, :, :HALO].reshape(lon_devices, tracer_count * HALO, lon_cols), cy[:, 0, :1]],
                axis=1,
            )
            coming = shift(going, "lat", -1, False)
            north_in = coming[:, : tracer_count * HALO].reshape(
                lon_devices, tracer_count, HALO, lon_cols
            )
            north_cy = jnp.where(is_north, 0.0, coming[:, None, tracer_count * HALO :])
            north_courant = jnp.concatenate([cy, north_cy], axis=2)
        else:
            north_in = shift(state[:, :, :HALO], "lat", -1, False)
        edge = jnp.where(is_south, state[:, :, :HALO], state[:, :, lat_rows - HALO :])
        far = jnp.roll(edge, lon_devices // 2, axis=0)
        far_rev = jnp.concatenate([far[:, :, 2:3], far[:, :, 1:2], far[:, :, 0:1]], axis=2)
        south_rows = jnp.where(is_south, far_rev, south_in)
        north_rows = jnp.where(is_north, far_rev, north_in)
        extended = jnp.concatenate([south_rows, state, north_rows], axis=2)
        wrapped = jnp.concatenate(
            [
                jnp.roll(state[..., lon_cols - HALO :], -1, axis=0),
                state,
                jnp.roll(state[..., :HALO], 1, axis=0),
            ],
            axis=3,
        )
        zonal = ppm_flux(wrapped, east_courant, 3, lon_cols)
        zonal_change = lax.optimization_barrier(zonal[..., 1:] - zonal[..., :-1])
        meridional = ppm_flux(extended, north_courant, 2, lat_rows) * face_weight[:, None]
        change = zonal_change + (meridional[:, :, 1:] - meridional[:, :, :-1]) / center_weight[:, None]
        state = state - change
        rows = state.reshape(lon_devices, count, lon_cols)
        rows = filter_rows(rows, basis, roots, weights, polar, 0, True)
        state = rows.reshape(lon_devices, tracer_count, lat_rows, lon_cols)

    back = [state[0]] + [
        shift(state[(lon_devices - by) % lon_devices], "lon", by, True) for by in range(1, lon_devices)
    ]
    levels = []
    for level in range(level_count):
        pick = back[0]
        for by in range(1, lon_devices):
            pick = jnp.where((lon_index - by) % lon_devices == level, back[by], pick)
        levels.append(pick)
    return jnp.stack(levels, axis=1)


def on_device(tracers, courant_x, courant_y, cutoffs):
    if tracers.shape[1] == lax.axis_size("lon") and tracers.shape[2] >= HALO:
        return transposed_path(tracers, courant_x, courant_y, cutoffs)
    return tiled_path(tracers, courant_x, courant_y, cutoffs)


def solution(mesh):
    in_specs = (P(None, None, "lat", "lon"), P(None, "lat", "lon"), P(None, "lat", "lon"), P())
    out_specs = P(None, None, "lat", "lon")
    return jax.shard_map(
        on_device, mesh=mesh, in_specs=in_specs, out_specs=out_specs, check_vma=False
    )
```

```python
import math

import jax
import jax.numpy as jnp
from jax import lax
from jax.sharding import PartitionSpec as P


KMAX = 720
SUBSTEPS = 2
HALO = 3
MATMUL_PRECISION = lax.Precision.HIGH


def shift(x, axis, by, wrap):
    size = lax.axis_size(axis)
    pairs = [(i, (i + by) % size) for i in range(size) if wrap or 0 <= i + by < size]
    return lax.ppermute(x, axis, pairs)


def product_basis(tiles, cols, circle):
    split = max(b for b in range(1, cols + 1) if cols % b == 0 and b * b <= cols)
    per_class = KMAX // tiles
    k = tiles * jnp.arange(per_class, dtype=jnp.int32)[None, :] + jnp.arange(
        tiles, dtype=jnp.int32
    )[:, None]
    a = jnp.arange(cols // split, dtype=jnp.int32)
    b = jnp.arange(split, dtype=jnp.int32)
    step = 2.0 * math.pi / circle
    coarse = ((split * a[None, None, :] * k[:, :, None]) % circle).astype(jnp.float32) * step
    fine = ((b[None, None, :] * k[:, :, None]) % circle).astype(jnp.float32) * step
    ca, sa = jnp.cos(coarse)[:, :, :, None], jnp.sin(coarse)[:, :, :, None]
    cb, sb = jnp.cos(fine)[:, :, None], jnp.sin(fine)[:, :, None]
    cos_qk = (ca * cb - sa * sb).reshape(tiles, per_class, cols)
    sin_qk = (sa * cb + ca * sb).reshape(tiles, per_class, cols)
    return jnp.concatenate([cos_qk, sin_qk], axis=1)


def window(values, first_cell, last_cell, dim_at):
    return lax.slice_in_dim(values, first_cell, last_cell, axis=dim_at)


def ppm_flux(padded, courant, dim_at, cell_count):
    edge_values = 7.0 / 12.0 * (
        window(padded, 1, cell_count + 4, dim_at) + window(padded, 2, cell_count + 5, dim_at)
    ) - 1.0 / 12.0 * (
        window(padded, 0, cell_count + 3, dim_at) + window(padded, 3, cell_count + 6, dim_at)
    )
    left_edge = window(edge_values, 0, cell_count + 1, dim_at)
    mid_edge = window(edge_values, 1, cell_count + 2, dim_at)
    right_edge = window(edge_values, 2, cell_count + 3, dim_at)
    left_cell = window(padded, 2, cell_count + 3, dim_at)
    right_cell = window(padded, 3, cell_count + 4, dim_at)
    magnitude = jnp.abs(courant)
    six_left = 6.0 * left_cell - 3.0 * (left_edge + mid_edge)
    six_right = 6.0 * right_cell - 3.0 * (mid_edge + right_edge)
    from_left = mid_edge - 0.5 * magnitude * (
        mid_edge - left_edge - (1.0 - magnitude * (2.0 / 3.0)) * six_left
    )
    from_right = mid_edge + 0.5 * magnitude * (
        right_edge - mid_edge + (1.0 - magnitude * (2.0 / 3.0)) * six_right
    )
    return courant * jnp.where(courant >= 0.0, from_left, from_right)


def root_table(count, tile_of=None):
    d = jnp.arange(count, dtype=jnp.int32)
    tile = d if tile_of is None else tile_of
    angle = (d[:, None] * tile[None, :] % count).astype(jnp.float32) * (2.0 * math.pi / count)
    cos_dr, sin_dr = jnp.cos(angle), jnp.sin(angle)
    cos_dr = jnp.where(jnp.abs(cos_dr) < 1e-6, 0.0, cos_dr)
    sin_dr = jnp.where(jnp.abs(sin_dr) < 1e-6, 0.0, sin_dr)
    return cos_dr, sin_dr


def class_basis(tiles, cols, circle, halo=HALO):
    per_class = KMAX // tiles
    r = jnp.arange(tiles, dtype=jnp.int32)
    m = jnp.arange(per_class, dtype=jnp.int32)
    q = jnp.arange(-halo, cols + halo, dtype=jnp.int32) % circle
    k = tiles * m[None, :] + r[:, None]
    phase = (q[None, :, None] * k[:, None, :]) % circle
    angle = phase.astype(jnp.float32) * (2.0 * math.pi / circle)
    return jnp.concatenate([jnp.cos(angle), jnp.sin(angle)], axis=2)


def filter_rows(rows, basis, roots, weights, polar, halo=HALO, m_major=False):
    _, count, cols = rows.shape
    cos_dr, sin_dr = roots
    z_re = jnp.sum(cos_dr[:, :, None, None] * rows[None], axis=1)
    z_im = -jnp.sum(sin_dr[:, :, None, None] * rows[None], axis=1)
    z = jnp.concatenate([z_re, z_im], axis=1)
    z = jnp.pad(z, ((0, 0), (0, 0), (halo, halo)))
    q_axis, m_axis = (2, 1) if m_major else (1, 2)
    prod = lax.dot_general(z, basis, (((2,), (q_axis,)), ((0,), (0,))), precision=MATMUL_PRECISION)
    per_class = basis.shape[m_axis] // 2
    zc, zs = prod[:, :count, :per_class], prod[:, :count, per_class:]
    wc, ws = prod[:, count:, :per_class], prod[:, count:, per_class:]
    real = (zc + ws) * weights
    imag = (zs - wc) * weights
    spec = jnp.concatenate(
        [jnp.concatenate([real, imag], axis=2), jnp.concatenate([-imag, real], axis=2)], axis=1
    )
    back = lax.dot_general(spec, basis, (((2,), (m_axis,)), ((0,), (0,))), precision=MATMUL_PRECISION)
    w_re, w_im = back[:, :count], back[:, count:]
    smooth = jnp.sum(
        cos_dr[:, :, None, None] * w_re[:, None] - sin_dr[:, :, None, None] * w_im[:, None], axis=0
    )
    wide = rows
    if halo:
        left = jnp.roll(rows[:, :, cols - halo :], 1, axis=0)
        right = jnp.roll(rows[:, :, :halo], -1, axis=0)
        wide = jnp.concatenate([left, rows, right], axis=2)
    return jnp.where(polar[None, :, None], smooth, wide)


def tiled_path(tracers, courant_x, courant_y, cutoffs):
    tracer_count, level_count, lat_rows, lon_cols = tracers.shape
    field_count = tracer_count * level_count
    lat_devices = lax.axis_size("lat")
    lon_devices = lax.axis_size("lon")
    lat_index = lax.axis_index("lat")
    lon_index = lax.axis_index("lon")
    circle = lon_cols * lon_devices
    total_rows = lat_rows * lat_devices
    row_global = lat_index * lat_rows + jnp.arange(lat_rows, dtype=jnp.int32)
    face_global = lat_index * lat_rows + jnp.arange(lat_rows + 1, dtype=jnp.int32)
    face_angle = (face_global.astype(jnp.float32) / total_rows - 0.5) * math.pi
    face_weight = jnp.where(
        (face_global == 0) | (face_global == total_rows), 0.0, jnp.cos(face_angle)
    )
    center_weight = jnp.cos(((row_global.astype(jnp.float32) + 0.5) / total_rows - 0.5) * math.pi)
    is_south = lat_index == 0
    is_north = lat_index == lat_devices - 1

    count = field_count * lat_rows // lon_devices
    flat = lon_index * count + jnp.arange(count, dtype=jnp.int32)
    held_global = lat_index * lat_rows + flat % lat_rows
    polar = (held_global < total_rows // 4) | (held_global >= total_rows - total_rows // 4)
    cut = jnp.take(cutoffs, held_global)
    per_class = KMAX // lon_devices
    k = lon_devices * jnp.arange(per_class, dtype=jnp.int32)[None, :] + jnp.arange(
        lon_devices, dtype=jnp.int32
    )[:, None]
    scale = jnp.where(k == 0, 1.0 / circle, 2.0 / circle).astype(jnp.float32)
    weights = jnp.where(k[:, None, :] < cut[None, :, None], scale[:, None, :], 0.0)
    basis = class_basis(lon_devices, lon_cols, circle)
    roots = root_table(lon_devices)

    west_cx = shift(courant_x[:, :, lon_cols - 1 :], "lon", 1, True)
    north_cy = shift(courant_y[:, :1], "lat", -1, False)
    east_courant = jnp.concatenate([west_cx, courant_x], axis=2)
    north_courant = jnp.concatenate(
        [courant_y, jnp.where(is_north, 0.0, north_cy)], axis=1
    )

    def lat_halos(state):
        south_in = shift(state[:, :, lat_rows - HALO :], "lat", 1, False)
        north_in = shift(state[:, :, :HALO], "lat", -1, False)
        edge = jnp.where(is_south, state[:, :, :HALO], state[:, :, lat_rows - HALO :])
        far = shift(edge, "lon", lon_devices // 2, True)
        far_rev = jnp.concatenate([far[:, :, 2:3], far[:, :, 1:2], far[:, :, 0:1]], axis=2)
        south_rows = jnp.where(is_south, far_rev, south_in)
        north_rows = jnp.where(is_north, far_rev, north_in)
        return jnp.concatenate([south_rows, state, north_rows], axis=2)

    state = tracers
    west_in = shift(state[..., lon_cols - HALO :], "lon", 1, True)
    east_in = shift(state[..., :HALO], "lon", -1, True)
    wrapped = jnp.concatenate([west_in, state, east_in], axis=3)
    for substep in range(SUBSTEPS):
        extended = lat_halos(state)
        zonal = ppm_flux(wrapped, east_courant, 3, lon_cols)
        meridional = ppm_flux(extended, north_courant, 2, lat_rows) * face_weight[:, None]
        change = (
            zonal[..., 1:]
            - zonal[..., :-1]
            + (meridional[:, :, 1:] - meridional[:, :, :-1]) / center_weight[:, None]
        )
        state = state - change
        rows = state.reshape(lon_devices, count, lon_cols)
        rows = lax.all_to_all(rows, "lon", 0, 0)
        wide = filter_rows(rows, basis, roots, weights, polar)
        if substep == SUBSTEPS - 1:
            wide = wide[:, :, HALO : HALO + lon_cols]
        wide = lax.all_to_all(wide, "lon", 0, 0)
        wrapped = wide.reshape(tracer_count, level_count, lat_rows, wide.shape[2])
        state = wrapped if substep == SUBSTEPS - 1 else wrapped[..., HALO : HALO + lon_cols]
    return state


def transposed_path(tracers, courant_x, courant_y, cutoffs):
    tracer_count, level_count, lat_rows, lon_cols = tracers.shape
    lat_devices = lax.axis_size("lat")
    lon_devices = lax.axis_size("lon")
    lat_index = lax.axis_index("lat")
    circle = lon_cols * lon_devices
    total_rows = lat_rows * lat_devices
    row_global = lat_index * lat_rows + jnp.arange(lat_rows, dtype=jnp.int32)
    face_global = lat_index * lat_rows + jnp.arange(lat_rows + 1, dtype=jnp.int32)
    face_angle = (face_global.astype(jnp.float32) / total_rows - 0.5) * math.pi
    face_weight = jnp.where(
        (face_global == 0) | (face_global == total_rows), 0.0, jnp.cos(face_angle)
    )
    center_weight = jnp.cos(((row_global.astype(jnp.float32) + 0.5) / total_rows - 0.5) * math.pi)
    is_south = lat_index == 0
    is_north = lat_index == lat_devices - 1

    count = tracer_count * lat_rows
    lon_index = lax.axis_index("lon")

    def payload_for(level):
        return jnp.concatenate(
            [
                lax.dynamic_index_in_dim(tracers, level, 1, keepdims=False).reshape(count, lon_cols),
                lax.dynamic_index_in_dim(courant_x, level, 0, keepdims=False),
                lax.dynamic_index_in_dim(courant_y, level, 0, keepdims=False),
            ],
            axis=0,
        )

    pieces = [payload_for(lon_index)]
    for by in range(1, lon_devices):
        pieces.append(
            lax.ppermute(payload_for(lon_index ^ by), "lon", [(i, i ^ by) for i in range(lon_devices)])
        )
    positions = jnp.arange(lon_devices, dtype=jnp.int32)
    tile_at = lon_index ^ positions
    west_at = lon_index ^ ((tile_at - 1) % lon_devices)
    east_at = lon_index ^ ((tile_at + 1) % lon_devices)
    payload = jnp.stack(pieces)
    state = payload[:, :count].reshape(lon_devices, tracer_count, lat_rows, lon_cols)
    cx = payload[:, None, count : count + lat_rows]
    cy = payload[:, None, count + lat_rows :]
    east_courant = jnp.concatenate([jnp.take(cx[..., lon_cols - 1 :], west_at, axis=0), cx], axis=3)

    held_global = lat_index * lat_rows + jnp.arange(count, dtype=jnp.int32) % lat_rows
    polar = (held_global < total_rows // 4) | (held_global >= total_rows - total_rows // 4)
    cut = jnp.take(cutoffs, held_global)
    per_class = KMAX // lon_devices
    k = lon_devices * jnp.arange(per_class, dtype=jnp.int32)[None, :] + jnp.arange(
        lon_devices, dtype=jnp.int32
    )[:, None]
    scale = jnp.where(k == 0, 1.0 / circle, 2.0 / circle).astype(jnp.float32)
    weights = jnp.where(k[:, None, :] < cut[None, :, None], scale[:, None, :], 0.0)
    basis = product_basis(lon_devices, lon_cols, circle)
    roots = root_table(lon_devices, tile_at)

    for substep in range(SUBSTEPS):
        top = state[:, :, lat_rows - HALO :].reshape(lon_devices, tracer_count * HALO, lon_cols)
        bottom = state[:, :, :HALO].reshape(lon_devices, tracer_count * HALO, lon_cols)
        if substep == 0:
            bottom = jnp.concatenate([bottom, cy[:, 0, :1]], axis=1)
            top = jnp.concatenate([top, jnp.zeros_like(cy[:, 0, :1])], axis=1)
        is_even = lat_index % 2 == 0
        recv_a = lax.ppermute(
            jnp.where(is_even, top, bottom), "lat", [(i, i ^ 1) for i in range(lat_devices) if i ^ 1 < lat_devices]
        )
        recv_b = lax.ppermute(
            jnp.where(is_even, bottom, top),
            "lat",
            [(i, i + (1 if i % 2 else -1)) for i in range(lat_devices) if 0 <= i + (1 if i % 2 else -1) < lat_devices],
        )
        from_south = jnp.where(is_even, recv_b, recv_a)
        from_north = jnp.where(is_even, recv_a, recv_b)
        south_in = from_south[:, : tracer_count * HALO].reshape(
            lon_devices, tracer_count, HALO, lon_cols
        )
        north_in = from_north[:, : tracer_count * HALO].reshape(
            lon_devices, tracer_count, HALO, lon_cols
        )
        if substep == 0:
            north_cy = jnp.where(is_north, 0.0, from_north[:, None, tracer_count * HALO :])
            north_courant = jnp.concatenate([cy, north_cy], axis=2)
        edge = jnp.where(is_south, state[:, :, :HALO], state[:, :, lat_rows - HALO :])
        far = jnp.roll(edge, lon_devices // 2, axis=0)
        far_rev = jnp.concatenate([far[:, :, 2:3], far[:, :, 1:2], far[:, :, 0:1]], axis=2)
        south_rows = jnp.where(is_south, far_rev, south_in)
        north_rows = jnp.where(is_north, far_rev, north_in)
        extended = jnp.concatenate([south_rows, state, north_rows], axis=2)
        wrapped = jnp.concatenate(
            [
                jnp.take(state[..., lon_cols - HALO :], west_at, axis=0),
                state,
                jnp.take(state[..., :HALO], east_at, axis=0),
            ],
            axis=3,
        )
        zonal = ppm_flux(wrapped, east_courant, 3, lon_cols)
        zonal_change = lax.optimization_barrier(zonal[..., 1:] - zonal[..., :-1])
        meridional = ppm_flux(extended, north_courant, 2, lat_rows) * face_weight[:, None]
        change = zonal_change + (meridional[:, :, 1:] - meridional[:, :, :-1]) / center_weight[:, None]
        state = state - change
        rows = state.reshape(lon_devices, count, lon_cols)
        rows = filter_rows(rows, basis, roots, weights, polar, 0, True)
        state = rows.reshape(lon_devices, tracer_count, lat_rows, lon_cols)

    back = [state[0]] + [
        lax.ppermute(state[by], "lon", [(i, i ^ by) for i in range(lon_devices)])
        for by in range(1, lon_devices)
    ]
    levels = []
    for level in range(level_count):
        pick = back[0]
        for by in range(1, lon_devices):
            pick = jnp.where((lon_index ^ by) == level, back[by], pick)
        levels.append(pick)
    return jnp.stack(levels, axis=1)


def on_device(tracers, courant_x, courant_y, cutoffs):
    lon_devices = lax.axis_size("lon")
    power_of_two = lon_devices & (lon_devices - 1) == 0
    if tracers.shape[1] == lon_devices and power_of_two and tracers.shape[2] >= HALO:
        return transposed_path(tracers, courant_x, courant_y, cutoffs)
    return tiled_path(tracers, courant_x, courant_y, cutoffs)


def solution(mesh):
    in_specs = (P(None, None, "lat", "lon"), P(None, "lat", "lon"), P(None, "lat", "lon"), P())
    out_specs = P(None, None, "lat", "lon")
    return jax.shard_map(
        on_device, mesh=mesh, in_specs=in_specs, out_specs=out_specs, check_vma=False
    )
```

```python
import math

import jax
import jax.numpy as jnp
from jax import lax
from jax.sharding import PartitionSpec as P


KMAX = 720
SUBSTEPS = 2
HALO = 3
MATMUL_PRECISION = lax.Precision.HIGH


def shift(x, axis, by, wrap):
    size = lax.axis_size(axis)
    pairs = [(i, (i + by) % size) for i in range(size) if wrap or 0 <= i + by < size]
    return lax.ppermute(x, axis, pairs)


def product_basis(tiles, cols, circle):
    split = max(b for b in range(1, cols + 1) if cols % b == 0 and b * b <= cols)
    per_class = KMAX // tiles
    k = tiles * jnp.arange(per_class, dtype=jnp.int32)[None, :] + jnp.arange(
        tiles, dtype=jnp.int32
    )[:, None]
    a = jnp.arange(cols // split, dtype=jnp.int32)
    b = jnp.arange(split, dtype=jnp.int32)
    step = 2.0 * math.pi / circle
    coarse = ((split * a[None, None, :] * k[:, :, None]) % circle).astype(jnp.float32) * step
    fine = ((b[None, None, :] * k[:, :, None]) % circle).astype(jnp.float32) * step
    ca, sa = jnp.cos(coarse)[:, :, :, None], jnp.sin(coarse)[:, :, :, None]
    cb, sb = jnp.cos(fine)[:, :, None], jnp.sin(fine)[:, :, None]
    cos_qk = (ca * cb - sa * sb).reshape(tiles, per_class, cols)
    sin_qk = (sa * cb + ca * sb).reshape(tiles, per_class, cols)
    return jnp.concatenate([cos_qk, sin_qk], axis=1)


def window(values, first_cell, last_cell, dim_at):
    return lax.slice_in_dim(values, first_cell, last_cell, axis=dim_at)


def ppm_flux(padded, courant, dim_at, cell_count):
    edge_values = 7.0 / 12.0 * (
        window(padded, 1, cell_count + 4, dim_at) + window(padded, 2, cell_count + 5, dim_at)
    ) - 1.0 / 12.0 * (
        window(padded, 0, cell_count + 3, dim_at) + window(padded, 3, cell_count + 6, dim_at)
    )
    left_edge = window(edge_values, 0, cell_count + 1, dim_at)
    mid_edge = window(edge_values, 1, cell_count + 2, dim_at)
    right_edge = window(edge_values, 2, cell_count + 3, dim_at)
    left_cell = window(padded, 2, cell_count + 3, dim_at)
    right_cell = window(padded, 3, cell_count + 4, dim_at)
    magnitude = jnp.abs(courant)
    six_left = 6.0 * left_cell - 3.0 * (left_edge + mid_edge)
    six_right = 6.0 * right_cell - 3.0 * (mid_edge + right_edge)
    from_left = mid_edge - 0.5 * magnitude * (
        mid_edge - left_edge - (1.0 - magnitude * (2.0 / 3.0)) * six_left
    )
    from_right = mid_edge + 0.5 * magnitude * (
        right_edge - mid_edge + (1.0 - magnitude * (2.0 / 3.0)) * six_right
    )
    return courant * jnp.where(courant >= 0.0, from_left, from_right)


def root_table(count, tile_of=None):
    d = jnp.arange(count, dtype=jnp.int32)
    tile = d if tile_of is None else tile_of
    angle = (d[:, None] * tile[None, :] % count).astype(jnp.float32) * (2.0 * math.pi / count)
    cos_dr, sin_dr = jnp.cos(angle), jnp.sin(angle)
    cos_dr = jnp.where(jnp.abs(cos_dr) < 1e-6, 0.0, cos_dr)
    sin_dr = jnp.where(jnp.abs(sin_dr) < 1e-6, 0.0, sin_dr)
    return cos_dr, sin_dr


def class_basis(tiles, cols, circle, halo=HALO):
    per_class = KMAX // tiles
    r = jnp.arange(tiles, dtype=jnp.int32)
    m = jnp.arange(per_class, dtype=jnp.int32)
    q = jnp.arange(-halo, cols + halo, dtype=jnp.int32) % circle
    k = tiles * m[None, :] + r[:, None]
    phase = (q[None, :, None] * k[:, None, :]) % circle
    angle = phase.astype(jnp.float32) * (2.0 * math.pi / circle)
    return jnp.concatenate([jnp.cos(angle), jnp.sin(angle)], axis=2)


def filter_rows(rows, basis, roots, weights, polar, halo=HALO, m_major=False):
    _, count, cols = rows.shape
    cos_dr, sin_dr = roots
    z_re = jnp.sum(cos_dr[:, :, None, None] * rows[None], axis=1)
    z_im = -jnp.sum(sin_dr[:, :, None, None] * rows[None], axis=1)
    z = jnp.concatenate([z_re, z_im], axis=1)
    z = jnp.pad(z, ((0, 0), (0, 0), (halo, halo)))
    q_axis, m_axis = (2, 1) if m_major else (1, 2)
    prod = lax.dot_general(z, basis, (((2,), (q_axis,)), ((0,), (0,))), precision=MATMUL_PRECISION)
    per_class = basis.shape[m_axis] // 2
    zc, zs = prod[:, :count, :per_class], prod[:, :count, per_class:]
    wc, ws = prod[:, count:, :per_class], prod[:, count:, per_class:]
    real = (zc + ws) * weights
    imag = (zs - wc) * weights
    spec = jnp.concatenate(
        [jnp.concatenate([real, imag], axis=2), jnp.concatenate([-imag, real], axis=2)], axis=1
    )
    back = lax.dot_general(spec, basis, (((2,), (m_axis,)), ((0,), (0,))), precision=MATMUL_PRECISION)
    w_re, w_im = back[:, :count], back[:, count:]
    smooth = jnp.sum(
        cos_dr[:, :, None, None] * w_re[:, None] - sin_dr[:, :, None, None] * w_im[:, None], axis=0
    )
    wide = rows
    if halo:
        left = jnp.roll(rows[:, :, cols - halo :], 1, axis=0)
        right = jnp.roll(rows[:, :, :halo], -1, axis=0)
        wide = jnp.concatenate([left, rows, right], axis=2)
    return jnp.where(polar[None, :, None], smooth, wide)


def tiled_path(tracers, courant_x, courant_y, cutoffs):
    tracer_count, level_count, lat_rows, lon_cols = tracers.shape
    field_count = tracer_count * level_count
    lat_devices = lax.axis_size("lat")
    lon_devices = lax.axis_size("lon")
    lat_index = lax.axis_index("lat")
    lon_index = lax.axis_index("lon")
    circle = lon_cols * lon_devices
    total_rows = lat_rows * lat_devices
    row_global = lat_index * lat_rows + jnp.arange(lat_rows, dtype=jnp.int32)
    face_global = lat_index * lat_rows + jnp.arange(lat_rows + 1, dtype=jnp.int32)
    face_angle = (face_global.astype(jnp.float32) / total_rows - 0.5) * math.pi
    face_weight = jnp.where(
        (face_global == 0) | (face_global == total_rows), 0.0, jnp.cos(face_angle)
    )
    center_weight = jnp.cos(((row_global.astype(jnp.float32) + 0.5) / total_rows - 0.5) * math.pi)
    is_south = lat_index == 0
    is_north = lat_index == lat_devices - 1

    count = field_count * lat_rows // lon_devices
    flat = lon_index * count + jnp.arange(count, dtype=jnp.int32)
    held_global = lat_index * lat_rows + flat % lat_rows
    polar = (held_global < total_rows // 4) | (held_global >= total_rows - total_rows // 4)
    cut = jnp.take(cutoffs, held_global)
    per_class = KMAX // lon_devices
    k = lon_devices * jnp.arange(per_class, dtype=jnp.int32)[None, :] + jnp.arange(
        lon_devices, dtype=jnp.int32
    )[:, None]
    scale = jnp.where(k == 0, 1.0 / circle, 2.0 / circle).astype(jnp.float32)
    weights = jnp.where(k[:, None, :] < cut[None, :, None], scale[:, None, :], 0.0)
    basis = class_basis(lon_devices, lon_cols, circle)
    roots = root_table(lon_devices)

    west_cx = shift(courant_x[:, :, lon_cols - 1 :], "lon", 1, True)
    north_cy = shift(courant_y[:, :1], "lat", -1, False)
    east_courant = jnp.concatenate([west_cx, courant_x], axis=2)
    north_courant = jnp.concatenate(
        [courant_y, jnp.where(is_north, 0.0, north_cy)], axis=1
    )

    def lat_halos(state):
        south_in = shift(state[:, :, lat_rows - HALO :], "lat", 1, False)
        north_in = shift(state[:, :, :HALO], "lat", -1, False)
        edge = jnp.where(is_south, state[:, :, :HALO], state[:, :, lat_rows - HALO :])
        far = shift(edge, "lon", lon_devices // 2, True)
        far_rev = jnp.concatenate([far[:, :, 2:3], far[:, :, 1:2], far[:, :, 0:1]], axis=2)
        south_rows = jnp.where(is_south, far_rev, south_in)
        north_rows = jnp.where(is_north, far_rev, north_in)
        return jnp.concatenate([south_rows, state, north_rows], axis=2)

    state = tracers
    west_in = shift(state[..., lon_cols - HALO :], "lon", 1, True)
    east_in = shift(state[..., :HALO], "lon", -1, True)
    wrapped = jnp.concatenate([west_in, state, east_in], axis=3)
    for substep in range(SUBSTEPS):
        extended = lat_halos(state)
        zonal = ppm_flux(wrapped, east_courant, 3, lon_cols)
        meridional = ppm_flux(extended, north_courant, 2, lat_rows) * face_weight[:, None]
        change = (
            zonal[..., 1:]
            - zonal[..., :-1]
            + (meridional[:, :, 1:] - meridional[:, :, :-1]) / center_weight[:, None]
        )
        state = state - change
        rows = state.reshape(lon_devices, count, lon_cols)
        rows = lax.all_to_all(rows, "lon", 0, 0)
        wide = filter_rows(rows, basis, roots, weights, polar)
        if substep == SUBSTEPS - 1:
            wide = wide[:, :, HALO : HALO + lon_cols]
        wide = lax.all_to_all(wide, "lon", 0, 0)
        wrapped = wide.reshape(tracer_count, level_count, lat_rows, wide.shape[2])
        state = wrapped if substep == SUBSTEPS - 1 else wrapped[..., HALO : HALO + lon_cols]
    return state


def transposed_path(tracers, courant_x, courant_y, cutoffs):
    tracer_count, level_count, lat_rows, lon_cols = tracers.shape
    lat_devices = lax.axis_size("lat")
    lon_devices = lax.axis_size("lon")
    lat_index = lax.axis_index("lat")
    circle = lon_cols * lon_devices
    total_rows = lat_rows * lat_devices
    row_global = lat_index * lat_rows + jnp.arange(lat_rows, dtype=jnp.int32)
    face_global = lat_index * lat_rows + jnp.arange(lat_rows + 1, dtype=jnp.int32)
    face_angle = (face_global.astype(jnp.float32) / total_rows - 0.5) * math.pi
    face_weight = jnp.where(
        (face_global == 0) | (face_global == total_rows), 0.0, jnp.cos(face_angle)
    )
    center_weight = jnp.cos(((row_global.astype(jnp.float32) + 0.5) / total_rows - 0.5) * math.pi)
    is_south = lat_index == 0
    is_north = lat_index == lat_devices - 1

    count = tracer_count * lat_rows
    lon_index = lax.axis_index("lon")

    def payload_for(level):
        return jnp.concatenate(
            [
                lax.dynamic_index_in_dim(tracers, level, 1, keepdims=False).reshape(count, lon_cols),
                lax.dynamic_index_in_dim(courant_x, level, 0, keepdims=False),
                lax.dynamic_index_in_dim(courant_y, level, 0, keepdims=False),
            ],
            axis=0,
        )

    pieces = [payload_for(lon_index)]
    for by in range(1, lon_devices):
        pieces.append(shift(payload_for((lon_index + by) % lon_devices), "lon", by, True))
    payload = jnp.stack(pieces)
    state = payload[:, :count].reshape(lon_devices, tracer_count, lat_rows, lon_cols)
    cx = payload[:, None, count : count + lat_rows]
    cy = payload[:, None, count + lat_rows :]
    east_courant = jnp.concatenate([jnp.roll(cx[..., lon_cols - 1 :], -1, axis=0), cx], axis=3)

    held_global = lat_index * lat_rows + jnp.arange(count, dtype=jnp.int32) % lat_rows
    polar = (held_global < total_rows // 4) | (held_global >= total_rows - total_rows // 4)
    cut = jnp.take(cutoffs, held_global)
    per_class = KMAX // lon_devices
    k = lon_devices * jnp.arange(per_class, dtype=jnp.int32)[None, :] + jnp.arange(
        lon_devices, dtype=jnp.int32
    )[:, None]
    scale = jnp.where(k == 0, 1.0 / circle, 2.0 / circle).astype(jnp.float32)
    weights = jnp.where(k[:, None, :] < cut[None, :, None], scale[:, None, :], 0.0)
    basis = product_basis(lon_devices, lon_cols, circle)
    roots = root_table(
        lon_devices, (lax.axis_index("lon") - jnp.arange(lon_devices, dtype=jnp.int32)) % lon_devices
    )

    for substep in range(SUBSTEPS):
        top = state[:, :, lat_rows - HALO :].reshape(lon_devices, tracer_count * HALO, lon_cols)
        bottom = state[:, :, :HALO].reshape(lon_devices, tracer_count * HALO, lon_cols)
        if substep == 0:
            bottom = jnp.concatenate([bottom, cy[:, 0, :1]], axis=1)
            top = jnp.concatenate([top, jnp.zeros_like(cy[:, 0, :1])], axis=1)
        is_even = lat_index % 2 == 0
        recv_a = lax.ppermute(
            jnp.where(is_even, top, bottom), "lat", [(i, i ^ 1) for i in range(lat_devices) if i ^ 1 < lat_devices]
        )
        recv_b = lax.ppermute(
            jnp.where(is_even, bottom, top),
            "lat",
            [(i, i + (1 if i % 2 else -1)) for i in range(lat_devices) if 0 <= i + (1 if i % 2 else -1) < lat_devices],
        )
        from_south = jnp.where(is_even, recv_b, recv_a)
        from_north = jnp.where(is_even, recv_a, recv_b)
        south_in = from_south[:, : tracer_count * HALO].reshape(
            lon_devices, tracer_count, HALO, lon_cols
        )
        north_in = from_north[:, : tracer_count * HALO].reshape(
            lon_devices, tracer_count, HALO, lon_cols
        )
        if substep == 0:
            north_cy = jnp.where(is_north, 0.0, from_north[:, None, tracer_count * HALO :])
            north_courant = jnp.concatenate([cy, north_cy], axis=2)
        edge = jnp.where(is_south, state[:, :, :HALO], state[:, :, lat_rows - HALO :])
        far = jnp.roll(edge, lon_devices // 2, axis=0)
        far_rev = jnp.concatenate([far[:, :, 2:3], far[:, :, 1:2], far[:, :, 0:1]], axis=2)
        south_rows = jnp.where(is_south, far_rev, south_in)
        north_rows = jnp.where(is_north, far_rev, north_in)
        extended = jnp.concatenate([south_rows, state, north_rows], axis=2)
        wrapped = jnp.concatenate(
            [
                jnp.roll(state[..., lon_cols - HALO :], -1, axis=0),
                state,
                jnp.roll(state[..., :HALO], 1, axis=0),
            ],
            axis=3,
        )
        zonal = ppm_flux(wrapped, east_courant, 3, lon_cols)
        zonal_change = lax.optimization_barrier(zonal[..., 1:] - zonal[..., :-1])
        meridional = ppm_flux(extended, north_courant, 2, lat_rows) * face_weight[:, None]
        change = zonal_change + (meridional[:, :, 1:] - meridional[:, :, :-1]) / center_weight[:, None]
        state = state - change
        rows = state.reshape(lon_devices, count, lon_cols)
        rows = filter_rows(rows, basis, roots, weights, polar, 0, True)
        state = rows.reshape(lon_devices, tracer_count, lat_rows, lon_cols)

    back = [state[0]] + [
        shift(state[(lon_devices - by) % lon_devices], "lon", by, True) for by in range(1, lon_devices)
    ]
    levels = []
    for level in range(level_count):
        pick = back[0]
        for by in range(1, lon_devices):
            pick = jnp.where((lon_index - by) % lon_devices == level, back[by], pick)
        levels.append(pick)
    return jnp.stack(levels, axis=1)


def on_device(tracers, courant_x, courant_y, cutoffs):
    if tracers.shape[1] == lax.axis_size("lon") and tracers.shape[2] >= HALO:
        return transposed_path(tracers, courant_x, courant_y, cutoffs)
    return tiled_path(tracers, courant_x, courant_y, cutoffs)


def solution(mesh):
    in_specs = (P(None, None, "lat", "lon"), P(None, "lat", "lon"), P(None, "lat", "lon"), P())
    out_specs = P(None, None, "lat", "lon")
    return jax.shard_map(
        on_device, mesh=mesh, in_specs=in_specs, out_specs=out_specs, check_vma=False
    )
```

```python
import math

import jax
import jax.numpy as jnp
from jax import lax
from jax.sharding import PartitionSpec as P


KMAX = 720
SUBSTEPS = 2
HALO = 3
MATMUL_PRECISION = lax.Precision.HIGH


def shift(x, axis, by, wrap):
    size = lax.axis_size(axis)
    pairs = [(i, (i + by) % size) for i in range(size) if wrap or 0 <= i + by < size]
    return lax.ppermute(x, axis, pairs)


def product_basis(tiles, cols, circle):
    split = max(b for b in range(1, cols + 1) if cols % b == 0 and b * b <= cols)
    per_class = KMAX // tiles
    k = tiles * jnp.arange(per_class, dtype=jnp.int32)[None, :] + jnp.arange(
        tiles, dtype=jnp.int32
    )[:, None]
    a = jnp.arange(cols // split, dtype=jnp.int32)
    b = jnp.arange(split, dtype=jnp.int32)
    step = 2.0 * math.pi / circle
    coarse = ((split * a[None, None, :] * k[:, :, None]) % circle).astype(jnp.float32) * step
    fine = ((b[None, None, :] * k[:, :, None]) % circle).astype(jnp.float32) * step
    ca, sa = jnp.cos(coarse)[:, :, :, None], jnp.sin(coarse)[:, :, :, None]
    cb, sb = jnp.cos(fine)[:, :, None], jnp.sin(fine)[:, :, None]
    cos_qk = (ca * cb - sa * sb).reshape(tiles, per_class, cols)
    sin_qk = (sa * cb + ca * sb).reshape(tiles, per_class, cols)
    return jnp.concatenate([cos_qk, sin_qk], axis=1)


def window(values, first_cell, last_cell, dim_at):
    return lax.slice_in_dim(values, first_cell, last_cell, axis=dim_at)


def ppm_flux(padded, courant, dim_at, cell_count):
    edge_values = 7.0 / 12.0 * (
        window(padded, 1, cell_count + 4, dim_at) + window(padded, 2, cell_count + 5, dim_at)
    ) - 1.0 / 12.0 * (
        window(padded, 0, cell_count + 3, dim_at) + window(padded, 3, cell_count + 6, dim_at)
    )
    left_edge = window(edge_values, 0, cell_count + 1, dim_at)
    mid_edge = window(edge_values, 1, cell_count + 2, dim_at)
    right_edge = window(edge_values, 2, cell_count + 3, dim_at)
    left_cell = window(padded, 2, cell_count + 3, dim_at)
    right_cell = window(padded, 3, cell_count + 4, dim_at)
    magnitude = jnp.abs(courant)
    six_left = 6.0 * left_cell - 3.0 * (left_edge + mid_edge)
    six_right = 6.0 * right_cell - 3.0 * (mid_edge + right_edge)
    from_left = mid_edge - 0.5 * magnitude * (
        mid_edge - left_edge - (1.0 - magnitude * (2.0 / 3.0)) * six_left
    )
    from_right = mid_edge + 0.5 * magnitude * (
        right_edge - mid_edge + (1.0 - magnitude * (2.0 / 3.0)) * six_right
    )
    return courant * jnp.where(courant >= 0.0, from_left, from_right)


def root_table(count, tile_of=None):
    d = jnp.arange(count, dtype=jnp.int32)
    tile = d if tile_of is None else tile_of
    angle = (d[:, None] * tile[None, :] % count).astype(jnp.float32) * (2.0 * math.pi / count)
    cos_dr, sin_dr = jnp.cos(angle), jnp.sin(angle)
    cos_dr = jnp.where(jnp.abs(cos_dr) < 1e-6, 0.0, cos_dr)
    sin_dr = jnp.where(jnp.abs(sin_dr) < 1e-6, 0.0, sin_dr)
    return cos_dr, sin_dr


def class_basis(tiles, cols, circle, halo=HALO):
    per_class = KMAX // tiles
    r = jnp.arange(tiles, dtype=jnp.int32)
    m = jnp.arange(per_class, dtype=jnp.int32)
    q = jnp.arange(-halo, cols + halo, dtype=jnp.int32) % circle
    k = tiles * m[None, :] + r[:, None]
    phase = (q[None, :, None] * k[:, None, :]) % circle
    angle = phase.astype(jnp.float32) * (2.0 * math.pi / circle)
    return jnp.concatenate([jnp.cos(angle), jnp.sin(angle)], axis=2)


def filter_rows(rows, basis, roots, weights, polar, halo=HALO, m_major=False):
    _, count, cols = rows.shape
    cos_dr, sin_dr = roots
    z_re = jnp.sum(cos_dr[:, :, None, None] * rows[None], axis=1)
    z_im = -jnp.sum(sin_dr[:, :, None, None] * rows[None], axis=1)
    z = jnp.concatenate([z_re, z_im], axis=1)
    z = jnp.pad(z, ((0, 0), (0, 0), (halo, halo)))
    q_axis, m_axis = (2, 1) if m_major else (1, 2)
    prod = lax.dot_general(z, basis, (((2,), (q_axis,)), ((0,), (0,))), precision=MATMUL_PRECISION)
    per_class = basis.shape[m_axis] // 2
    zc, zs = prod[:, :count, :per_class], prod[:, :count, per_class:]
    wc, ws = prod[:, count:, :per_class], prod[:, count:, per_class:]
    real = (zc + ws) * weights
    imag = (zs - wc) * weights
    spec = jnp.concatenate(
        [jnp.concatenate([real, imag], axis=2), jnp.concatenate([-imag, real], axis=2)], axis=1
    )
    back = lax.dot_general(spec, basis, (((2,), (m_axis,)), ((0,), (0,))), precision=MATMUL_PRECISION)
    w_re, w_im = back[:, :count], back[:, count:]
    smooth = jnp.sum(
        cos_dr[:, :, None, None] * w_re[:, None] - sin_dr[:, :, None, None] * w_im[:, None], axis=0
    )
    wide = rows
    if halo:
        left = jnp.roll(rows[:, :, cols - halo :], 1, axis=0)
        right = jnp.roll(rows[:, :, :halo], -1, axis=0)
        wide = jnp.concatenate([left, rows, right], axis=2)
    return jnp.where(polar[None, :, None], smooth, wide)


def tiled_path(tracers, courant_x, courant_y, cutoffs):
    tracer_count, level_count, lat_rows, lon_cols = tracers.shape
    field_count = tracer_count * level_count
    lat_devices = lax.axis_size("lat")
    lon_devices = lax.axis_size("lon")
    lat_index = lax.axis_index("lat")
    lon_index = lax.axis_index("lon")
    circle = lon_cols * lon_devices
    total_rows = lat_rows * lat_devices
    row_global = lat_index * lat_rows + jnp.arange(lat_rows, dtype=jnp.int32)
    face_global = lat_index * lat_rows + jnp.arange(lat_rows + 1, dtype=jnp.int32)
    face_angle = (face_global.astype(jnp.float32) / total_rows - 0.5) * math.pi
    face_weight = jnp.where(
        (face_global == 0) | (face_global == total_rows), 0.0, jnp.cos(face_angle)
    )
    center_weight = jnp.cos(((row_global.astype(jnp.float32) + 0.5) / total_rows - 0.5) * math.pi)
    is_south = lat_index == 0
    is_north = lat_index == lat_devices - 1

    count = field_count * lat_rows // lon_devices
    flat = lon_index * count + jnp.arange(count, dtype=jnp.int32)
    held_global = lat_index * lat_rows + flat % lat_rows
    polar = (held_global < total_rows // 4) | (held_global >= total_rows - total_rows // 4)
    cut = jnp.take(cutoffs, held_global)
    per_class = KMAX // lon_devices
    k = lon_devices * jnp.arange(per_class, dtype=jnp.int32)[None, :] + jnp.arange(
        lon_devices, dtype=jnp.int32
    )[:, None]
    scale = jnp.where(k == 0, 1.0 / circle, 2.0 / circle).astype(jnp.float32)
    weights = jnp.where(k[:, None, :] < cut[None, :, None], scale[:, None, :], 0.0)
    basis = class_basis(lon_devices, lon_cols, circle)
    roots = root_table(lon_devices)

    west_cx = shift(courant_x[:, :, lon_cols - 1 :], "lon", 1, True)
    north_cy = shift(courant_y[:, :1], "lat", -1, False)
    east_courant = jnp.concatenate([west_cx, courant_x], axis=2)
    north_courant = jnp.concatenate(
        [courant_y, jnp.where(is_north, 0.0, north_cy)], axis=1
    )

    def lat_halos(state):
        south_in = shift(state[:, :, lat_rows - HALO :], "lat", 1, False)
        north_in = shift(state[:, :, :HALO], "lat", -1, False)
        edge = jnp.where(is_south, state[:, :, :HALO], state[:, :, lat_rows - HALO :])
        far = shift(edge, "lon", lon_devices // 2, True)
        far_rev = jnp.concatenate([far[:, :, 2:3], far[:, :, 1:2], far[:, :, 0:1]], axis=2)
        south_rows = jnp.where(is_south, far_rev, south_in)
        north_rows = jnp.where(is_north, far_rev, north_in)
        return jnp.concatenate([south_rows, state, north_rows], axis=2)

    state = tracers
    west_in = shift(state[..., lon_cols - HALO :], "lon", 1, True)
    east_in = shift(state[..., :HALO], "lon", -1, True)
    wrapped = jnp.concatenate([west_in, state, east_in], axis=3)
    for substep in range(SUBSTEPS):
        extended = lat_halos(state)
        zonal = ppm_flux(wrapped, east_courant, 3, lon_cols)
        meridional = ppm_flux(extended, north_courant, 2, lat_rows) * face_weight[:, None]
        change = (
            zonal[..., 1:]
            - zonal[..., :-1]
            + (meridional[:, :, 1:] - meridional[:, :, :-1]) / center_weight[:, None]
        )
        state = state - change
        rows = state.reshape(lon_devices, count, lon_cols)
        rows = lax.all_to_all(rows, "lon", 0, 0)
        wide = filter_rows(rows, basis, roots, weights, polar)
        if substep == SUBSTEPS - 1:
            wide = wide[:, :, HALO : HALO + lon_cols]
        wide = lax.all_to_all(wide, "lon", 0, 0)
        wrapped = wide.reshape(tracer_count, level_count, lat_rows, wide.shape[2])
        state = wrapped if substep == SUBSTEPS - 1 else wrapped[..., HALO : HALO + lon_cols]
    return state


def transposed_path(tracers, courant_x, courant_y, cutoffs):
    tracer_count, level_count, lat_rows, lon_cols = tracers.shape
    lat_devices = lax.axis_size("lat")
    lon_devices = lax.axis_size("lon")
    lat_index = lax.axis_index("lat")
    circle = lon_cols * lon_devices
    total_rows = lat_rows * lat_devices
    row_global = lat_index * lat_rows + jnp.arange(lat_rows, dtype=jnp.int32)
    face_global = lat_index * lat_rows + jnp.arange(lat_rows + 1, dtype=jnp.int32)
    face_angle = (face_global.astype(jnp.float32) / total_rows - 0.5) * math.pi
    face_weight = jnp.where(
        (face_global == 0) | (face_global == total_rows), 0.0, jnp.cos(face_angle)
    )
    center_weight = jnp.cos(((row_global.astype(jnp.float32) + 0.5) / total_rows - 0.5) * math.pi)
    is_south = lat_index == 0
    is_north = lat_index == lat_devices - 1

    count = tracer_count * lat_rows
    lon_index = lax.axis_index("lon")

    def payload_for(level):
        return jnp.concatenate(
            [
                lax.dynamic_index_in_dim(tracers, level, 1, keepdims=False).reshape(count, lon_cols),
                lax.dynamic_index_in_dim(courant_x, level, 0, keepdims=False),
                lax.dynamic_index_in_dim(courant_y, level, 0, keepdims=False),
            ],
            axis=0,
        )

    pieces = [payload_for(lon_index)]
    for by in range(1, lon_devices):
        pieces.append(shift(payload_for((lon_index + by) % lon_devices), "lon", by, True))
    payload = jnp.stack(pieces)
    state = payload[:, :count].reshape(lon_devices, tracer_count, lat_rows, lon_cols)
    cx = payload[:, None, count : count + lat_rows]
    cy = payload[:, None, count + lat_rows :]
    east_courant = jnp.concatenate([jnp.roll(cx[..., lon_cols - 1 :], -1, axis=0), cx], axis=3)

    held_global = lat_index * lat_rows + jnp.arange(count, dtype=jnp.int32) % lat_rows
    polar = (held_global < total_rows // 4) | (held_global >= total_rows - total_rows // 4)
    cut = jnp.take(cutoffs, held_global)
    per_class = KMAX // lon_devices
    k = lon_devices * jnp.arange(per_class, dtype=jnp.int32)[None, :] + jnp.arange(
        lon_devices, dtype=jnp.int32
    )[:, None]
    scale = jnp.where(k == 0, 1.0 / circle, 2.0 / circle).astype(jnp.float32)
    weights = jnp.where(k[:, None, :] < cut[None, :, None], scale[:, None, :], 0.0)
    basis = product_basis(lon_devices, lon_cols, circle)
    roots = root_table(
        lon_devices, (lax.axis_index("lon") - jnp.arange(lon_devices, dtype=jnp.int32)) % lon_devices
    )

    for substep in range(SUBSTEPS):
        top = state[:, :, lat_rows - HALO :].reshape(lon_devices, tracer_count * HALO, lon_cols)
        bottom = state[:, :, :HALO].reshape(lon_devices, tracer_count * HALO, lon_cols)
        if substep == 0:
            bottom = jnp.concatenate([bottom, cy[:, 0, :1]], axis=1)
            top = jnp.concatenate([top, jnp.zeros_like(cy[:, 0, :1])], axis=1)
        is_even = lat_index % 2 == 0
        recv_a = lax.ppermute(
            jnp.where(is_even, top, bottom), "lat", [(i, i ^ 1) for i in range(lat_devices) if i ^ 1 < lat_devices]
        )
        recv_b = lax.ppermute(
            jnp.where(is_even, bottom, top),
            "lat",
            [(i, i + (1 if i % 2 else -1)) for i in range(lat_devices) if 0 <= i + (1 if i % 2 else -1) < lat_devices],
        )
        from_south = jnp.where(is_even, recv_b, recv_a)
        from_north = jnp.where(is_even, recv_a, recv_b)
        south_in = from_south[:, : tracer_count * HALO].reshape(
            lon_devices, tracer_count, HALO, lon_cols
        )
        north_in = from_north[:, : tracer_count * HALO].reshape(
            lon_devices, tracer_count, HALO, lon_cols
        )
        if substep == 0:
            north_cy = jnp.where(is_north, 0.0, from_north[:, None, tracer_count * HALO :])
            north_courant = jnp.concatenate([cy, north_cy], axis=2)
        edge = jnp.where(is_south, state[:, :, :HALO], state[:, :, lat_rows - HALO :])
        far = jnp.roll(edge, lon_devices // 2, axis=0)
        far_rev = jnp.concatenate([far[:, :, 2:3], far[:, :, 1:2], far[:, :, 0:1]], axis=2)
        south_rows = jnp.where(is_south, far_rev, south_in)
        north_rows = jnp.where(is_north, far_rev, north_in)
        extended = jnp.concatenate([south_rows, state, north_rows], axis=2)
        wrapped = jnp.concatenate(
            [
                jnp.roll(state[..., lon_cols - HALO :], -1, axis=0),
                state,
                jnp.roll(state[..., :HALO], 1, axis=0),
            ],
            axis=3,
        )
        zonal = ppm_flux(wrapped, east_courant, 3, lon_cols)
        zonal_change = lax.optimization_barrier(zonal[..., 1:] - zonal[..., :-1])
        meridional = ppm_flux(extended, north_courant, 2, lat_rows) * face_weight[:, None]
        change = zonal_change + (meridional[:, :, 1:] - meridional[:, :, :-1]) / center_weight[:, None]
        state = state - change
        rows = state.reshape(lon_devices, count, lon_cols)
        rows = filter_rows(rows, basis, roots, weights, polar, 0, True)
        state = rows.reshape(lon_devices, tracer_count, lat_rows, lon_cols)

    back = [state[0]]
    for by in range(1, lon_devices):
        held_at = (lon_index - (lon_index ^ by)) % lon_devices
        part = lax.dynamic_index_in_dim(state, held_at, 0, keepdims=False)
        back.append(lax.ppermute(part, "lon", [(i, i ^ by) for i in range(lon_devices)]))
    levels = []
    for level in range(level_count):
        pick = back[0]
        for by in range(1, lon_devices):
            pick = jnp.where((lon_index ^ by) == level, back[by], pick)
        levels.append(pick)
    return jnp.stack(levels, axis=1)


def on_device(tracers, courant_x, courant_y, cutoffs):
    lon_devices = lax.axis_size("lon")
    power_of_two = lon_devices & (lon_devices - 1) == 0
    if tracers.shape[1] == lon_devices and power_of_two and tracers.shape[2] >= HALO:
        return transposed_path(tracers, courant_x, courant_y, cutoffs)
    return tiled_path(tracers, courant_x, courant_y, cutoffs)


def solution(mesh):
    in_specs = (P(None, None, "lat", "lon"), P(None, "lat", "lon"), P(None, "lat", "lon"), P())
    out_specs = P(None, None, "lat", "lon")
    return jax.shard_map(
        on_device, mesh=mesh, in_specs=in_specs, out_specs=out_specs, check_vma=False
    )
```

```python
import math

import jax
import jax.numpy as jnp
from jax import lax
from jax.sharding import PartitionSpec as P


KMAX = 720
SUBSTEPS = 2
HALO = 3
MATMUL_PRECISION = lax.Precision.HIGH


def shift(x, axis, by, wrap):
    size = lax.axis_size(axis)
    pairs = [(i, (i + by) % size) for i in range(size) if wrap or 0 <= i + by < size]
    return lax.ppermute(x, axis, pairs)


def product_basis(tiles, cols, circle):
    split = max(b for b in range(1, cols + 1) if cols % b == 0 and b * b <= cols)
    per_class = KMAX // tiles
    k = tiles * jnp.arange(per_class, dtype=jnp.int32)[None, :] + jnp.arange(
        tiles, dtype=jnp.int32
    )[:, None]
    a = jnp.arange(cols // split, dtype=jnp.int32)
    b = jnp.arange(split, dtype=jnp.int32)
    step = 2.0 * math.pi / circle
    coarse = ((split * a[None, None, :] * k[:, :, None]) % circle).astype(jnp.float32) * step
    fine = ((b[None, None, :] * k[:, :, None]) % circle).astype(jnp.float32) * step
    ca, sa = jnp.cos(coarse)[:, :, :, None], jnp.sin(coarse)[:, :, :, None]
    cb, sb = jnp.cos(fine)[:, :, None], jnp.sin(fine)[:, :, None]
    cos_qk = (ca * cb - sa * sb).reshape(tiles, per_class, cols)
    sin_qk = (sa * cb + ca * sb).reshape(tiles, per_class, cols)
    return jnp.concatenate([cos_qk, sin_qk], axis=1)


def window(values, first_cell, last_cell, dim_at):
    return lax.slice_in_dim(values, first_cell, last_cell, axis=dim_at)


def ppm_flux(padded, courant, dim_at, cell_count):
    edge_values = 7.0 / 12.0 * (
        window(padded, 1, cell_count + 4, dim_at) + window(padded, 2, cell_count + 5, dim_at)
    ) - 1.0 / 12.0 * (
        window(padded, 0, cell_count + 3, dim_at) + window(padded, 3, cell_count + 6, dim_at)
    )
    left_edge = window(edge_values, 0, cell_count + 1, dim_at)
    mid_edge = window(edge_values, 1, cell_count + 2, dim_at)
    right_edge = window(edge_values, 2, cell_count + 3, dim_at)
    left_cell = window(padded, 2, cell_count + 3, dim_at)
    right_cell = window(padded, 3, cell_count + 4, dim_at)
    magnitude = jnp.abs(courant)
    six_left = 6.0 * left_cell - 3.0 * (left_edge + mid_edge)
    six_right = 6.0 * right_cell - 3.0 * (mid_edge + right_edge)
    from_left = mid_edge - 0.5 * magnitude * (
        mid_edge - left_edge - (1.0 - magnitude * (2.0 / 3.0)) * six_left
    )
    from_right = mid_edge + 0.5 * magnitude * (
        right_edge - mid_edge + (1.0 - magnitude * (2.0 / 3.0)) * six_right
    )
    return courant * jnp.where(courant >= 0.0, from_left, from_right)


def root_table(count, tile_of=None):
    d = jnp.arange(count, dtype=jnp.int32)
    tile = d if tile_of is None else tile_of
    angle = (d[:, None] * tile[None, :] % count).astype(jnp.float32) * (2.0 * math.pi / count)
    cos_dr, sin_dr = jnp.cos(angle), jnp.sin(angle)
    cos_dr = jnp.where(jnp.abs(cos_dr) < 1e-6, 0.0, cos_dr)
    sin_dr = jnp.where(jnp.abs(sin_dr) < 1e-6, 0.0, sin_dr)
    return cos_dr, sin_dr


def class_basis(tiles, cols, circle, halo=HALO):
    per_class = KMAX // tiles
    r = jnp.arange(tiles, dtype=jnp.int32)
    m = jnp.arange(per_class, dtype=jnp.int32)
    q = jnp.arange(-halo, cols + halo, dtype=jnp.int32) % circle
    k = tiles * m[None, :] + r[:, None]
    phase = (q[None, :, None] * k[:, None, :]) % circle
    angle = phase.astype(jnp.float32) * (2.0 * math.pi / circle)
    return jnp.concatenate([jnp.cos(angle), jnp.sin(angle)], axis=2)


def filter_rows(rows, basis, roots, weights, polar, halo=HALO, m_major=False):
    _, count, cols = rows.shape
    cos_dr, sin_dr = roots
    z_re = jnp.sum(cos_dr[:, :, None, None] * rows[None], axis=1)
    z_im = -jnp.sum(sin_dr[:, :, None, None] * rows[None], axis=1)
    z = jnp.concatenate([z_re, z_im], axis=1)
    z = jnp.pad(z, ((0, 0), (0, 0), (halo, halo)))
    q_axis, m_axis = (2, 1) if m_major else (1, 2)
    prod = lax.dot_general(z, basis, (((2,), (q_axis,)), ((0,), (0,))), precision=MATMUL_PRECISION)
    per_class = basis.shape[m_axis] // 2
    zc, zs = prod[:, :count, :per_class], prod[:, :count, per_class:]
    wc, ws = prod[:, count:, :per_class], prod[:, count:, per_class:]
    real = (zc + ws) * weights
    imag = (zs - wc) * weights
    spec = jnp.concatenate(
        [jnp.concatenate([real, imag], axis=2), jnp.concatenate([-imag, real], axis=2)], axis=1
    )
    back = lax.dot_general(spec, basis, (((2,), (m_axis,)), ((0,), (0,))), precision=MATMUL_PRECISION)
    w_re, w_im = back[:, :count], back[:, count:]
    smooth = jnp.sum(
        cos_dr[:, :, None, None] * w_re[:, None] - sin_dr[:, :, None, None] * w_im[:, None], axis=0
    )
    wide = rows
    if halo:
        left = jnp.roll(rows[:, :, cols - halo :], 1, axis=0)
        right = jnp.roll(rows[:, :, :halo], -1, axis=0)
        wide = jnp.concatenate([left, rows, right], axis=2)
    return jnp.where(polar[None, :, None], smooth, wide)


def tiled_path(tracers, courant_x, courant_y, cutoffs):
    tracer_count, level_count, lat_rows, lon_cols = tracers.shape
    field_count = tracer_count * level_count
    lat_devices = lax.axis_size("lat")
    lon_devices = lax.axis_size("lon")
    lat_index = lax.axis_index("lat")
    lon_index = lax.axis_index("lon")
    circle = lon_cols * lon_devices
    total_rows = lat_rows * lat_devices
    row_global = lat_index * lat_rows + jnp.arange(lat_rows, dtype=jnp.int32)
    face_global = lat_index * lat_rows + jnp.arange(lat_rows + 1, dtype=jnp.int32)
    face_angle = (face_global.astype(jnp.float32) / total_rows - 0.5) * math.pi
    face_weight = jnp.where(
        (face_global == 0) | (face_global == total_rows), 0.0, jnp.cos(face_angle)
    )
    center_weight = jnp.cos(((row_global.astype(jnp.float32) + 0.5) / total_rows - 0.5) * math.pi)
    is_south = lat_index == 0
    is_north = lat_index == lat_devices - 1

    count = field_count * lat_rows // lon_devices
    flat = lon_index * count + jnp.arange(count, dtype=jnp.int32)
    held_global = lat_index * lat_rows + flat % lat_rows
    polar = (held_global < total_rows // 4) | (held_global >= total_rows - total_rows // 4)
    cut = jnp.take(cutoffs, held_global)
    per_class = KMAX // lon_devices
    k = lon_devices * jnp.arange(per_class, dtype=jnp.int32)[None, :] + jnp.arange(
        lon_devices, dtype=jnp.int32
    )[:, None]
    scale = jnp.where(k == 0, 1.0 / circle, 2.0 / circle).astype(jnp.float32)
    weights = jnp.where(k[:, None, :] < cut[None, :, None], scale[:, None, :], 0.0)
    basis = class_basis(lon_devices, lon_cols, circle)
    roots = root_table(lon_devices)

    west_cx = shift(courant_x[:, :, lon_cols - 1 :], "lon", 1, True)
    north_cy = shift(courant_y[:, :1], "lat", -1, False)
    east_courant = jnp.concatenate([west_cx, courant_x], axis=2)
    north_courant = jnp.concatenate(
        [courant_y, jnp.where(is_north, 0.0, north_cy)], axis=1
    )

    def lat_halos(state):
        south_in = shift(state[:, :, lat_rows - HALO :], "lat", 1, False)
        north_in = shift(state[:, :, :HALO], "lat", -1, False)
        edge = jnp.where(is_south, state[:, :, :HALO], state[:, :, lat_rows - HALO :])
        far = shift(edge, "lon", lon_devices // 2, True)
        far_rev = jnp.concatenate([far[:, :, 2:3], far[:, :, 1:2], far[:, :, 0:1]], axis=2)
        south_rows = jnp.where(is_south, far_rev, south_in)
        north_rows = jnp.where(is_north, far_rev, north_in)
        return jnp.concatenate([south_rows, state, north_rows], axis=2)

    state = tracers
    west_in = shift(state[..., lon_cols - HALO :], "lon", 1, True)
    east_in = shift(state[..., :HALO], "lon", -1, True)
    wrapped = jnp.concatenate([west_in, state, east_in], axis=3)
    for substep in range(SUBSTEPS):
        extended = lat_halos(state)
        zonal = ppm_flux(wrapped, east_courant, 3, lon_cols)
        meridional = ppm_flux(extended, north_courant, 2, lat_rows) * face_weight[:, None]
        change = (
            zonal[..., 1:]
            - zonal[..., :-1]
            + (meridional[:, :, 1:] - meridional[:, :, :-1]) / center_weight[:, None]
        )
        state = state - change
        rows = state.reshape(lon_devices, count, lon_cols)
        rows = lax.all_to_all(rows, "lon", 0, 0)
        wide = filter_rows(rows, basis, roots, weights, polar)
        if substep == SUBSTEPS - 1:
            wide = wide[:, :, HALO : HALO + lon_cols]
        wide = lax.all_to_all(wide, "lon", 0, 0)
        wrapped = wide.reshape(tracer_count, level_count, lat_rows, wide.shape[2])
        state = wrapped if substep == SUBSTEPS - 1 else wrapped[..., HALO : HALO + lon_cols]
    return state


def transposed_path(tracers, courant_x, courant_y, cutoffs):
    tracer_count, level_count, lat_rows, lon_cols = tracers.shape
    lat_devices = lax.axis_size("lat")
    lon_devices = lax.axis_size("lon")
    lat_index = lax.axis_index("lat")
    circle = lon_cols * lon_devices
    total_rows = lat_rows * lat_devices
    row_global = lat_index * lat_rows + jnp.arange(lat_rows, dtype=jnp.int32)
    face_global = lat_index * lat_rows + jnp.arange(lat_rows + 1, dtype=jnp.int32)
    face_angle = (face_global.astype(jnp.float32) / total_rows - 0.5) * math.pi
    face_weight = jnp.where(
        (face_global == 0) | (face_global == total_rows), 0.0, jnp.cos(face_angle)
    )
    center_weight = jnp.cos(((row_global.astype(jnp.float32) + 0.5) / total_rows - 0.5) * math.pi)
    is_south = lat_index == 0
    is_north = lat_index == lat_devices - 1

    count = tracer_count * lat_rows
    lon_index = lax.axis_index("lon")

    def payload_for(level):
        return jnp.concatenate(
            [
                lax.dynamic_index_in_dim(tracers, level, 1, keepdims=False).reshape(count, lon_cols),
                lax.dynamic_index_in_dim(courant_x, level, 0, keepdims=False),
                lax.dynamic_index_in_dim(courant_y, level, 0, keepdims=False),
            ],
            axis=0,
        )

    pieces = [payload_for(lon_index)]
    for by in range(1, lon_devices):
        pieces.append(shift(payload_for((lon_index + by) % lon_devices), "lon", by, True))
    payload = jnp.stack(pieces)
    state = payload[:, :count].reshape(lon_devices, tracer_count, lat_rows, lon_cols)
    cx = payload[:, None, count : count + lat_rows]
    cy = payload[:, None, count + lat_rows :]
    east_courant = jnp.concatenate([jnp.roll(cx[..., lon_cols - 1 :], -1, axis=0), cx], axis=3)

    held_global = lat_index * lat_rows + jnp.arange(count, dtype=jnp.int32) % lat_rows
    polar = (held_global < total_rows // 4) | (held_global >= total_rows - total_rows // 4)
    cut = jnp.take(cutoffs, held_global)
    per_class = KMAX // lon_devices
    k = lon_devices * jnp.arange(per_class, dtype=jnp.int32)[None, :] + jnp.arange(
        lon_devices, dtype=jnp.int32
    )[:, None]
    scale = jnp.where(k == 0, 1.0 / circle, 2.0 / circle).astype(jnp.float32)
    weights = jnp.where(k[:, None, :] < cut[None, :, None], scale[:, None, :], 0.0)
    basis = product_basis(lon_devices, lon_cols, circle)
    roots = root_table(
        lon_devices, (lax.axis_index("lon") - jnp.arange(lon_devices, dtype=jnp.int32)) % lon_devices
    )

    for substep in range(SUBSTEPS):
        top = state[:, :, lat_rows - HALO :].reshape(lon_devices, tracer_count * HALO, lon_cols)
        bottom = state[:, :, :HALO].reshape(lon_devices, tracer_count * HALO, lon_cols)
        if substep == 0:
            bottom = jnp.concatenate([bottom, cy[:, 0, :1]], axis=1)
            top = jnp.concatenate([top, jnp.zeros_like(cy[:, 0, :1])], axis=1)
        is_even = lat_index % 2 == 0
        recv_a = lax.ppermute(
            jnp.where(is_even, top, bottom), "lat", [(i, i ^ 1) for i in range(lat_devices) if i ^ 1 < lat_devices]
        )
        recv_b = lax.ppermute(
            jnp.where(is_even, bottom, top),
            "lat",
            [(i, i + (1 if i % 2 else -1)) for i in range(lat_devices) if 0 <= i + (1 if i % 2 else -1) < lat_devices],
        )
        from_south = jnp.where(is_even, recv_b, recv_a)
        from_north = jnp.where(is_even, recv_a, recv_b)
        south_in = from_south[:, : tracer_count * HALO].reshape(
            lon_devices, tracer_count, HALO, lon_cols
        )
        north_in = from_north[:, : tracer_count * HALO].reshape(
            lon_devices, tracer_count, HALO, lon_cols
        )
        if substep == 0:
            north_cy = jnp.where(is_north, 0.0, from_north[:, None, tracer_count * HALO :])
            north_courant = jnp.concatenate([cy, north_cy], axis=2)
        edge = jnp.where(is_south, state[:, :, :HALO], state[:, :, lat_rows - HALO :])
        far = jnp.roll(edge, lon_devices // 2, axis=0)
        far_rev = jnp.concatenate([far[:, :, 2:3], far[:, :, 1:2], far[:, :, 0:1]], axis=2)
        south_rows = jnp.where(is_south, far_rev, south_in)
        north_rows = jnp.where(is_north, far_rev, north_in)
        extended = jnp.concatenate([south_rows, state, north_rows], axis=2)
        wrapped = jnp.concatenate(
            [
                jnp.roll(state[..., lon_cols - HALO :], -1, axis=0),
                state,
                jnp.roll(state[..., :HALO], 1, axis=0),
            ],
            axis=3,
        )
        zonal = ppm_flux(wrapped, east_courant, 3, lon_cols)
        zonal_change = lax.optimization_barrier(zonal[..., 1:] - zonal[..., :-1])
        meridional = ppm_flux(extended, north_courant, 2, lat_rows) * face_weight[:, None]
        change = zonal_change + (meridional[:, :, 1:] - meridional[:, :, :-1]) / center_weight[:, None]
        state = state - change
        rows = state.reshape(lon_devices, count, lon_cols)
        rows = filter_rows(rows, basis, roots, weights, polar, 0, True)
        state = rows.reshape(lon_devices, tracer_count, lat_rows, lon_cols)

    back = [state[0]]
    for by in range(1, lon_devices):
        back.append(shift(state[(lon_devices - by) % lon_devices], "lon", by, True))
    levels = []
    for level in range(level_count):
        pick = back[0]
        for by in range(1, lon_devices):
            pick = jnp.where((lon_index - by) % lon_devices == level, back[by], pick)
        levels.append(pick)
    return jnp.stack(levels, axis=1)


def on_device(tracers, courant_x, courant_y, cutoffs):
    if tracers.shape[1] == lax.axis_size("lon") and tracers.shape[2] >= HALO:
        return transposed_path(tracers, courant_x, courant_y, cutoffs)
    return tiled_path(tracers, courant_x, courant_y, cutoffs)


def solution(mesh):
    in_specs = (P(None, None, "lat", "lon"), P(None, "lat", "lon"), P(None, "lat", "lon"), P())
    out_specs = P(None, None, "lat", "lon")
    return jax.shard_map(
        on_device, mesh=mesh, in_specs=in_specs, out_specs=out_specs, check_vma=False
    )
```
